128 devices in a mesh: seq: 16 (over x_hi, z, core), kvh: 8 (over x_lo, y).
Axes of the slice: x: 4 (x_hi: 2, x_lo: 2; x = x_hi * 2 + x_lo), y: 4, z: 4, core: 2. Of those that a mesh axis runs over, the one named last changes fastest.
Arguments:
- normed: bfloat16 [4096, 4096], P('seq'), may hold values from -8 to 8
- w_query: bfloat16 [4096, 4096], P(None, 'kvh'), may hold values from -1 to 1, as said below
- w_key: bfloat16 [4096, 1024], P(None, 'kvh'), may hold values from -1 to 1, as said below
- w_value: bfloat16 [4096, 1024], P(None, 'kvh'), may hold values from -0.09375 to 0.09375
- positions: int32 [4096], P('seq'), may hold values from 0 to 4222, as said below
- block_mask: int32 [32, 32], P('seq'), may hold values from 0 to 1, as said below
- grad_attn: bfloat16 [4096, 4096], P('seq', 'kvh'), may hold values from -6 to 6
Outputs:
- grad_normed: bfloat16 [4096, 4096], P('seq', 'kvh')
- grad_wq: float32 [4096, 4096], P('seq', 'kvh')
- grad_wk: float32 [4096, 1024], P('seq', 'kvh')
- grad_wv: float32 [4096, 1024], P('seq', 'kvh')
The draws below stay inside these ranges and needn't reach their ends.
Inputs may be any that keep to these rules, and one draw needn't show every extreme that they name: Within a block positions rise by one per token; block b starts between b * 128 and (b + 1) * 128 - 1, block 0 at 0, the last block at its latest start. `block_mask`: the diagonal is 1; a block may read only blocks of earlier rounds besides itself; entries for earlier rounds are 0 or 1. `w_query`: entries of about 4096^(-1/2) in size. `w_key`: entries of about 4096^(-1/2) in size.
All inputs are finite; a program needn't handle non-finite values.
Results may differ from the reference program's by a relative error of at most 0.019.
The reference program's roundings to bfloat16 on the way (of `values`, `weights` and `grad_scores`) count: a program that leaves them out, or rounds other values in their place, can miss the bound.
Values may be sent and summed in bfloat16 or wider, within the bound.
No kernel may reach another device: no remote copies, remote signals or barrier semaphores. Data moves between devices by JAX's collectives and lax.ppermute only.
A program may use at most 128 MiB of HBM per device.

```python
import jax
import jax.numpy as jnp
from jax import lax

D = 4096
HEADS = 32
KV_HEADS = 8
HEAD = 128
GROUP = 4
BLOCK = 128
AGENTS = 8
BLOCKS = 32
TOKENS = 4096


def draw_positions(key, part):
    offsets = jax.random.randint(key, (BLOCKS,), 0, BLOCK)
    block_index = jnp.arange(BLOCKS)
    offsets = jnp.where(block_index == 0, 0, offsets)
    offsets = jnp.where(block_index == BLOCKS - 1, BLOCK - 1, offsets)
    starts = block_index * BLOCK + offsets
    return (starts[:, None] + jnp.arange(BLOCK)[None, :]).reshape(BLOCKS * BLOCK).astype(jnp.int32)


def draw_block_mask(key, part):
    block_index = jnp.arange(BLOCKS)
    round_index = block_index // AGENTS
    coins = jax.random.randint(key, (BLOCKS, BLOCKS), 0, 4)
    earlier = round_index[None, :] < round_index[:, None]
    diagonal = block_index[:, None] == block_index[None, :]
    return jnp.where(diagonal, 1, jnp.where(earlier & (coins > 0), 1, 0)).astype(jnp.int32)


def projection_pair(key):
    seed_query = jax.random.fold_in(key, 101)
    seed_keys = jax.random.fold_in(key, 102)
    spread = D ** (-0.5)
    query_weight = jnp.clip(jax.random.normal(seed_query, (D, HEADS * HEAD), jnp.float32), -6.0, 6.0) * spread
    key_weight = jnp.clip(jax.random.normal(seed_keys, (D, KV_HEADS * HEAD), jnp.float32), -6.0, 6.0) * spread
    return (query_weight, key_weight)


def draw_w_query(key, part):
    return projection_pair(key)[0].astype(jnp.bfloat16)


def draw_w_key(key, part):
    return projection_pair(key)[1].astype(jnp.bfloat16)


def draw_normed(key, part):
    return jnp.clip(jax.random.normal(jax.random.fold_in(key, 103), (TOKENS, D), jnp.float32), -6.0, 6.0).astype(jnp.bfloat16)


def block_scale(own_key, extent, cuts, low, top_value):
    factor_of, own = 1.0, jax.random.fold_in(own_key, 6)
    for axis_at, blocks in cuts:
        heights = jnp.exp(jax.random.uniform(jax.random.fold_in(own, axis_at), (blocks,), jnp.float32, low / len(cuts), top_value / len(cuts)))
        factor_of = factor_of * jnp.repeat(heights, extent[axis_at] // blocks).reshape([-1 if axis == axis_at else 1 for axis in range(len(extent))])
    return factor_of


def centred(own_key, shape, width, most, cuts=(), held_as=jnp.bfloat16):
    gain = block_scale(own_key, shape, cuts, -0.22, 0.18) if cuts else 1.0
    result = jax.random.normal(own_key, shape, jnp.float32) * width * gain
    return jnp.minimum(jnp.maximum(result, -most), most).astype(held_as)


def setup_inputs(seed: int = 0) -> dict:
    arg_keys = jax.random.split(jax.random.key(seed), 8)
    return {
        "normed": draw_normed(jax.random.fold_in(arg_keys[7], 71), 0),
        "w_query": draw_w_query(jax.random.fold_in(arg_keys[7], 71), 0),
        "w_key": draw_w_key(jax.random.fold_in(arg_keys[7], 71), 0),
        "w_value": centred(arg_keys[3], (D, KV_HEADS * HEAD), D ** -0.5, 0.09375, ((1, 8),)),
        "positions": draw_positions(jax.random.fold_in(arg_keys[7], 71), 0),
        "block_mask": draw_block_mask(jax.random.fold_in(arg_keys[7], 71), 0),
        "grad_attn": centred(arg_keys[6], (TOKENS, HEADS * HEAD), 1.0, 6.0, ((0, 16), (1, 8))),
    }


THETA = 500000.0


def rotate(values, positions, rotation_sign):
    tok_rows = values.shape[0]
    head_count = values.shape[1] // HEAD
    half_size = HEAD // 2
    pieces = values.reshape(tok_rows, head_count, HEAD)
    frequency = THETA ** (-(jnp.arange(half_size, dtype=jnp.float32) * (2.0 / HEAD)))
    angles = positions.astype(jnp.float32)[:, None] * frequency[None, :]
    cosine = jnp.cos(angles)[:, None, :]
    sine_part = rotation_sign * jnp.sin(angles)[:, None, :]
    lower_half = pieces[:, :, :half_size]
    upper_half = pieces[:, :, half_size:]
    turned = jnp.concatenate([lower_half * cosine - upper_half * sine_part, upper_half * cosine + lower_half * sine_part], axis=2)
    return turned.reshape(tok_rows, head_count * HEAD)


def visible(mask_table, query_block0, query_count, key_block0, key_count):
    query_local = jnp.arange(query_count)
    key_local = jnp.arange(key_count)
    query_block = query_block0 + query_local // BLOCK
    key_block = key_block0 + key_local // BLOCK
    allowed = jnp.repeat(jnp.repeat(mask_table, BLOCK, axis=0), BLOCK, axis=1) == 1
    inner_ok = (key_local % BLOCK)[None, :] <= (query_local % BLOCK)[:, None]
    return allowed & ((query_block[:, None] != key_block[None, :]) | inner_ok)


def product(form, left, right):
    return jnp.einsum(form, left.astype(jnp.float32), right.astype(jnp.float32))


def head_group(queries, keys, values, grad_heads, seen):
    score_scale = HEAD ** -0.5
    scores = product('tgd,sd->gts', queries, keys) * score_scale
    scores = jnp.where(seen[None], scores, -1e30)
    row_max = jnp.max(scores, axis=2, keepdims=True)
    log_total = row_max[:, :, 0] + jnp.log(jnp.sum(jnp.exp(scores - row_max), axis=2))
    probs = jnp.where(seen[None], jnp.exp(scores - log_total[:, :, None]), 0.0)
    weights = probs.astype(jnp.bfloat16)
    outputs = product('gts,sd->gtd', weights, values)
    row_dots = jnp.sum(outputs * jnp.transpose(grad_heads.astype(jnp.float32), (1, 0, 2)), axis=2)
    grad_probs = product('tgd,sd->gts', grad_heads, values)
    grad_scores = (probs * (grad_probs - row_dots[:, :, None]) * score_scale).astype(jnp.bfloat16)
    grad_query = product('gts,sd->tgd', grad_scores, keys)
    grad_key = product('gts,tgd->sd', grad_scores, queries)
    grad_value = product('gts,tgd->sd', weights, grad_heads)
    return grad_query, grad_key, grad_value


def reference(normed, w_query, w_key, w_value, positions, block_mask, grad_attn):
    tokens = normed.shape[0]
    queries = rotate(jnp.dot(normed, w_query, preferred_element_type=jnp.float32), positions, 1.0).astype(jnp.bfloat16)
    keys = rotate(jnp.dot(normed, w_key, preferred_element_type=jnp.float32), positions, 1.0).astype(jnp.bfloat16)
    values = jnp.dot(normed, w_value, preferred_element_type=jnp.float32).astype(jnp.bfloat16)
    seen = visible(block_mask, 0, tokens, 0, tokens)
    query_groups = jnp.transpose(queries.reshape(tokens, KV_HEADS, GROUP, HEAD), (1, 0, 2, 3))
    grad_groups = jnp.transpose(grad_attn.reshape(tokens, KV_HEADS, GROUP, HEAD), (1, 0, 2, 3))
    key_groups = jnp.transpose(keys.reshape(tokens, KV_HEADS, HEAD), (1, 0, 2))
    value_groups = jnp.transpose(values.reshape(tokens, KV_HEADS, HEAD), (1, 0, 2))
    grad_query, grad_key, grad_value = lax.map(lambda items: head_group(items[0], items[1], items[2], items[3], seen), (query_groups, key_groups, value_groups, grad_groups))
    grad_query = jnp.transpose(grad_query, (1, 0, 2, 3)).reshape(tokens, HEADS * HEAD)
    grad_key = jnp.transpose(grad_key, (1, 0, 2)).reshape(tokens, KV_HEADS * HEAD)
    grad_value = jnp.transpose(grad_value, (1, 0, 2)).reshape(tokens, KV_HEADS * HEAD)
    query_grad = rotate(grad_query, positions, -1.0).astype(jnp.bfloat16)
    key_grad = rotate(grad_key, positions, -1.0).astype(jnp.bfloat16)
    value_grad = grad_value.astype(jnp.bfloat16)
    grad_wq = jnp.dot(normed.T, query_grad, preferred_element_type=jnp.float32)
    grad_wk = jnp.dot(normed.T, key_grad, preferred_element_type=jnp.float32)
    grad_wv = jnp.dot(normed.T, value_grad, preferred_element_type=jnp.float32)
    grad_normed = jnp.dot(query_grad, w_query.T, preferred_element_type=jnp.float32)
    grad_normed = grad_normed + jnp.dot(key_grad, w_key.T, preferred_element_type=jnp.float32)
    grad_normed = grad_normed + jnp.dot(value_grad, w_value.T, preferred_element_type=jnp.float32)
    return (grad_normed.astype(jnp.bfloat16), grad_wq, grad_wk, grad_wv)
```

```python
import jax
import jax.numpy as jnp
from jax import lax
from jax.sharding import PartitionSpec as P

HEAD = 128
BLOCK = 128


THETA = 500000.0


def rotate(values, positions, rotation_sign):
    tok_rows = values.shape[0]
    head_count = values.shape[1] // HEAD
    half_size = HEAD // 2
    pieces = values.reshape(tok_rows, head_count, HEAD)
    frequency = THETA ** (-(jnp.arange(half_size, dtype=jnp.float32) * (2.0 / HEAD)))
    angles = positions.astype(jnp.float32)[:, None] * frequency[None, :]
    cosine = jnp.cos(angles)[:, None, :]
    sine_part = rotation_sign * jnp.sin(angles)[:, None, :]
    lower_half = pieces[:, :, :half_size]
    upper_half = pieces[:, :, half_size:]
    turned = jnp.concatenate(
        [
            lower_half * cosine - upper_half * sine_part,
            upper_half * cosine + lower_half * sine_part,
        ],
        axis=2,
    )
    return turned.reshape(tok_rows, head_count * HEAD)


def visible(mask_table, query_block0, query_count, key_count):
    query_local = jnp.arange(query_count)
    key_local = jnp.arange(key_count)
    query_block = query_block0 + query_local // BLOCK
    key_block = key_local // BLOCK
    allowed = jnp.repeat(jnp.repeat(mask_table, BLOCK, axis=0), BLOCK, axis=1) == 1
    inner_ok = (key_local % BLOCK)[None, :] <= (query_local % BLOCK)[:, None]
    return allowed & ((query_block[:, None] != key_block[None, :]) | inner_ok)


def product(form, left, right):
    return jnp.einsum(form, left, right, preferred_element_type=jnp.float32)


def masked_scores(queries, keys, seen):
    scores = product("tgd,sd->gts", queries, keys) * HEAD ** (-0.5)
    return jnp.where(seen[None], scores, -1e30)


def softmax_stats(queries, keys, values, grad_heads, seen):
    scores = masked_scores(queries, keys, seen)
    row_max = jnp.max(scores, axis=2, keepdims=True)
    log_total = row_max[:, :, 0] + jnp.log(jnp.sum(jnp.exp(scores - row_max), axis=2))
    weights = jnp.where(seen[None], jnp.exp(scores - log_total[:, :, None]), 0.0).astype(
        jnp.bfloat16
    )
    outputs = product("gts,sd->gtd", weights, values)
    row_dots = jnp.sum(outputs * jnp.transpose(grad_heads.astype(jnp.float32), (1, 0, 2)), axis=2)
    return (log_total, row_dots)


def attention_grads(queries, keys, values, grad_heads, seen, log_total, row_dots):
    scores = masked_scores(queries, keys, seen)
    probs = jnp.where(seen[None], jnp.exp(scores - log_total[:, :, None]), 0.0)
    weights = probs.astype(jnp.bfloat16)
    grad_probs = product("tgd,sd->gts", grad_heads, values)
    grad_scores = (probs * (grad_probs - row_dots[:, :, None]) * HEAD ** (-0.5)).astype(
        jnp.bfloat16
    )
    grad_query = product("gts,sd->tgd", grad_scores, keys)
    grad_key = product("gts,tgd->sd", grad_scores, queries)
    grad_value = product("gts,tgd->sd", weights, grad_heads)
    return (grad_query, grad_key, grad_value)


def gather_rows(block, axis):
    count = lax.axis_size(axis)
    copies = jnp.broadcast_to(block[None], (count,) + block.shape)
    joined = lax.all_to_all(copies, axis, 0, 0, tiled=True)
    return joined.reshape((count * block.shape[0],) + block.shape[1:])


def scatter_sum(parts, axis):
    arrived = lax.all_to_all(parts, axis, 0, 0, tiled=True)
    return jnp.sum(arrived.astype(jnp.float32), axis=0)


def body(normed, w_query, w_key, w_value, positions, block_mask, grad_attn):
    tok_rows = normed.shape[0]
    group_size = w_query.shape[1] // w_key.shape[1]
    width_query = group_size * HEAD
    blk_local = tok_rows // BLOCK
    seq_count = lax.axis_size("seq")
    kvh_count = lax.axis_size("kvh")
    my_index = lax.axis_index("seq")
    queries = rotate(
        jnp.dot(normed, w_query, preferred_element_type=jnp.float32), positions, 1.0
    ).astype(jnp.bfloat16)
    keys = rotate(
        jnp.dot(normed, w_key, preferred_element_type=jnp.float32), positions, 1.0
    ).astype(jnp.bfloat16)
    values = jnp.dot(normed, w_value, preferred_element_type=jnp.float32).astype(jnp.bfloat16)
    kv_all = gather_rows(jnp.concatenate([keys, values], axis=1), "seq")
    keys_all = kv_all[:, :HEAD]
    values_all = kv_all[:, HEAD:]
    seen = visible(block_mask, my_index * blk_local, tok_rows, keys_all.shape[0])
    query_heads = queries.reshape(tok_rows, group_size, HEAD)
    grad_heads = grad_attn.reshape(tok_rows, group_size, HEAD)
    log_total, row_dots = softmax_stats(query_heads, keys_all, values_all, grad_heads, seen)
    grad_query, grad_key, grad_value = attention_grads(
        query_heads, keys_all, values_all, grad_heads, seen, log_total, row_dots
    )
    query_grad = rotate(grad_query.reshape(tok_rows, width_query), positions, -1.0).astype(
        jnp.bfloat16
    )
    kv_terms = jnp.concatenate([grad_key, grad_value], axis=1).astype(jnp.bfloat16)
    kv_total = scatter_sum(kv_terms.reshape(seq_count, tok_rows, 2 * HEAD), "seq")
    tokens_first = (((0,), (0,)), ((), ()))
    grad_wq = lax.psum_scatter(
        lax.dot_general(normed, query_grad, tokens_first, preferred_element_type=jnp.float32).astype(
            jnp.bfloat16
        ),
        "seq",
        scatter_dimension=0,
        tiled=True,
    ).astype(jnp.float32)
    contract = (((1,), (1,)), ((), ()))
    partial_input = lax.dot_general(
        query_grad, w_query, contract, preferred_element_type=jnp.float32
    )
    key_grad = rotate(kv_total[:, :HEAD], positions, -1.0).astype(jnp.bfloat16)
    value_grad = kv_total[:, HEAD:].astype(jnp.bfloat16)
    kv_grad = jnp.concatenate([key_grad, value_grad], axis=1)
    grad_wkv = lax.psum_scatter(
        lax.dot_general(normed, kv_grad, tokens_first, preferred_element_type=jnp.float32).astype(
            jnp.bfloat16
        ),
        "seq",
        scatter_dimension=0,
        tiled=True,
    ).astype(jnp.float32)
    grad_wk = grad_wkv[:, :HEAD]
    grad_wv = grad_wkv[:, HEAD:]
    partial_input = partial_input + lax.dot_general(
        key_grad, w_key, contract, preferred_element_type=jnp.float32
    )
    partial_input = partial_input + lax.dot_general(
        value_grad, w_value, contract, preferred_element_type=jnp.float32
    )
    feat = partial_input.shape[1] // kvh_count
    input_terms = partial_input.astype(jnp.bfloat16).reshape(tok_rows, kvh_count, feat)
    grad_normed = scatter_sum(jnp.transpose(input_terms, (1, 0, 2)), "kvh").astype(jnp.bfloat16)
    return (grad_normed, grad_wq, grad_wk, grad_wv)


def solution(mesh):
    in_specs = (
        P("seq", None),
        P(None, "kvh"),
        P(None, "kvh"),
        P(None, "kvh"),
        P("seq"),
        P("seq", None),
        P("seq", "kvh"),
    )
    out_specs = (P("seq", "kvh"), P("seq", "kvh"), P("seq", "kvh"), P("seq", "kvh"))
    return jax.shard_map(body, mesh=mesh, in_specs=in_specs, out_specs=out_specs, check_vma=False)
```

```python
import jax
import jax.numpy as jnp
from jax import lax
from jax.sharding import PartitionSpec as P

HEAD = 128
BLOCK = 128


THETA = 500000.0


def rotate(values, positions, rotation_sign):
    tok_rows = values.shape[0]
    head_count = values.shape[1] // HEAD
    half_size = HEAD // 2
    pieces = values.reshape(tok_rows, head_count, HEAD)
    frequency = THETA ** (-(jnp.arange(half_size, dtype=jnp.float32) * (2.0 / HEAD)))
    angles = positions.astype(jnp.float32)[:, None] * frequency[None, :]
    cosine = jnp.cos(angles)[:, None, :]
    sine_part = rotation_sign * jnp.sin(angles)[:, None, :]
    lower_half = pieces[:, :, :half_size]
    upper_half = pieces[:, :, half_size:]
    turned = jnp.concatenate(
        [
            lower_half * cosine - upper_half * sine_part,
            upper_half * cosine + lower_half * sine_part,
        ],
        axis=2,
    )
    return turned.reshape(tok_rows, head_count * HEAD)


def visible(mask_table, query_block0, query_count, key_count):
    query_local = jnp.arange(query_count)
    key_local = jnp.arange(key_count)
    query_block = query_block0 + query_local // BLOCK
    key_block = key_local // BLOCK
    allowed = jnp.repeat(jnp.repeat(mask_table, BLOCK, axis=0), BLOCK, axis=1) == 1
    inner_ok = (key_local % BLOCK)[None, :] <= (query_local % BLOCK)[:, None]
    return allowed & ((query_block[:, None] != key_block[None, :]) | inner_ok)


def product(form, left, right):
    return jnp.einsum(form, left, right, preferred_element_type=jnp.float32)


def masked_scores(queries, keys, seen):
    scores = product("tgd,sd->gts", queries, keys) * HEAD ** (-0.5)
    return jnp.where(seen[None], scores, -1e30)


def softmax_stats(queries, keys, values, grad_heads, seen):
    scores = masked_scores(queries, keys, seen)
    row_max = jnp.max(scores, axis=2, keepdims=True)
    log_total = row_max[:, :, 0] + jnp.log(jnp.sum(jnp.exp(scores - row_max), axis=2))
    weights = jnp.where(seen[None], jnp.exp(scores - log_total[:, :, None]), 0.0).astype(
        jnp.bfloat16
    )
    outputs = product("gts,sd->gtd", weights, values)
    row_dots = jnp.sum(outputs * jnp.transpose(grad_heads.astype(jnp.float32), (1, 0, 2)), axis=2)
    return (log_total, row_dots)


def attention_grads(queries, keys, values, grad_heads, seen, log_total, row_dots):
    scores = masked_scores(queries, keys, seen)
    probs = jnp.where(seen[None], jnp.exp(scores - log_total[:, :, None]), 0.0)
    weights = probs.astype(jnp.bfloat16)
    grad_probs = product("tgd,sd->gts", grad_heads, values)
    grad_scores = (probs * (grad_probs - row_dots[:, :, None]) * HEAD ** (-0.5)).astype(
        jnp.bfloat16
    )
    grad_query = product("gts,sd->tgd", grad_scores, keys)
    grad_key = product("gts,tgd->sd", grad_scores, queries)
    grad_value = product("gts,tgd->sd", weights, grad_heads)
    return (grad_query, grad_key, grad_value)


SEQ_AXES = ("seq_x", "seq_z", "seq_core")
KVH_AXES = ("kvh_x", "kvh_y")
PAIR = [(0, 1), (1, 0)]


def seq_position():
    return (lax.axis_index("seq_x") * lax.axis_size("seq_z") + lax.axis_index("seq_z")) * 2 + lax.axis_index(
        "seq_core"
    )


def gather_rows(block):
    chips = lax.axis_size("seq_x") * lax.axis_size("seq_z")
    copies = jnp.broadcast_to(block[None], (chips,) + block.shape)
    mine = lax.all_to_all(copies, ("seq_x", "seq_z"), 0, 0, tiled=True)
    other = lax.ppermute(mine, "seq_core", PAIR)
    first = lax.axis_index("seq_core") == 0
    low = jnp.where(first, mine, other)
    high = jnp.where(first, other, mine)
    joined = jnp.stack([low, high], axis=1)
    return joined.reshape((chips * 2 * block.shape[0],) + block.shape[1:])


def pair_reduce(terms):
    chips = lax.axis_size("seq_x") * lax.axis_size("seq_z")
    split = terms.reshape((chips, 2, terms.shape[0] // (2 * chips)) + terms.shape[1:])
    core = lax.axis_index("seq_core")
    keep = lax.dynamic_index_in_dim(split, core, axis=1, keepdims=False)
    send = lax.dynamic_index_in_dim(split, 1 - core, axis=1, keepdims=False)
    got = lax.ppermute(send, "seq_core", PAIR)
    return (keep.astype(jnp.float32) + got.astype(jnp.float32)).astype(jnp.bfloat16)


def scatter_sum(parts, axis):
    arrived = lax.all_to_all(parts, axis, 0, 0, tiled=True)
    return jnp.sum(arrived.astype(jnp.float32), axis=0)


def body(normed, w_query, w_key, w_value, positions, block_mask, grad_attn):
    tok_rows = normed.shape[0]
    group_size = w_query.shape[1] // w_key.shape[1]
    width_query = group_size * HEAD
    blk_local = tok_rows // BLOCK
    kvh_count = lax.axis_size("kvh_x") * lax.axis_size("kvh_y")
    my_index = seq_position()
    queries = rotate(
        jnp.dot(normed, w_query, preferred_element_type=jnp.float32), positions, 1.0
    ).astype(jnp.bfloat16)
    keys = rotate(
        jnp.dot(normed, w_key, preferred_element_type=jnp.float32), positions, 1.0
    ).astype(jnp.bfloat16)
    values = jnp.dot(normed, w_value, preferred_element_type=jnp.float32).astype(jnp.bfloat16)
    kv_all = gather_rows(jnp.concatenate([keys, values], axis=1))
    keys_all = kv_all[:, :HEAD]
    values_all = kv_all[:, HEAD:]
    seen = visible(block_mask, my_index * blk_local, tok_rows, keys_all.shape[0])
    query_heads = queries.reshape(tok_rows, group_size, HEAD)
    grad_heads = grad_attn.reshape(tok_rows, group_size, HEAD)
    log_total, row_dots = softmax_stats(query_heads, keys_all, values_all, grad_heads, seen)
    grad_query, grad_key, grad_value = attention_grads(
        query_heads, keys_all, values_all, grad_heads, seen, log_total, row_dots
    )
    query_grad = rotate(grad_query.reshape(tok_rows, width_query), positions, -1.0).astype(
        jnp.bfloat16
    )
    kv_terms = jnp.concatenate([grad_key, grad_value], axis=1).astype(jnp.bfloat16)
    kv_total = scatter_sum(pair_reduce(kv_terms), ("seq_x", "seq_z"))
    tokens_first = (((0,), (0,)), ((), ()))
    wq_terms = pair_reduce(
        lax.dot_general(normed, query_grad, tokens_first, preferred_element_type=jnp.float32).astype(
            jnp.bfloat16
        )
    )
    grad_wq = lax.psum_scatter(
        wq_terms.reshape((-1,) + wq_terms.shape[2:]),
        ("seq_x", "seq_z"),
        scatter_dimension=0,
        tiled=True,
    ).astype(jnp.float32)
    contract = (((1,), (1,)), ((), ()))
    partial_input = lax.dot_general(
        query_grad, w_query, contract, preferred_element_type=jnp.float32
    )
    key_grad = rotate(kv_total[:, :HEAD], positions, -1.0).astype(jnp.bfloat16)
    value_grad = kv_total[:, HEAD:].astype(jnp.bfloat16)
    kv_grad = jnp.concatenate([key_grad, value_grad], axis=1)
    wkv_terms = pair_reduce(
        lax.dot_general(normed, kv_grad, tokens_first, preferred_element_type=jnp.float32).astype(
            jnp.bfloat16
        )
    )
    grad_wkv = scatter_sum(wkv_terms, ("seq_x", "seq_z"))
    grad_wk = grad_wkv[:, :HEAD]
    grad_wv = grad_wkv[:, HEAD:]
    partial_input = partial_input + lax.dot_general(
        key_grad, w_key, contract, preferred_element_type=jnp.float32
    )
    partial_input = partial_input + lax.dot_general(
        value_grad, w_value, contract, preferred_element_type=jnp.float32
    )
    feat = partial_input.shape[1] // kvh_count
    input_terms = partial_input.astype(jnp.bfloat16).reshape(tok_rows, kvh_count, feat)
    grad_normed = scatter_sum(jnp.transpose(input_terms, (1, 0, 2)), KVH_AXES).astype(jnp.bfloat16)
    return (grad_normed, grad_wq, grad_wk, grad_wv)


def solution(mesh):
    seq_x = 2
    seq_size = mesh.shape["seq"]
    kvh_size = mesh.shape["kvh"]
    grid = mesh.devices.reshape(seq_x, seq_size // (2 * seq_x), 2, 2, kvh_size // 2)
    fine = jax.sharding.Mesh(grid, SEQ_AXES + KVH_AXES)
    in_specs = (
        P(SEQ_AXES, None),
        P(None, KVH_AXES),
        P(None, KVH_AXES),
        P(None, KVH_AXES),
        P(SEQ_AXES),
        P(SEQ_AXES, None),
        P(SEQ_AXES, KVH_AXES),
    )
    out_specs = (P(SEQ_AXES, KVH_AXES),) * 4
    return jax.shard_map(body, mesh=fine, in_specs=in_specs, out_specs=out_specs, check_vma=False)
```

```python
import jax
import jax.numpy as jnp
from jax import lax
from jax.sharding import PartitionSpec as P

HEAD = 128
BLOCK = 128


THETA = 500000.0


def rotate(values, positions, rotation_sign):
    tok_rows = values.shape[0]
    head_count = values.shape[1] // HEAD
    half_size = HEAD // 2
    pieces = values.reshape(tok_rows, head_count, HEAD)
    frequency = THETA ** (-(jnp.arange(half_size, dtype=jnp.float32) * (2.0 / HEAD)))
    angles = positions.astype(jnp.float32)[:, None] * frequency[None, :]
    cosine = jnp.cos(angles)[:, None, :]
    sine_part = rotation_sign * jnp.sin(angles)[:, None, :]
    lower_half = pieces[:, :, :half_size]
    upper_half = pieces[:, :, half_size:]
    turned = jnp.concatenate(
        [
            lower_half * cosine - upper_half * sine_part,
            upper_half * cosine + lower_half * sine_part,
        ],
        axis=2,
    )
    return turned.reshape(tok_rows, head_count * HEAD)


def visible(mask_rows, query_block0, query_count, key_blocks, key_inner):
    query_local = jnp.arange(query_count)
    query_block = query_block0 + query_local // BLOCK
    table = jnp.take(mask_rows, key_blocks, axis=1) == 1
    allowed = jnp.repeat(table, BLOCK, axis=0)
    inner_ok = key_inner[None, :] <= (query_local % BLOCK)[:, None]
    return allowed & ((query_block[:, None] != key_blocks[None, :]) | inner_ok)


def product(form, left, right):
    return jnp.einsum(form, left, right, preferred_element_type=jnp.float32)


def masked_scores(queries, keys, seen):
    scores = product("tgd,sd->gts", queries, keys) * HEAD ** (-0.5)
    return jnp.where(seen[None], scores, -1e30)


def softmax_stats(queries, keys, values, grad_heads, seen):
    scores = masked_scores(queries, keys, seen)
    row_max = jnp.max(scores, axis=2, keepdims=True)
    log_total = row_max[:, :, 0] + jnp.log(jnp.sum(jnp.exp(scores - row_max), axis=2))
    weights = jnp.where(seen[None], jnp.exp(scores - log_total[:, :, None]), 0.0).astype(
        jnp.bfloat16
    )
    outputs = product("gts,sd->gtd", weights, values)
    row_dots = jnp.sum(outputs * jnp.transpose(grad_heads.astype(jnp.float32), (1, 0, 2)), axis=2)
    return (log_total, row_dots)


def attention_grads(queries, keys, values, grad_heads, seen, log_total, row_dots):
    scores = masked_scores(queries, keys, seen)
    probs = jnp.where(seen[None], jnp.exp(scores - log_total[:, :, None]), 0.0)
    weights = probs.astype(jnp.bfloat16)
    grad_probs = product("tgd,sd->gts", grad_heads, values)
    grad_scores = (probs * (grad_probs - row_dots[:, :, None]) * HEAD ** (-0.5)).astype(
        jnp.bfloat16
    )
    grad_query = product("gts,sd->tgd", grad_scores, keys)
    grad_key = product("gts,tgd->sd", grad_scores, queries)
    grad_value = product("gts,tgd->sd", weights, grad_heads)
    return (grad_query, grad_key, grad_value)


SEQ_AXES = ("seq_x", "seq_z", "seq_core")
KVH_AXES = ("kvh_x", "kvh_y")
PAIR = [(0, 1), (1, 0)]


def seq_position():
    return (lax.axis_index("seq_x") * lax.axis_size("seq_z") + lax.axis_index("seq_z")) * 2 + lax.axis_index(
        "seq_core"
    )


def gather_rows(block):
    chips = lax.axis_size("seq_x") * lax.axis_size("seq_z")
    copies = jnp.broadcast_to(block[None], (chips,) + block.shape)
    mine = lax.all_to_all(copies, ("seq_x", "seq_z"), 0, 0, tiled=True)
    other = lax.ppermute(mine, "seq_core", PAIR)
    joined = jnp.stack([mine, other], axis=0)
    return joined.reshape((2 * chips * block.shape[0],) + block.shape[1:])


def pair_sum(keep, send):
    got = lax.ppermute(send.astype(jnp.bfloat16), "seq_core", PAIR)
    return (keep.astype(jnp.float32) + got.astype(jnp.float32)).astype(jnp.bfloat16)


def scatter_sum(parts, axis):
    arrived = lax.all_to_all(parts, axis, 0, 0, tiled=True)
    return jnp.sum(arrived.astype(jnp.float32), axis=0)


def body(normed, w_query, w_key, w_value, positions, block_mask, grad_attn):
    tok_rows = normed.shape[0]
    group_size = w_query.shape[1] // w_key.shape[1]
    width_query = group_size * HEAD
    blk_local = tok_rows // BLOCK
    chips = lax.axis_size("seq_x") * lax.axis_size("seq_z")
    kvh_count = lax.axis_size("kvh_x") * lax.axis_size("kvh_y")
    core = lax.axis_index("seq_core")
    my_index = seq_position()
    queries = rotate(
        jnp.dot(normed, w_query, preferred_element_type=jnp.float32), positions, 1.0
    ).astype(jnp.bfloat16)
    keys = rotate(
        jnp.dot(normed, w_key, preferred_element_type=jnp.float32), positions, 1.0
    ).astype(jnp.bfloat16)
    values = jnp.dot(normed, w_value, preferred_element_type=jnp.float32).astype(jnp.bfloat16)
    kv_all = gather_rows(jnp.concatenate([keys, values], axis=1))
    keys_all = kv_all[:, :HEAD]
    values_all = kv_all[:, HEAD:]
    key_count = keys_all.shape[0]
    spot = jnp.arange(key_count)
    side = spot // (chips * tok_rows)
    chip = (spot // tok_rows) % chips
    key_token = (chip * 2 + jnp.where(side == 0, core, 1 - core)) * tok_rows + spot % tok_rows
    seen = visible(block_mask, my_index * blk_local, tok_rows, key_token // BLOCK, key_token % BLOCK)
    query_heads = queries.reshape(tok_rows, group_size, HEAD)
    grad_heads = grad_attn.reshape(tok_rows, group_size, HEAD)
    log_total, row_dots = softmax_stats(query_heads, keys_all, values_all, grad_heads, seen)
    grad_query, grad_key, grad_value = attention_grads(
        query_heads, keys_all, values_all, grad_heads, seen, log_total, row_dots
    )
    query_grad = rotate(grad_query.reshape(tok_rows, width_query), positions, -1.0).astype(
        jnp.bfloat16
    )
    kv_terms = jnp.concatenate([grad_key, grad_value], axis=1).reshape(2, chips, tok_rows, 2 * HEAD)
    kv_total = scatter_sum(pair_sum(kv_terms[0], kv_terms[1]), ("seq_x", "seq_z"))
    feat_split = normed.reshape(tok_rows, chips, 2, normed.shape[1] // (2 * chips))
    normed_keep = lax.dynamic_index_in_dim(feat_split, core, axis=2, keepdims=False)
    normed_send = lax.dynamic_index_in_dim(feat_split, 1 - core, axis=2, keepdims=False)
    tokens_first = (((0,), (0,)), ((), ()))

    def weight_terms(grads):
        keep = lax.dot_general(normed_keep, grads, tokens_first, preferred_element_type=jnp.float32)
        send = lax.dot_general(normed_send, grads, tokens_first, preferred_element_type=jnp.float32)
        return scatter_sum(pair_sum(keep, send), ("seq_x", "seq_z"))

    grad_wq = weight_terms(query_grad)
    contract = (((1,), (1,)), ((), ()))
    partial_input = lax.dot_general(
        w_query, query_grad, contract, preferred_element_type=jnp.float32
    )
    key_grad = rotate(kv_total[:, :HEAD], positions, -1.0).astype(jnp.bfloat16)
    value_grad = kv_total[:, HEAD:].astype(jnp.bfloat16)
    kv_grad = jnp.concatenate([key_grad, value_grad], axis=1)
    grad_wkv = weight_terms(kv_grad)
    grad_wk = grad_wkv[:, :HEAD]
    grad_wv = grad_wkv[:, HEAD:]
    partial_input = partial_input + lax.dot_general(
        w_key, key_grad, contract, preferred_element_type=jnp.float32
    )
    partial_input = partial_input + lax.dot_general(
        w_value, value_grad, contract, preferred_element_type=jnp.float32
    )
    feat = partial_input.shape[0] // kvh_count
    input_terms = partial_input.astype(jnp.bfloat16).reshape(kvh_count, feat, tok_rows)
    grad_normed = scatter_sum(input_terms, KVH_AXES).T.astype(jnp.bfloat16)
    return (grad_normed, grad_wq, grad_wk, grad_wv)


def solution(mesh):
    seq_x = 2
    seq_size = mesh.shape["seq"]
    kvh_size = mesh.shape["kvh"]
    grid = mesh.devices.reshape(seq_x, seq_size // (2 * seq_x), 2, 2, kvh_size // 2)
    fine = jax.sharding.Mesh(grid, SEQ_AXES + KVH_AXES)
    in_specs = (
        P(SEQ_AXES, None),
        P(None, KVH_AXES),
        P(None, KVH_AXES),
        P(None, KVH_AXES),
        P(SEQ_AXES),
        P(SEQ_AXES, None),
        P(SEQ_AXES, KVH_AXES),
    )
    out_specs = (P(SEQ_AXES, KVH_AXES),) * 4
    return jax.shard_map(body, mesh=fine, in_specs=in_specs, out_specs=out_specs, check_vma=False)
```

```python
import jax
import jax.numpy as jnp
from jax import lax
from jax.sharding import PartitionSpec as P

HEAD = 128
BLOCK = 128


THETA = 500000.0


def rotate(values, positions, rotation_sign):
    tok_rows = values.shape[0]
    head_count = values.shape[1] // HEAD
    half_size = HEAD // 2
    pieces = values.reshape(tok_rows, head_count, HEAD)
    frequency = THETA ** (-(jnp.arange(half_size, dtype=jnp.float32) * (2.0 / HEAD)))
    angles = positions.astype(jnp.float32)[:, None] * frequency[None, :]
    cosine = jnp.cos(angles)[:, None, :]
    sine_part = rotation_sign * jnp.sin(angles)[:, None, :]
    lower_half = pieces[:, :, :half_size]
    upper_half = pieces[:, :, half_size:]
    turned = jnp.concatenate(
        [
            lower_half * cosine - upper_half * sine_part,
            upper_half * cosine + lower_half * sine_part,
        ],
        axis=2,
    )
    return turned.reshape(tok_rows, head_count * HEAD)


def visible(mask_rows, query_block0, query_count, chunk_blocks, key_inner):
    query_local = jnp.arange(query_count)
    query_block = query_block0 + query_local // BLOCK
    table = jnp.take(mask_rows, chunk_blocks, axis=1) == 1
    key_blocks = jnp.repeat(chunk_blocks, BLOCK)
    allowed = jnp.repeat(jnp.repeat(table, BLOCK, axis=0), BLOCK, axis=1)
    inner_ok = key_inner[None, :] <= (query_local % BLOCK)[:, None]
    return allowed & ((query_block[:, None] != key_blocks[None, :]) | inner_ok)


def product(form, left, right):
    return jnp.einsum(form, left, right, preferred_element_type=jnp.float32)


def masked_scores(queries, keys, seen):
    scores = product("tgd,sd->gts", queries, keys) * HEAD ** (-0.5)
    return jnp.where(seen[None], scores, -1e30)


def softmax_stats(queries, keys, values, grad_heads, seen):
    scores = masked_scores(queries, keys, seen)
    row_max = jnp.max(scores, axis=2, keepdims=True)
    log_total = row_max[:, :, 0] + jnp.log(jnp.sum(jnp.exp(scores - row_max), axis=2))
    weights = jnp.where(seen[None], jnp.exp(scores - log_total[:, :, None]), 0.0).astype(
        jnp.bfloat16
    )
    outputs = product("gts,sd->gtd", weights, values)
    row_dots = jnp.sum(outputs * jnp.transpose(grad_heads.astype(jnp.float32), (1, 0, 2)), axis=2)
    return (log_total, row_dots)


def attention_grads(queries, keys, values, grad_heads, seen, log_total, row_dots):
    scores = masked_scores(queries, keys, seen)
    probs = jnp.where(seen[None], jnp.exp(scores - log_total[:, :, None]), 0.0)
    weights = probs.astype(jnp.bfloat16)
    grad_probs = product("tgd,sd->gts", grad_heads, values)
    grad_scores = (probs * (grad_probs - row_dots[:, :, None]) * HEAD ** (-0.5)).astype(
        jnp.bfloat16
    )
    grad_query = product("gts,sd->tgd", grad_scores, keys)
    grad_key = product("gts,tgd->sd", grad_scores, queries)
    grad_value = product("gts,tgd->sd", weights, grad_heads)
    return (grad_query, grad_key, grad_value)


SEQ_AXES = ("seq_x", "seq_z", "seq_core")
KVH_AXES = ("kvh_x", "kvh_y")
PAIR = [(0, 1), (1, 0)]


def seq_position():
    return (lax.axis_index("seq_x") * lax.axis_size("seq_z") + lax.axis_index("seq_z")) * 2 + lax.axis_index(
        "seq_core"
    )


def gather_rows(block):
    chips = lax.axis_size("seq_x") * lax.axis_size("seq_z")
    copies = jnp.broadcast_to(block[None], (chips,) + block.shape)
    mine = lax.all_to_all(copies, ("seq_x", "seq_z"), 0, 0, tiled=True)
    other = lax.ppermute(mine, "seq_core", PAIR)
    joined = jnp.stack([mine, other], axis=0)
    return joined.reshape((2 * chips * block.shape[0],) + block.shape[1:])


def pair_sum(keep, send):
    got = lax.ppermute(send.astype(jnp.bfloat16), "seq_core", PAIR)
    return (keep.astype(jnp.float32) + got.astype(jnp.float32)).astype(jnp.bfloat16)


def scatter_sum(parts, axis):
    arrived = lax.all_to_all(parts, axis, 0, 0, tiled=True)
    return jnp.sum(arrived.astype(jnp.float32), axis=0)


def body(normed, w_query, w_key, w_value, positions, block_mask, grad_attn):
    tok_rows = normed.shape[0]
    group_size = w_query.shape[1] // w_key.shape[1]
    width_query = group_size * HEAD
    blk_local = tok_rows // BLOCK
    chips = lax.axis_size("seq_x") * lax.axis_size("seq_z")
    kvh_count = lax.axis_size("kvh_x") * lax.axis_size("kvh_y")
    core = lax.axis_index("seq_core")
    my_index = seq_position()
    queries = rotate(
        jnp.dot(normed, w_query, preferred_element_type=jnp.float32), positions, 1.0
    ).astype(jnp.bfloat16)
    keys = rotate(
        jnp.dot(normed, w_key, preferred_element_type=jnp.float32), positions, 1.0
    ).astype(jnp.bfloat16)
    values = jnp.dot(normed, w_value, preferred_element_type=jnp.float32).astype(jnp.bfloat16)
    kv_all = gather_rows(jnp.concatenate([keys, values], axis=1))
    keys_all = kv_all[:, :HEAD]
    values_all = kv_all[:, HEAD:]
    key_count = keys_all.shape[0]
    chunk = jnp.arange(key_count // BLOCK)
    per_shard = tok_rows // BLOCK
    side = chunk // (chips * per_shard)
    chip = (chunk // per_shard) % chips
    chunk_blocks = (chip * 2 + jnp.where(side == 0, core, 1 - core)) * per_shard + chunk % per_shard
    seen = visible(block_mask, my_index * blk_local, tok_rows, chunk_blocks, jnp.arange(key_count) % BLOCK)
    query_heads = queries.reshape(tok_rows, group_size, HEAD)
    grad_heads = grad_attn.reshape(tok_rows, group_size, HEAD)
    log_total, row_dots = softmax_stats(query_heads, keys_all, values_all, grad_heads, seen)
    grad_query, grad_key, grad_value = attention_grads(
        query_heads, keys_all, values_all, grad_heads, seen, log_total, row_dots
    )
    query_grad = rotate(grad_query.reshape(tok_rows, width_query), positions, -1.0).astype(
        jnp.bfloat16
    )
    kv_terms = jnp.concatenate([grad_key, grad_value], axis=1).reshape(2, chips, tok_rows, 2 * HEAD)
    feat_split = normed.reshape(tok_rows, chips, 2, normed.shape[1] // (2 * chips))
    normed_even = feat_split[:, :, 0, :]
    normed_odd = feat_split[:, :, 1, :]
    tokens_first = (((0,), (0,)), ((), ()))
    first = core == 0

    def weight_halves(grads):
        even = lax.dot_general(normed_even, grads, tokens_first, preferred_element_type=jnp.float32)
        odd = lax.dot_general(normed_odd, grads, tokens_first, preferred_element_type=jnp.float32)
        return jnp.where(first, even, odd), jnp.where(first, odd, even)

    wq_keep, wq_send = weight_halves(query_grad)
    joint = pair_sum(
        jnp.concatenate([kv_terms[0], wq_keep], axis=2), jnp.concatenate([kv_terms[1], wq_send], axis=2)
    )
    joint_total = scatter_sum(joint, ("seq_x", "seq_z"))
    kv_total = joint_total[:, : 2 * HEAD]
    grad_wq = joint_total[:, 2 * HEAD :]

    def weight_terms(grads):
        keep, send = weight_halves(grads)
        return scatter_sum(pair_sum(keep, send), ("seq_x", "seq_z"))

    contract = (((1,), (1,)), ((), ()))
    partial_input = lax.dot_general(
        w_query, query_grad, contract, preferred_element_type=jnp.float32
    )
    key_grad = rotate(kv_total[:, :HEAD], positions, -1.0).astype(jnp.bfloat16)
    value_grad = kv_total[:, HEAD:].astype(jnp.bfloat16)
    kv_grad = jnp.concatenate([key_grad, value_grad], axis=1)
    grad_wkv = weight_terms(kv_grad)
    grad_wk = grad_wkv[:, :HEAD]
    grad_wv = grad_wkv[:, HEAD:]
    partial_input = partial_input + lax.dot_general(
        w_key, key_grad, contract, preferred_element_type=jnp.float32
    )
    partial_input = partial_input + lax.dot_general(
        w_value, value_grad, contract, preferred_element_type=jnp.float32
    )
    feat = partial_input.shape[0] // kvh_count
    input_terms = partial_input.astype(jnp.bfloat16).reshape(kvh_count, feat, tok_rows)
    grad_normed = scatter_sum(input_terms, KVH_AXES).T.astype(jnp.bfloat16)
    return (grad_normed, grad_wq, grad_wk, grad_wv)


def solution(mesh):
    seq_x = 2
    seq_size = mesh.shape["seq"]
    kvh_size = mesh.shape["kvh"]
    grid = mesh.devices.reshape(seq_x, seq_size // (2 * seq_x), 2, 2, kvh_size // 2)
    fine = jax.sharding.Mesh(grid, SEQ_AXES + KVH_AXES)
    in_specs = (
        P(SEQ_AXES, None),
        P(None, KVH_AXES),
        P(None, KVH_AXES),
        P(None, KVH_AXES),
        P(SEQ_AXES),
        P(SEQ_AXES, None),
        P(SEQ_AXES, KVH_AXES),
    )
    out_specs = (P(SEQ_AXES, KVH_AXES),) * 4
    return jax.shard_map(body, mesh=fine, in_specs=in_specs, out_specs=out_specs, check_vma=False)
```

```python
import jax
import jax.numpy as jnp
from jax import lax
from jax.sharding import PartitionSpec as P

HEAD = 128
BLOCK = 128


THETA = 500000.0


def rotate(values, positions, rotation_sign):
    tok_rows = values.shape[0]
    head_count = values.shape[1] // HEAD
    half_size = HEAD // 2
    pieces = values.reshape(tok_rows, head_count, HEAD)
    frequency = THETA ** (-(jnp.arange(half_size, dtype=jnp.float32) * (2.0 / HEAD)))
    angles = positions.astype(jnp.float32)[:, None] * frequency[None, :]
    cosine = jnp.cos(angles)[:, None, :]
    sine_part = rotation_sign * jnp.sin(angles)[:, None, :]
    lower_half = pieces[:, :, :half_size]
    upper_half = pieces[:, :, half_size:]
    turned = jnp.concatenate(
        [
            lower_half * cosine - upper_half * sine_part,
            upper_half * cosine + lower_half * sine_part,
        ],
        axis=2,
    )
    return turned.reshape(tok_rows, head_count * HEAD)


def visible(mask_rows, query_block0, query_count, chunk_blocks, key_inner):
    query_local = jnp.arange(query_count)
    query_block = query_block0 + query_local // BLOCK
    table = jnp.take(mask_rows, chunk_blocks, axis=1) == 1
    key_blocks = jnp.repeat(chunk_blocks, BLOCK)
    allowed = jnp.repeat(jnp.repeat(table, BLOCK, axis=0), BLOCK, axis=1)
    inner_ok = key_inner[None, :] <= (query_local % BLOCK)[:, None]
    return allowed & ((query_block[:, None] != key_blocks[None, :]) | inner_ok)


def product(form, left, right):
    return jnp.einsum(form, left, right, preferred_element_type=jnp.float32)


def masked_scores(queries, keys, seen):
    scores = product("tgd,sd->gts", queries, keys) * HEAD ** (-0.5)
    return jnp.where(seen[None], scores, -1e30)


def softmax_stats(queries, keys, values, grad_heads, seen):
    scores = masked_scores(queries, keys, seen)
    row_max = jnp.max(scores, axis=2, keepdims=True)
    log_total = row_max[:, :, 0] + jnp.log(jnp.sum(jnp.exp(scores - row_max), axis=2))
    weights = jnp.where(seen[None], jnp.exp(scores - log_total[:, :, None]), 0.0).astype(
        jnp.bfloat16
    )
    outputs = product("gts,sd->gtd", weights, values)
    row_dots = jnp.sum(outputs * jnp.transpose(grad_heads.astype(jnp.float32), (1, 0, 2)), axis=2)
    return (log_total, row_dots)


def attention_grads(queries, keys, values, grad_heads, seen, log_total, row_dots):
    scores = masked_scores(queries, keys, seen)
    probs = jnp.where(seen[None], jnp.exp(scores - log_total[:, :, None]), 0.0)
    weights = probs.astype(jnp.bfloat16)
    grad_probs = product("tgd,sd->gts", grad_heads, values)
    grad_scores = (probs * (grad_probs - row_dots[:, :, None]) * HEAD ** (-0.5)).astype(
        jnp.bfloat16
    )
    grad_query = product("gts,sd->tgd", grad_scores, keys)
    grad_key = product("gts,tgd->sd", grad_scores, queries)
    grad_value = product("gts,tgd->sd", weights, grad_heads)
    return (grad_query, grad_key, grad_value)


SEQ_AXES = ("seq_x", "seq_z", "seq_core")
KVH_AXES = ("kvh_x", "kvh_y")
PAIR = [(0, 1), (1, 0)]


def seq_position():
    return (lax.axis_index("seq_x") * lax.axis_size("seq_z") + lax.axis_index("seq_z")) * 2 + lax.axis_index(
        "seq_core"
    )


def swap(value, axis):
    return lax.ppermute(value, axis, PAIR)


def ordered_pair(value, axis):
    return jnp.stack([value, swap(value, axis)], axis=0)


def gather_rows(block):
    z_count = lax.axis_size("seq_z")
    by_x = ordered_pair(block, "seq_x")
    copies = jnp.broadcast_to(by_x[None], (z_count,) + by_x.shape)
    by_z = lax.all_to_all(copies, "seq_z", 0, 0, tiled=True)
    by_core = ordered_pair(by_z, "seq_core")
    return by_core.reshape((-1,) + block.shape[1:])


def reduce_rows(terms):
    got = swap(terms[1].astype(jnp.bfloat16), "seq_core")
    level = (terms[0].astype(jnp.float32) + got.astype(jnp.float32)).astype(jnp.bfloat16)
    arrived = lax.all_to_all(level, "seq_z", 0, 0, tiled=True)
    level = jnp.sum(arrived.astype(jnp.float32), axis=0)
    got = swap(level[1].astype(jnp.bfloat16), "seq_x")
    return level[0] + got.astype(jnp.float32)


def body(normed, w_query, w_key, w_value, positions, block_mask, grad_attn):
    tok_rows = normed.shape[0]
    group_size = w_query.shape[1] // w_key.shape[1]
    width_query = group_size * HEAD
    blk_local = tok_rows // BLOCK
    z_count = lax.axis_size("seq_z")
    core = lax.axis_index("seq_core")
    x_hi = lax.axis_index("seq_x")
    my_index = seq_position()
    queries = rotate(
        jnp.dot(normed, w_query, preferred_element_type=jnp.float32), positions, 1.0
    ).astype(jnp.bfloat16)
    keys = rotate(
        jnp.dot(normed, w_key, preferred_element_type=jnp.float32), positions, 1.0
    ).astype(jnp.bfloat16)
    values = jnp.dot(normed, w_value, preferred_element_type=jnp.float32).astype(jnp.bfloat16)
    kv_all = gather_rows(jnp.concatenate([keys, values], axis=1))
    keys_all = kv_all[:, :HEAD]
    values_all = kv_all[:, HEAD:]
    key_count = keys_all.shape[0]
    per_shard = tok_rows // BLOCK
    chunk = jnp.arange(key_count // BLOCK)
    core_side = chunk // (z_count * 2 * per_shard)
    z_src = (chunk // (2 * per_shard)) % z_count
    x_side = (chunk // per_shard) % 2
    source = (jnp.where(x_side == 0, x_hi, 1 - x_hi) * z_count + z_src) * 2 + jnp.where(
        core_side == 0, core, 1 - core
    )
    chunk_blocks = source * per_shard + chunk % per_shard
    seen = visible(block_mask, my_index * blk_local, tok_rows, chunk_blocks, jnp.arange(key_count) % BLOCK)
    query_heads = queries.reshape(tok_rows, group_size, HEAD)
    grad_heads = grad_attn.reshape(tok_rows, group_size, HEAD)
    log_total, row_dots = softmax_stats(query_heads, keys_all, values_all, grad_heads, seen)
    grad_query, grad_key, grad_value = attention_grads(
        query_heads, keys_all, values_all, grad_heads, seen, log_total, row_dots
    )
    query_grad = rotate(grad_query.reshape(tok_rows, width_query), positions, -1.0).astype(
        jnp.bfloat16
    )
    kv_terms = jnp.concatenate([grad_key, grad_value], axis=1)
    by_feature = normed.reshape(tok_rows, 2, z_count, 2, normed.shape[1] // (4 * z_count))
    by_feature = jnp.transpose(by_feature, (0, 3, 2, 1, 4))
    by_feature = jnp.where(core == 0, by_feature, by_feature[:, ::-1])
    by_feature = jnp.where(x_hi == 0, by_feature, by_feature[:, :, :, ::-1])
    normed_perm = by_feature.reshape(tok_rows, normed.shape[1])
    tokens_first = (((0,), (0,)), ((), ()))
    feat_rows = normed.shape[1] // (4 * z_count)

    def weight_terms(grads):
        full = lax.dot_general(normed_perm, grads, tokens_first, preferred_element_type=jnp.float32)
        return full.reshape((2, z_count, 2, feat_rows) + grads.shape[1:])

    joint = jnp.concatenate(
        [kv_terms.reshape((2, z_count, 2, tok_rows) + kv_terms.shape[1:]), weight_terms(query_grad)],
        axis=-1,
    )
    joint_total = reduce_rows(joint)
    kv_total = joint_total[:, : 2 * HEAD]
    grad_wq = joint_total[:, 2 * HEAD :]
    contract = (((1,), (1,)), ((), ()))
    partial_input = lax.dot_general(
        w_query, query_grad, contract, preferred_element_type=jnp.float32
    )
    key_grad = rotate(kv_total[:, :HEAD], positions, -1.0).astype(jnp.bfloat16)
    value_grad = kv_total[:, HEAD:].astype(jnp.bfloat16)
    kv_grad = jnp.concatenate([key_grad, value_grad], axis=1)
    grad_wkv = reduce_rows(weight_terms(kv_grad))
    grad_wk = grad_wkv[:, :HEAD]
    grad_wv = grad_wkv[:, HEAD:]
    partial_input = partial_input + lax.dot_general(
        w_key, key_grad, contract, preferred_element_type=jnp.float32
    )
    partial_input = partial_input + lax.dot_general(
        w_value, value_grad, contract, preferred_element_type=jnp.float32
    )
    y_count = lax.axis_size("kvh_y")
    input_terms = partial_input.reshape((2, y_count, -1, tok_rows))
    first = lax.axis_index("kvh_x") == 0
    keep = jnp.where(first, input_terms[0], input_terms[1])
    send = jnp.where(first, input_terms[1], input_terms[0]).astype(jnp.bfloat16)
    level = (keep + swap(send, "kvh_x").astype(jnp.float32)).astype(jnp.bfloat16)
    arrived = lax.all_to_all(level, "kvh_y", 0, 0, tiled=True)
    grad_normed = jnp.sum(arrived.astype(jnp.float32), axis=0).T.astype(jnp.bfloat16)
    return (grad_normed, grad_wq, grad_wk, grad_wv)


def solution(mesh):
    seq_x = 2
    seq_size = mesh.shape["seq"]
    kvh_size = mesh.shape["kvh"]
    grid = mesh.devices.reshape(seq_x, seq_size // (2 * seq_x), 2, 2, kvh_size // 2)
    fine = jax.sharding.Mesh(grid, SEQ_AXES + KVH_AXES)
    in_specs = (
        P(SEQ_AXES, None),
        P(None, KVH_AXES),
        P(None, KVH_AXES),
        P(None, KVH_AXES),
        P(SEQ_AXES),
        P(SEQ_AXES, None),
        P(SEQ_AXES, KVH_AXES),
    )
    out_specs = (P(SEQ_AXES, KVH_AXES),) * 4
    return jax.shard_map(body, mesh=fine, in_specs=in_specs, out_specs=out_specs, check_vma=False)
```

```python
import jax
import jax.numpy as jnp
from jax import lax
from jax.sharding import PartitionSpec as P

HEAD = 128
BLOCK = 128


THETA = 500000.0


def rotate(values, positions, rotation_sign):
    tok_rows = values.shape[0]
    head_count = values.shape[1] // HEAD
    half_size = HEAD // 2
    pieces = values.reshape(tok_rows, head_count, HEAD)
    frequency = THETA ** (-(jnp.arange(half_size, dtype=jnp.float32) * (2.0 / HEAD)))
    angles = positions.astype(jnp.float32)[:, None] * frequency[None, :]
    cosine = jnp.cos(angles)[:, None, :]
    sine_part = rotation_sign * jnp.sin(angles)[:, None, :]
    lower_half = pieces[:, :, :half_size]
    upper_half = pieces[:, :, half_size:]
    turned = jnp.concatenate(
        [
            lower_half * cosine - upper_half * sine_part,
            upper_half * cosine + lower_half * sine_part,
        ],
        axis=2,
    )
    return turned.reshape(tok_rows, head_count * HEAD)


def visible(mask_rows, query_block0, query_count, chunk_blocks, key_inner):
    query_local = jnp.arange(query_count)
    query_block = query_block0 + query_local // BLOCK
    table = jnp.take(mask_rows, chunk_blocks, axis=1) == 1
    key_blocks = jnp.repeat(chunk_blocks, BLOCK)
    allowed = jnp.repeat(jnp.repeat(table, BLOCK, axis=0), BLOCK, axis=1)
    inner_ok = key_inner[None, :] <= (query_local % BLOCK)[:, None]
    return allowed & ((query_block[:, None] != key_blocks[None, :]) | inner_ok)


def product(form, left, right):
    return jnp.einsum(form, left, right, preferred_element_type=jnp.float32)


def masked_scores(queries, keys, seen):
    scores = product("tgd,sd->gts", queries, keys) * HEAD ** (-0.5)
    return jnp.where(seen[None], scores, -1e30)


def softmax_stats(queries, keys, values, grad_heads, seen):
    scores = masked_scores(queries, keys, seen)
    row_max = jnp.max(scores, axis=2, keepdims=True)
    log_total = row_max[:, :, 0] + jnp.log(jnp.sum(jnp.exp(scores - row_max), axis=2))
    weights = jnp.where(seen[None], jnp.exp(scores - log_total[:, :, None]), 0.0).astype(
        jnp.bfloat16
    )
    outputs = product("gts,sd->gtd", weights, values)
    row_dots = jnp.sum(outputs * jnp.transpose(grad_heads.astype(jnp.float32), (1, 0, 2)), axis=2)
    return (log_total, row_dots)


def attention_grads(queries, keys, values, grad_heads, seen, log_total, row_dots):
    scores = masked_scores(queries, keys, seen)
    probs = jnp.where(seen[None], jnp.exp(scores - log_total[:, :, None]), 0.0)
    weights = probs.astype(jnp.bfloat16)
    grad_probs = product("tgd,sd->gts", grad_heads, values)
    grad_scores = (probs * (grad_probs - row_dots[:, :, None]) * HEAD ** (-0.5)).astype(
        jnp.bfloat16
    )
    grad_query = product("gts,sd->tgd", grad_scores, keys)
    grad_key = product("gts,tgd->sd", grad_scores, queries)
    grad_value = product("gts,tgd->sd", weights, grad_heads)
    return (grad_query, grad_key, grad_value)


SEQ_AXES = ("seq_x", "seq_z", "seq_core")
KVH_AXES = ("kvh_x", "kvh_y")
PAIR = [(0, 1), (1, 0)]


def seq_position():
    return (lax.axis_index("seq_x") * lax.axis_size("seq_z") + lax.axis_index("seq_z")) * 2 + lax.axis_index(
        "seq_core"
    )


def gather_rows(block):
    chips = lax.axis_size("seq_x") * lax.axis_size("seq_z")
    copies = jnp.broadcast_to(block[None], (chips,) + block.shape)
    mine = lax.all_to_all(copies, ("seq_x", "seq_z"), 0, 0, tiled=True)
    other = lax.ppermute(mine, "seq_core", PAIR)
    joined = jnp.stack([mine, other], axis=0)
    return joined.reshape((2 * chips * block.shape[0],) + block.shape[1:])


def pair_sum(keep, send):
    got = lax.ppermute(send.astype(jnp.bfloat16), "seq_core", PAIR)
    return (keep.astype(jnp.float32) + got.astype(jnp.float32)).astype(jnp.bfloat16)


def scatter_sum(parts, axis):
    arrived = lax.all_to_all(parts, axis, 0, 0, tiled=True)
    return jnp.sum(arrived.astype(jnp.float32), axis=0)


def body(normed, w_query, w_key, w_value, positions, block_mask, grad_attn):
    tok_rows = normed.shape[0]
    group_size = w_query.shape[1] // w_key.shape[1]
    width_query = group_size * HEAD
    blk_local = tok_rows // BLOCK
    chips = lax.axis_size("seq_x") * lax.axis_size("seq_z")
    kvh_count = lax.axis_size("kvh_x") * lax.axis_size("kvh_y")
    core = lax.axis_index("seq_core")
    my_index = seq_position()
    queries = rotate(
        jnp.dot(normed, w_query, preferred_element_type=jnp.float32), positions, 1.0
    ).astype(jnp.bfloat16)
    keys = rotate(
        jnp.dot(normed, w_key, preferred_element_type=jnp.float32), positions, 1.0
    ).astype(jnp.bfloat16)
    values = jnp.dot(normed, w_value, preferred_element_type=jnp.float32).astype(jnp.bfloat16)
    kv_all = gather_rows(jnp.concatenate([keys, values], axis=1))
    keys_all = kv_all[:, :HEAD]
    values_all = kv_all[:, HEAD:]
    key_count = keys_all.shape[0]
    chunk = jnp.arange(key_count // BLOCK)
    per_shard = tok_rows // BLOCK
    side = chunk // (chips * per_shard)
    chip = (chunk // per_shard) % chips
    chunk_blocks = (chip * 2 + jnp.where(side == 0, core, 1 - core)) * per_shard + chunk % per_shard
    seen = visible(block_mask, my_index * blk_local, tok_rows, chunk_blocks, jnp.arange(key_count) % BLOCK)
    query_heads = queries.reshape(tok_rows, group_size, HEAD)
    grad_heads = grad_attn.reshape(tok_rows, group_size, HEAD)
    log_total, row_dots = softmax_stats(query_heads, keys_all, values_all, grad_heads, seen)
    grad_query, grad_key, grad_value = attention_grads(
        query_heads, keys_all, values_all, grad_heads, seen, log_total, row_dots
    )
    query_grad = rotate(grad_query.reshape(tok_rows, width_query), positions, -1.0).astype(
        jnp.bfloat16
    )
    kv_terms = jnp.concatenate([grad_key, grad_value], axis=1).reshape(2, chips, tok_rows, 2 * HEAD)
    feat_split = normed.reshape(tok_rows, chips, 2, normed.shape[1] // (2 * chips))
    normed_even = feat_split[:, :, 0, :]
    normed_odd = feat_split[:, :, 1, :]
    tokens_first = (((0,), (0,)), ((), ()))
    first = core == 0

    def weight_halves(grads):
        even = lax.dot_general(normed_even, grads, tokens_first, preferred_element_type=jnp.float32)
        odd = lax.dot_general(normed_odd, grads, tokens_first, preferred_element_type=jnp.float32)
        return jnp.where(first, even, odd), jnp.where(first, odd, even)

    kv_total = scatter_sum(pair_sum(kv_terms[0], kv_terms[1]), ("seq_x", "seq_z"))
    wq_keep, wq_send = weight_halves(query_grad)
    wq_terms = pair_sum(wq_keep, wq_send)
    grad_wq = lax.psum_scatter(
        wq_terms.reshape((-1,) + wq_terms.shape[2:]), ("seq_x", "seq_z"), scatter_dimension=0, tiled=True
    ).astype(jnp.float32)

    def weight_terms(grads):
        keep, send = weight_halves(grads)
        return scatter_sum(pair_sum(keep, send), ("seq_x", "seq_z"))

    contract = (((1,), (1,)), ((), ()))
    partial_input = lax.dot_general(
        w_query, query_grad, contract, preferred_element_type=jnp.float32
    )
    key_grad = rotate(kv_total[:, :HEAD], positions, -1.0).astype(jnp.bfloat16)
    value_grad = kv_total[:, HEAD:].astype(jnp.bfloat16)
    kv_grad = jnp.concatenate([key_grad, value_grad], axis=1)
    grad_wkv = weight_terms(kv_grad)
    grad_wk = grad_wkv[:, :HEAD]
    grad_wv = grad_wkv[:, HEAD:]
    partial_input = partial_input + lax.dot_general(
        w_key, key_grad, contract, preferred_element_type=jnp.float32
    )
    partial_input = partial_input + lax.dot_general(
        w_value, value_grad, contract, preferred_element_type=jnp.float32
    )
    feat = partial_input.shape[0] // kvh_count
    input_terms = partial_input.astype(jnp.bfloat16).reshape(kvh_count, feat, tok_rows)
    grad_normed = scatter_sum(input_terms, KVH_AXES).T.astype(jnp.bfloat16)
    return (grad_normed, grad_wq, grad_wk, grad_wv)


def solution(mesh):
    seq_x = 2
    seq_size = mesh.shape["seq"]
    kvh_size = mesh.shape["kvh"]
    grid = mesh.devices.reshape(seq_x, seq_size // (2 * seq_x), 2, 2, kvh_size // 2)
    fine = jax.sharding.Mesh(grid, SEQ_AXES + KVH_AXES)
    in_specs = (
        P(SEQ_AXES, None),
        P(None, KVH_AXES),
        P(None, KVH_AXES),
        P(None, KVH_AXES),
        P(SEQ_AXES),
        P(SEQ_AXES, None),
        P(SEQ_AXES, KVH_AXES),
    )
    out_specs = (P(SEQ_AXES, KVH_AXES),) * 4
    return jax.shard_map(body, mesh=fine, in_specs=in_specs, out_specs=out_specs, check_vma=False)
```

```python
import jax
import jax.numpy as jnp
from jax import lax
from jax.sharding import PartitionSpec as P
from jax.experimental import pallas as pl
from jax.experimental.pallas import tpu as pltpu

HEAD = 128
BLOCK = 128


THETA = 500000.0


def rotate(values, positions, rotation_sign):
    tok_rows = values.shape[0]
    head_count = values.shape[1] // HEAD
    half_size = HEAD // 2
    pieces = values.reshape(tok_rows, head_count, HEAD)
    frequency = THETA ** (-(jnp.arange(half_size, dtype=jnp.float32) * (2.0 / HEAD)))
    angles = positions.astype(jnp.float32)[:, None] * frequency[None, :]
    cosine = jnp.cos(angles)[:, None, :]
    sine_part = rotation_sign * jnp.sin(angles)[:, None, :]
    lower_half = pieces[:, :, :half_size]
    upper_half = pieces[:, :, half_size:]
    turned = jnp.concatenate(
        [
            lower_half * cosine - upper_half * sine_part,
            upper_half * cosine + lower_half * sine_part,
        ],
        axis=2,
    )
    return turned.reshape(tok_rows, head_count * HEAD)


def visible(mask_rows, query_block0, query_count, chunk_blocks, key_inner):
    query_local = jnp.arange(query_count)
    query_block = query_block0 + query_local // BLOCK
    table = jnp.take(mask_rows, chunk_blocks, axis=1) == 1
    key_blocks = jnp.repeat(chunk_blocks, BLOCK)
    allowed = jnp.repeat(jnp.repeat(table, BLOCK, axis=0), BLOCK, axis=1)
    inner_ok = key_inner[None, :] <= (query_local % BLOCK)[:, None]
    return allowed & ((query_block[:, None] != key_blocks[None, :]) | inner_ok)


def product(form, left, right):
    return jnp.einsum(form, left, right, preferred_element_type=jnp.float32)


def masked_scores(queries, keys, seen):
    scores = product("tgd,sd->gts", queries, keys) * HEAD ** (-0.5)
    return jnp.where(seen[None], scores, -1e30)


def softmax_stats(queries, keys, values, grad_heads, seen):
    scores = masked_scores(queries, keys, seen)
    row_max = jnp.max(scores, axis=2, keepdims=True)
    log_total = row_max[:, :, 0] + jnp.log(jnp.sum(jnp.exp(scores - row_max), axis=2))
    weights = jnp.where(seen[None], jnp.exp(scores - log_total[:, :, None]), 0.0).astype(
        jnp.bfloat16
    )
    outputs = product("gts,sd->gtd", weights, values)
    row_dots = jnp.sum(outputs * jnp.transpose(grad_heads.astype(jnp.float32), (1, 0, 2)), axis=2)
    return (log_total, row_dots)


def attention_grads(queries, keys, values, grad_heads, seen, log_total, row_dots):
    scores = masked_scores(queries, keys, seen)
    probs = jnp.where(seen[None], jnp.exp(scores - log_total[:, :, None]), 0.0)
    weights = probs.astype(jnp.bfloat16)
    grad_probs = product("tgd,sd->gts", grad_heads, values)
    grad_scores = (probs * (grad_probs - row_dots[:, :, None]) * HEAD ** (-0.5)).astype(
        jnp.bfloat16
    )
    grad_query = product("gts,sd->tgd", grad_scores, keys)
    grad_key = product("gts,tgd->sd", grad_scores, queries)
    grad_value = product("gts,tgd->sd", weights, grad_heads)
    return (grad_query, grad_key, grad_value)


SEQ_AXES = ("seq_x", "seq_z", "seq_core")
KVH_AXES = ("kvh_x", "kvh_y")
PAIR = [(0, 1), (1, 0)]


def seq_position():
    return (lax.axis_index("seq_x") * lax.axis_size("seq_z") + lax.axis_index("seq_z")) * 2 + lax.axis_index(
        "seq_core"
    )


KEY_CHUNK = 512


def attention_kernel(seen_ref, q_ref, k_ref, v_ref, do_ref, dq_ref, dk_ref, dv_ref, s_scr, dp_scr):
    head = pl.program_id(0)
    scale = HEAD ** (-0.5)
    q = q_ref[0]
    grad_out = do_ref[0]
    rows = q.shape[0]
    chunks = k_ref.shape[0] // KEY_CHUNK
    nt = (((1,), (1,)), ((), ()))
    tn = (((0,), (0,)), ((), ()))

    def window(j):
        return pl.ds(pl.multiple_of(j * KEY_CHUNK, KEY_CHUNK), KEY_CHUNK)

    def scores_pass(j, top):
        cols = window(j)
        s = lax.dot_general(q, k_ref[cols, :], nt, preferred_element_type=jnp.float32) * scale
        s = jnp.where(seen_ref[:, cols] > 0, s, -1e30)
        s_scr[:, cols] = s
        dp_scr[:, cols] = lax.dot_general(
            grad_out, v_ref[cols, :], nt, preferred_element_type=jnp.float32
        )
        return jnp.maximum(top, jnp.max(s, axis=1, keepdims=True))

    top = lax.fori_loop(0, chunks, scores_pass, jnp.full((rows, 1), -jnp.inf, jnp.float32))

    def total_pass(j, total):
        s = s_scr[:, window(j)]
        return total + jnp.sum(jnp.exp(s - top), axis=1, keepdims=True)

    total = lax.fori_loop(0, chunks, total_pass, jnp.zeros((rows, 1), jnp.float32))
    log_total = top + jnp.log(total)

    def dots_pass(j, dots):
        cols = window(j)
        probs = jnp.where(seen_ref[:, cols] > 0, jnp.exp(s_scr[:, cols] - log_total), 0.0)
        s_scr[:, cols] = probs
        weights = probs.astype(jnp.bfloat16).astype(jnp.float32)
        return dots + jnp.sum(weights * dp_scr[:, cols], axis=1, keepdims=True)

    row_dots = lax.fori_loop(0, chunks, dots_pass, jnp.zeros((rows, 1), jnp.float32))

    @pl.when(head == 0)
    def _():
        dk_ref[...] = jnp.zeros_like(dk_ref)
        dv_ref[...] = jnp.zeros_like(dv_ref)

    def grads_pass(j, dq):
        cols = window(j)
        probs = s_scr[:, cols]
        weights = probs.astype(jnp.bfloat16)
        grad_scores = (probs * (dp_scr[:, cols] - row_dots) * scale).astype(jnp.bfloat16)
        dk_ref[cols, :] += lax.dot_general(grad_scores, q, tn, preferred_element_type=jnp.float32)
        dv_ref[cols, :] += lax.dot_general(weights, grad_out, tn, preferred_element_type=jnp.float32)
        return dq + jnp.dot(grad_scores, k_ref[cols, :], preferred_element_type=jnp.float32)

    dq_ref[0] = lax.fori_loop(0, chunks, grads_pass, jnp.zeros(q.shape, jnp.float32))


def attention_grads_fused(query_heads, keys, values, grad_heads, seen):
    rows, group, width = query_heads.shape
    key_count = keys.shape[0]
    q = jnp.transpose(query_heads, (1, 0, 2))
    g = jnp.transpose(grad_heads, (1, 0, 2))
    head_block = pl.BlockSpec((1, rows, width), lambda h: (h, 0, 0))
    whole_keys = pl.BlockSpec((key_count, width), lambda h: (0, 0))
    flops = 10 * group * rows * key_count * width
    dq, dk, dv = pl.pallas_call(
        attention_kernel,
        grid=(group,),
        in_specs=[
            pl.BlockSpec((rows, key_count), lambda h: (0, 0)),
            head_block,
            whole_keys,
            whole_keys,
            head_block,
        ],
        out_specs=[head_block, whole_keys, whole_keys],
        out_shape=[
            jax.ShapeDtypeStruct((group, rows, width), jnp.float32),
            jax.ShapeDtypeStruct((key_count, width), jnp.float32),
            jax.ShapeDtypeStruct((key_count, width), jnp.float32),
        ],
        scratch_shapes=[
            pltpu.VMEM((rows, key_count), jnp.float32),
            pltpu.VMEM((rows, key_count), jnp.float32),
        ],
        compiler_params=pltpu.CompilerParams(dimension_semantics=("arbitrary",)),
        cost_estimate=pl.CostEstimate(
            flops=flops,
            transcendentals=2 * group * rows * key_count,
            bytes_accessed=rows * key_count * 2 + 4 * key_count * width * 6,
        ),
    )(seen.astype(jnp.bfloat16), q, keys, values, g)
    return jnp.transpose(dq, (1, 0, 2)), dk, dv


def gather_rows(block):
    chips = lax.axis_size("seq_x") * lax.axis_size("seq_z")
    copies = jnp.broadcast_to(block[None], (chips,) + block.shape)
    mine = lax.all_to_all(copies, ("seq_x", "seq_z"), 0, 0, tiled=True)
    other = lax.ppermute(mine, "seq_core", PAIR)
    joined = jnp.stack([mine, other], axis=0)
    return joined.reshape((2 * chips * block.shape[0],) + block.shape[1:])


def pair_sum(keep, send):
    got = lax.ppermute(send.astype(jnp.bfloat16), "seq_core", PAIR)
    return (keep.astype(jnp.float32) + got.astype(jnp.float32)).astype(jnp.bfloat16)


def scatter_sum(parts, axis):
    arrived = lax.all_to_all(parts, axis, 0, 0, tiled=True)
    return jnp.sum(arrived.astype(jnp.float32), axis=0)


def body(normed, w_query, w_key, w_value, positions, block_mask, grad_attn):
    tok_rows = normed.shape[0]
    group_size = w_query.shape[1] // w_key.shape[1]
    width_query = group_size * HEAD
    blk_local = tok_rows // BLOCK
    chips = lax.axis_size("seq_x") * lax.axis_size("seq_z")
    kvh_count = lax.axis_size("kvh_x") * lax.axis_size("kvh_y")
    core = lax.axis_index("seq_core")
    my_index = seq_position()
    queries = rotate(
        jnp.dot(normed, w_query, preferred_element_type=jnp.float32), positions, 1.0
    ).astype(jnp.bfloat16)
    keys = rotate(
        jnp.dot(normed, w_key, preferred_element_type=jnp.float32), positions, 1.0
    ).astype(jnp.bfloat16)
    values = jnp.dot(normed, w_value, preferred_element_type=jnp.float32).astype(jnp.bfloat16)
    kv_all = gather_rows(jnp.concatenate([keys, values], axis=1))
    keys_all = kv_all[:, :HEAD]
    values_all = kv_all[:, HEAD:]
    key_count = keys_all.shape[0]
    chunk = jnp.arange(key_count // BLOCK)
    per_shard = tok_rows // BLOCK
    side = chunk // (chips * per_shard)
    chip = (chunk // per_shard) % chips
    chunk_blocks = (chip * 2 + jnp.where(side == 0, core, 1 - core)) * per_shard + chunk % per_shard
    seen = visible(block_mask, my_index * blk_local, tok_rows, chunk_blocks, jnp.arange(key_count) % BLOCK)
    query_heads = queries.reshape(tok_rows, group_size, HEAD)
    grad_heads = grad_attn.reshape(tok_rows, group_size, HEAD)
    grad_query, grad_key, grad_value = attention_grads_fused(
        query_heads, keys_all, values_all, grad_heads, seen
    )
    query_grad = rotate(grad_query.reshape(tok_rows, width_query), positions, -1.0).astype(
        jnp.bfloat16
    )
    kv_terms = jnp.concatenate([grad_key, grad_value], axis=1).reshape(2, chips, tok_rows, 2 * HEAD)
    feat_split = normed.reshape(tok_rows, chips, 2, normed.shape[1] // (2 * chips))
    normed_even = feat_split[:, :, 0, :]
    normed_odd = feat_split[:, :, 1, :]
    tokens_first = (((0,), (0,)), ((), ()))
    first = core == 0

    def weight_halves(grads):
        even = lax.dot_general(normed_even, grads, tokens_first, preferred_element_type=jnp.float32)
        odd = lax.dot_general(normed_odd, grads, tokens_first, preferred_element_type=jnp.float32)
        return jnp.where(first, even, odd), jnp.where(first, odd, even)

    wq_keep, wq_send = weight_halves(query_grad)
    joint = pair_sum(
        jnp.concatenate([kv_terms[0], wq_keep], axis=2), jnp.concatenate([kv_terms[1], wq_send], axis=2)
    )
    joint_total = scatter_sum(joint, ("seq_x", "seq_z"))
    kv_total = joint_total[:, : 2 * HEAD]
    grad_wq = joint_total[:, 2 * HEAD :]

    def weight_terms(grads):
        keep, send = weight_halves(grads)
        return scatter_sum(pair_sum(keep, send), ("seq_x", "seq_z"))

    contract = (((1,), (1,)), ((), ()))
    partial_input = lax.dot_general(
        w_query, query_grad, contract, preferred_element_type=jnp.float32
    )
    key_grad = rotate(kv_total[:, :HEAD], positions, -1.0).astype(jnp.bfloat16)
    value_grad = kv_total[:, HEAD:].astype(jnp.bfloat16)
    kv_grad = jnp.concatenate([key_grad, value_grad], axis=1)
    grad_wkv = weight_terms(kv_grad)
    grad_wk = grad_wkv[:, :HEAD]
    grad_wv = grad_wkv[:, HEAD:]
    partial_input = partial_input + lax.dot_general(
        w_key, key_grad, contract, preferred_element_type=jnp.float32
    )
    partial_input = partial_input + lax.dot_general(
        w_value, value_grad, contract, preferred_element_type=jnp.float32
    )
    feat = partial_input.shape[0] // kvh_count
    input_terms = partial_input.astype(jnp.bfloat16).reshape(kvh_count, feat, tok_rows)
    grad_normed = scatter_sum(input_terms, KVH_AXES).T.astype(jnp.bfloat16)
    return (grad_normed, grad_wq, grad_wk, grad_wv)


def solution(mesh):
    seq_x = 2
    seq_size = mesh.shape["seq"]
    kvh_size = mesh.shape["kvh"]
    grid = mesh.devices.reshape(seq_x, seq_size // (2 * seq_x), 2, 2, kvh_size // 2)
    fine = jax.sharding.Mesh(grid, SEQ_AXES + KVH_AXES)
    in_specs = (
        P(SEQ_AXES, None),
        P(None, KVH_AXES),
        P(None, KVH_AXES),
        P(None, KVH_AXES),
        P(SEQ_AXES),
        P(SEQ_AXES, None),
        P(SEQ_AXES, KVH_AXES),
    )
    out_specs = (P(SEQ_AXES, KVH_AXES),) * 4
    return jax.shard_map(body, mesh=fine, in_specs=in_specs, out_specs=out_specs, check_vma=False)
```

```python
import jax
import jax.numpy as jnp
from jax import lax
from jax.sharding import PartitionSpec as P

HEAD = 128
BLOCK = 128


THETA = 500000.0


def rotate(values, positions, rotation_sign):
    tok_rows = values.shape[0]
    head_count = values.shape[1] // HEAD
    half_size = HEAD // 2
    pieces = values.reshape(tok_rows, head_count, HEAD)
    frequency = THETA ** (-(jnp.arange(half_size, dtype=jnp.float32) * (2.0 / HEAD)))
    angles = positions.astype(jnp.float32)[:, None] * frequency[None, :]
    cosine = jnp.cos(angles)[:, None, :]
    sine_part = rotation_sign * jnp.sin(angles)[:, None, :]
    lower_half = pieces[:, :, :half_size]
    upper_half = pieces[:, :, half_size:]
    turned = jnp.concatenate(
        [
            lower_half * cosine - upper_half * sine_part,
            upper_half * cosine + lower_half * sine_part,
        ],
        axis=2,
    )
    return turned.reshape(tok_rows, head_count * HEAD)


def visible(mask_rows, query_block0, query_count, chunk_blocks, key_inner):
    query_local = jnp.arange(query_count)
    query_block = query_block0 + query_local // BLOCK
    table = jnp.take(mask_rows, chunk_blocks, axis=1) == 1
    key_blocks = jnp.repeat(chunk_blocks, BLOCK)
    allowed = jnp.repeat(jnp.repeat(table, BLOCK, axis=0), BLOCK, axis=1)
    inner_ok = key_inner[None, :] <= (query_local % BLOCK)[:, None]
    return allowed & ((query_block[:, None] != key_blocks[None, :]) | inner_ok)


def product(form, left, right):
    return jnp.einsum(form, left, right, preferred_element_type=jnp.float32)


def masked_scores(queries, keys, seen):
    scores = product("tgd,sd->gts", queries, keys) * HEAD ** (-0.5)
    return jnp.where(seen[None], scores, -1e30)


def attention_grads(queries, keys, values, grad_heads, seen):
    scores = masked_scores(queries, keys, seen)
    row_max = jnp.max(scores, axis=2, keepdims=True)
    log_total = row_max + jnp.log(jnp.sum(jnp.exp(scores - row_max), axis=2, keepdims=True))
    probs = jnp.where(seen[None], jnp.exp(scores - log_total), 0.0)
    weights = probs.astype(jnp.bfloat16)
    grad_probs = product("tgd,sd->gts", grad_heads, values)
    row_dots = jnp.sum(weights.astype(jnp.float32) * grad_probs, axis=2, keepdims=True)
    grad_scores = (probs * (grad_probs - row_dots) * HEAD ** (-0.5)).astype(jnp.bfloat16)
    grad_query = product("gts,sd->tgd", grad_scores, keys)
    grad_key = product("gts,tgd->sd", grad_scores, queries)
    grad_value = product("gts,tgd->sd", weights, grad_heads)
    return (grad_query, grad_key, grad_value)


SEQ_AXES = ("seq_x", "seq_z", "seq_core")
KVH_AXES = ("kvh_x", "kvh_y")
PAIR = [(0, 1), (1, 0)]


def seq_position():
    return (lax.axis_index("seq_x") * lax.axis_size("seq_z") + lax.axis_index("seq_z")) * 2 + lax.axis_index(
        "seq_core"
    )


def gather_rows(block):
    chips = lax.axis_size("seq_x") * lax.axis_size("seq_z")
    copies = jnp.broadcast_to(block[None], (chips,) + block.shape)
    mine = lax.all_to_all(copies, ("seq_x", "seq_z"), 0, 0, tiled=True)
    other = lax.ppermute(mine, "seq_core", PAIR)
    joined = jnp.stack([mine, other], axis=0)
    return joined.reshape((2 * chips * block.shape[0],) + block.shape[1:])


def pair_sum(keep, send):
    got = lax.ppermute(send.astype(jnp.bfloat16), "seq_core", PAIR)
    return (keep.astype(jnp.float32) + got.astype(jnp.float32)).astype(jnp.bfloat16)


def scatter_sum(parts, axis):
    arrived = lax.all_to_all(parts, axis, 0, 0, tiled=True)
    return jnp.sum(arrived.astype(jnp.float32), axis=0)


def body(normed, w_query, w_key, w_value, positions, block_mask, grad_attn):
    tok_rows = normed.shape[0]
    group_size = w_query.shape[1] // w_key.shape[1]
    width_query = group_size * HEAD
    blk_local = tok_rows // BLOCK
    chips = lax.axis_size("seq_x") * lax.axis_size("seq_z")
    kvh_count = lax.axis_size("kvh_x") * lax.axis_size("kvh_y")
    core = lax.axis_index("seq_core")
    my_index = seq_position()
    queries = rotate(
        jnp.dot(normed, w_query, preferred_element_type=jnp.float32), positions, 1.0
    ).astype(jnp.bfloat16)
    keys = rotate(
        jnp.dot(normed, w_key, preferred_element_type=jnp.float32), positions, 1.0
    ).astype(jnp.bfloat16)
    values = jnp.dot(normed, w_value, preferred_element_type=jnp.float32).astype(jnp.bfloat16)
    kv_all = gather_rows(jnp.concatenate([keys, values], axis=1))
    keys_all = kv_all[:, :HEAD]
    values_all = kv_all[:, HEAD:]
    key_count = keys_all.shape[0]
    chunk = jnp.arange(key_count // BLOCK)
    per_shard = tok_rows // BLOCK
    side = chunk // (chips * per_shard)
    chip = (chunk // per_shard) % chips
    chunk_blocks = (chip * 2 + jnp.where(side == 0, core, 1 - core)) * per_shard + chunk % per_shard
    seen = visible(block_mask, my_index * blk_local, tok_rows, chunk_blocks, jnp.arange(key_count) % BLOCK)
    query_heads = queries.reshape(tok_rows, group_size, HEAD)
    grad_heads = grad_attn.reshape(tok_rows, group_size, HEAD)
    grad_query, grad_key, grad_value = attention_grads(
        query_heads, keys_all, values_all, grad_heads, seen
    )
    query_grad = rotate(grad_query.reshape(tok_rows, width_query), positions, -1.0).astype(
        jnp.bfloat16
    )
    kv_terms = jnp.concatenate([grad_key, grad_value], axis=1).reshape(2, chips, tok_rows, 2 * HEAD)
    feat_split = normed.reshape(tok_rows, chips, 2, normed.shape[1] // (2 * chips))
    normed_even = feat_split[:, :, 0, :]
    normed_odd = feat_split[:, :, 1, :]
    tokens_first = (((0,), (0,)), ((), ()))
    first = core == 0

    def weight_halves(grads):
        even = lax.dot_general(normed_even, grads, tokens_first, preferred_element_type=jnp.float32)
        odd = lax.dot_general(normed_odd, grads, tokens_first, preferred_element_type=jnp.float32)
        return jnp.where(first, even, odd), jnp.where(first, odd, even)

    kv_total = scatter_sum(pair_sum(kv_terms[0], kv_terms[1]), ("seq_x", "seq_z"))
    wq_keep, wq_send = weight_halves(query_grad)
    grad_wq = scatter_sum(pair_sum(wq_keep, wq_send), ("seq_x", "seq_z"))

    def weight_terms(grads):
        keep, send = weight_halves(grads)
        return scatter_sum(pair_sum(keep, send), ("seq_x", "seq_z"))

    contract = (((1,), (1,)), ((), ()))
    partial_input = lax.dot_general(
        w_query, query_grad, contract, preferred_element_type=jnp.float32
    )
    key_grad = rotate(kv_total[:, :HEAD], positions, -1.0).astype(jnp.bfloat16)
    value_grad = kv_total[:, HEAD:].astype(jnp.bfloat16)
    kv_grad = jnp.concatenate([key_grad, value_grad], axis=1)
    grad_wkv = weight_terms(kv_grad)
    grad_wk = grad_wkv[:, :HEAD]
    grad_wv = grad_wkv[:, HEAD:]
    partial_input = partial_input + lax.dot_general(
        w_key, key_grad, contract, preferred_element_type=jnp.float32
    )
    partial_input = partial_input + lax.dot_general(
        w_value, value_grad, contract, preferred_element_type=jnp.float32
    )
    feat = partial_input.shape[0] // kvh_count
    input_terms = partial_input.astype(jnp.bfloat16).reshape(kvh_count, feat, tok_rows)
    grad_normed = scatter_sum(input_terms, KVH_AXES).T.astype(jnp.bfloat16)
    return (grad_normed, grad_wq, grad_wk, grad_wv)


def solution(mesh):
    seq_x = 2
    seq_size = mesh.shape["seq"]
    kvh_size = mesh.shape["kvh"]
    grid = mesh.devices.reshape(seq_x, seq_size // (2 * seq_x), 2, 2, kvh_size // 2)
    fine = jax.sharding.Mesh(grid, SEQ_AXES + KVH_AXES)
    in_specs = (
        P(SEQ_AXES, None),
        P(None, KVH_AXES),
        P(None, KVH_AXES),
        P(None, KVH_AXES),
        P(SEQ_AXES),
        P(SEQ_AXES, None),
        P(SEQ_AXES, KVH_AXES),
    )
    out_specs = (P(SEQ_AXES, KVH_AXES),) * 4
    return jax.shard_map(body, mesh=fine, in_specs=in_specs, out_specs=out_specs, check_vma=False)
```

```python
import jax
import jax.numpy as jnp
from jax import lax
from jax.sharding import PartitionSpec as P

HEAD = 128
BLOCK = 128


THETA = 500000.0


def rotate(values, positions, rotation_sign):
    tok_rows = values.shape[0]
    head_count = values.shape[1] // HEAD
    half_size = HEAD // 2
    pieces = values.reshape(tok_rows, head_count, HEAD)
    frequency = THETA ** (-(jnp.arange(half_size, dtype=jnp.float32) * (2.0 / HEAD)))
    angles = positions.astype(jnp.float32)[:, None] * frequency[None, :]
    cosine = jnp.cos(angles)[:, None, :]
    sine_part = rotation_sign * jnp.sin(angles)[:, None, :]
    lower_half = pieces[:, :, :half_size]
    upper_half = pieces[:, :, half_size:]
    turned = jnp.concatenate(
        [
            lower_half * cosine - upper_half * sine_part,
            upper_half * cosine + lower_half * sine_part,
        ],
        axis=2,
    )
    return turned.reshape(tok_rows, head_count * HEAD)


def visible(mask_rows, query_block0, query_count, chunk_blocks, key_inner):
    query_local = jnp.arange(query_count)
    query_block = query_block0 + query_local // BLOCK
    table = jnp.take(mask_rows, chunk_blocks, axis=1) == 1
    key_blocks = jnp.repeat(chunk_blocks, BLOCK)
    allowed = jnp.repeat(jnp.repeat(table, BLOCK, axis=0), BLOCK, axis=1)
    inner_ok = key_inner[None, :] <= (query_local % BLOCK)[:, None]
    return allowed & ((query_block[:, None] != key_blocks[None, :]) | inner_ok)


def product(form, left, right):
    return jnp.einsum(form, left, right, preferred_element_type=jnp.float32)


def masked_scores(queries, keys, seen):
    scores = product("tgd,sd->gts", queries, keys) * HEAD ** (-0.5)
    return jnp.where(seen[None], scores, -1e30)


def softmax_stats(queries, keys, values, grad_heads, seen):
    scores = masked_scores(queries, keys, seen)
    row_max = jnp.max(scores, axis=2, keepdims=True)
    log_total = row_max[:, :, 0] + jnp.log(jnp.sum(jnp.exp(scores - row_max), axis=2))
    weights = jnp.where(seen[None], jnp.exp(scores - log_total[:, :, None]), 0.0).astype(
        jnp.bfloat16
    )
    outputs = product("gts,sd->gtd", weights, values)
    row_dots = jnp.sum(outputs * jnp.transpose(grad_heads.astype(jnp.float32), (1, 0, 2)), axis=2)
    return (log_total, row_dots)


def attention_grads(queries, keys, values, grad_heads, seen, log_total, row_dots):
    scores = masked_scores(queries, keys, seen)
    probs = jnp.where(seen[None], jnp.exp(scores - log_total[:, :, None]), 0.0)
    weights = probs.astype(jnp.bfloat16)
    grad_probs = product("tgd,sd->gts", grad_heads, values)
    grad_scores = (probs * (grad_probs - row_dots[:, :, None]) * HEAD ** (-0.5)).astype(
        jnp.bfloat16
    )
    grad_query = product("gts,sd->tgd", grad_scores, keys)
    grad_key = product("gts,tgd->sd", grad_scores, queries)
    grad_value = product("gts,tgd->sd", weights, grad_heads)
    return (grad_query, grad_key, grad_value)


SEQ_AXES = ("seq_x", "seq_z", "seq_core")
KVH_AXES = ("kvh_x", "kvh_y")
PAIR = [(0, 1), (1, 0)]


def seq_position():
    return (lax.axis_index("seq_x") * lax.axis_size("seq_z") + lax.axis_index("seq_z")) * 2 + lax.axis_index(
        "seq_core"
    )


def gather_rows(block):
    chips = lax.axis_size("seq_x") * lax.axis_size("seq_z")
    copies = jnp.broadcast_to(block[None], (chips,) + block.shape)
    mine = lax.all_to_all(copies, ("seq_x", "seq_z"), 0, 0, tiled=True)
    other = lax.ppermute(mine, "seq_core", PAIR)
    joined = jnp.stack([mine, other], axis=0)
    return joined.reshape((2 * chips * block.shape[0],) + block.shape[1:])


def pair_sum(keep, send):
    got = lax.ppermute(send.astype(jnp.bfloat16), "seq_core", PAIR)
    return (keep.astype(jnp.float32) + got.astype(jnp.float32)).astype(jnp.bfloat16)


def scatter_sum(parts, axis):
    arrived = lax.all_to_all(parts, axis, 0, 0, tiled=True)
    return jnp.sum(arrived.astype(jnp.float32), axis=0)


def body(normed, w_query, w_key, w_value, positions, block_mask, grad_attn):
    tok_rows = normed.shape[0]
    group_size = w_query.shape[1] // w_key.shape[1]
    width_query = group_size * HEAD
    blk_local = tok_rows // BLOCK
    chips = lax.axis_size("seq_x") * lax.axis_size("seq_z")
    kvh_count = lax.axis_size("kvh_x") * lax.axis_size("kvh_y")
    core = lax.axis_index("seq_core")
    my_index = seq_position()
    queries = rotate(
        jnp.dot(normed, w_query, preferred_element_type=jnp.float32), positions, 1.0
    ).astype(jnp.bfloat16)
    keys = rotate(
        jnp.dot(normed, w_key, preferred_element_type=jnp.float32), positions, 1.0
    ).astype(jnp.bfloat16)
    values = jnp.dot(normed, w_value, preferred_element_type=jnp.float32).astype(jnp.bfloat16)
    kv_all = gather_rows(jnp.concatenate([keys, values], axis=1))
    keys_all = kv_all[:, :HEAD]
    values_all = kv_all[:, HEAD:]
    key_count = keys_all.shape[0]
    chunk = jnp.arange(key_count // BLOCK)
    per_shard = tok_rows // BLOCK
    side = chunk // (chips * per_shard)
    chip = (chunk // per_shard) % chips
    chunk_blocks = (chip * 2 + jnp.where(side == 0, core, 1 - core)) * per_shard + chunk % per_shard
    seen = visible(block_mask, my_index * blk_local, tok_rows, chunk_blocks, jnp.arange(key_count) % BLOCK)
    query_heads = queries.reshape(tok_rows, group_size, HEAD)
    grad_heads = grad_attn.reshape(tok_rows, group_size, HEAD)
    feat_split = normed.reshape(tok_rows, chips, 2, normed.shape[1] // (2 * chips))
    normed_even = feat_split[:, :, 0, :]
    normed_odd = feat_split[:, :, 1, :]
    tokens_first = (((0,), (0,)), ((), ()))
    first = core == 0

    def weight_halves(grads):
        even = lax.dot_general(normed_even, grads, tokens_first, preferred_element_type=jnp.float32)
        odd = lax.dot_general(normed_odd, grads, tokens_first, preferred_element_type=jnp.float32)
        return jnp.where(first, even, odd), jnp.where(first, odd, even)

    def head_pair(q_part, g_part):
        log_total, row_dots = softmax_stats(q_part, keys_all, values_all, g_part, seen)
        g_query, g_key, g_value = attention_grads(
            q_part, keys_all, values_all, g_part, seen, log_total, row_dots
        )
        q_grad = rotate(g_query.reshape(tok_rows, -1), positions, -1.0).astype(jnp.bfloat16)
        return q_grad, g_key, g_value

    half = group_size // 2
    query_grad_a, key_a, value_a = head_pair(query_heads[:, :half], grad_heads[:, :half])
    wq_keep, wq_send = weight_halves(query_grad_a)
    wq_terms_a, q_part_b, g_part_b = lax.optimization_barrier(
        (pair_sum(wq_keep, wq_send), query_heads[:, half:], grad_heads[:, half:])
    )
    grad_wq_a = scatter_sum(wq_terms_a, ("seq_x", "seq_z"))
    query_grad_b, key_b, value_b = head_pair(q_part_b, g_part_b)
    grad_wq_a, query_grad_b, key_b, value_b = lax.optimization_barrier(
        (grad_wq_a, query_grad_b, key_b, value_b)
    )
    query_grad = jnp.concatenate([query_grad_a, query_grad_b], axis=1)
    kv_terms = jnp.concatenate([key_a + key_b, value_a + value_b], axis=1).reshape(
        2, chips, tok_rows, 2 * HEAD
    )
    wq_keep, wq_send = weight_halves(query_grad_b)
    joint = pair_sum(
        jnp.concatenate([kv_terms[0], wq_keep], axis=2), jnp.concatenate([kv_terms[1], wq_send], axis=2)
    )
    joint_total = scatter_sum(joint, ("seq_x", "seq_z"))
    kv_total = joint_total[:, : 2 * HEAD]
    grad_wq = jnp.concatenate([grad_wq_a, joint_total[:, 2 * HEAD :]], axis=1)

    def weight_terms(grads):
        keep, send = weight_halves(grads)
        return scatter_sum(pair_sum(keep, send), ("seq_x", "seq_z"))

    contract = (((1,), (1,)), ((), ()))
    partial_input = lax.dot_general(
        w_query, query_grad, contract, preferred_element_type=jnp.float32
    )
    key_grad = rotate(kv_total[:, :HEAD], positions, -1.0).astype(jnp.bfloat16)
    value_grad = kv_total[:, HEAD:].astype(jnp.bfloat16)
    kv_grad = jnp.concatenate([key_grad, value_grad], axis=1)
    grad_wkv = weight_terms(kv_grad)
    grad_wk = grad_wkv[:, :HEAD]
    grad_wv = grad_wkv[:, HEAD:]
    partial_input = partial_input + lax.dot_general(
        w_key, key_grad, contract, preferred_element_type=jnp.float32
    )
    partial_input = partial_input + lax.dot_general(
        w_value, value_grad, contract, preferred_element_type=jnp.float32
    )
    feat = partial_input.shape[0] // kvh_count
    input_terms = partial_input.astype(jnp.bfloat16).reshape(kvh_count, feat, tok_rows)
    grad_normed = scatter_sum(input_terms, KVH_AXES).T.astype(jnp.bfloat16)
    return (grad_normed, grad_wq, grad_wk, grad_wv)


def solution(mesh):
    seq_x = 2
    seq_size = mesh.shape["seq"]
    kvh_size = mesh.shape["kvh"]
    grid = mesh.devices.reshape(seq_x, seq_size // (2 * seq_x), 2, 2, kvh_size // 2)
    fine = jax.sharding.Mesh(grid, SEQ_AXES + KVH_AXES)
    in_specs = (
        P(SEQ_AXES, None),
        P(None, KVH_AXES),
        P(None, KVH_AXES),
        P(None, KVH_AXES),
        P(SEQ_AXES),
        P(SEQ_AXES, None),
        P(SEQ_AXES, KVH_AXES),
    )
    out_specs = (P(SEQ_AXES, KVH_AXES),) * 4
    return jax.shard_map(body, mesh=fine, in_specs=in_specs, out_specs=out_specs, check_vma=False)
```

```python
import jax
import jax.numpy as jnp
from jax import lax
from jax.sharding import PartitionSpec as P

HEAD = 128
BLOCK = 128


THETA = 500000.0


def rotate(values, positions, rotation_sign):
    tok_rows = values.shape[0]
    head_count = values.shape[1] // HEAD
    half_size = HEAD // 2
    pieces = values.reshape(tok_rows, head_count, HEAD)
    frequency = THETA ** (-(jnp.arange(half_size, dtype=jnp.float32) * (2.0 / HEAD)))
    angles = positions.astype(jnp.float32)[:, None] * frequency[None, :]
    cosine = jnp.cos(angles)[:, None, :]
    sine_part = rotation_sign * jnp.sin(angles)[:, None, :]
    lower_half = pieces[:, :, :half_size]
    upper_half = pieces[:, :, half_size:]
    turned = jnp.concatenate(
        [
            lower_half * cosine - upper_half * sine_part,
            upper_half * cosine + lower_half * sine_part,
        ],
        axis=2,
    )
    return turned.reshape(tok_rows, head_count * HEAD)


def visible(mask_rows, query_block0, query_count, chunk_blocks, key_inner):
    query_local = jnp.arange(query_count)
    query_block = query_block0 + query_local // BLOCK
    table = jnp.take(mask_rows, chunk_blocks, axis=1) == 1
    key_blocks = jnp.repeat(chunk_blocks, BLOCK)
    allowed = jnp.repeat(jnp.repeat(table, BLOCK, axis=0), BLOCK, axis=1)
    inner_ok = key_inner[None, :] <= (query_local % BLOCK)[:, None]
    return allowed & ((query_block[:, None] != key_blocks[None, :]) | inner_ok)


def product(form, left, right):
    return jnp.einsum(form, left, right, preferred_element_type=jnp.float32)


def masked_scores(queries, keys, seen):
    scores = product("tgd,sd->gts", queries, keys) * HEAD ** (-0.5)
    return jnp.where(seen[None], scores, -1e30)


def softmax_stats(queries, keys, values, grad_heads, seen):
    scores = masked_scores(queries, keys, seen)
    row_max = jnp.max(scores, axis=2, keepdims=True)
    log_total = row_max[:, :, 0] + jnp.log(jnp.sum(jnp.exp(scores - row_max), axis=2))
    weights = jnp.where(seen[None], jnp.exp(scores - log_total[:, :, None]), 0.0).astype(
        jnp.bfloat16
    )
    outputs = product("gts,sd->gtd", weights, values)
    row_dots = jnp.sum(outputs * jnp.transpose(grad_heads.astype(jnp.float32), (1, 0, 2)), axis=2)
    return (log_total, row_dots)


def attention_grads(queries, keys, values, grad_heads, seen, log_total, row_dots):
    scores = masked_scores(queries, keys, seen)
    probs = jnp.where(seen[None], jnp.exp(scores - log_total[:, :, None]), 0.0)
    weights = probs.astype(jnp.bfloat16)
    grad_probs = product("tgd,sd->gts", grad_heads, values)
    grad_scores = (probs * (grad_probs - row_dots[:, :, None]) * HEAD ** (-0.5)).astype(
        jnp.bfloat16
    )
    grad_query = product("gts,sd->tgd", grad_scores, keys)
    grad_key = product("gts,tgd->sd", grad_scores, queries)
    grad_value = product("gts,tgd->sd", weights, grad_heads)
    return (grad_query, grad_key, grad_value)


SEQ_AXES = ("seq_x", "seq_z", "seq_core")
KVH_AXES = ("kvh_x", "kvh_y")
PAIR = [(0, 1), (1, 0)]


def seq_position():
    return (lax.axis_index("seq_x") * lax.axis_size("seq_z") + lax.axis_index("seq_z")) * 2 + lax.axis_index(
        "seq_core"
    )


def gather_rows(block):
    chips = lax.axis_size("seq_x") * lax.axis_size("seq_z")
    copies = jnp.broadcast_to(block[None], (chips,) + block.shape)
    mine = lax.all_to_all(copies, ("seq_x", "seq_z"), 0, 0, tiled=True)
    other = lax.ppermute(mine, "seq_core", PAIR)
    joined = jnp.stack([mine, other], axis=0)
    return joined.reshape((2 * chips * block.shape[0],) + block.shape[1:])


def pair_sum(keep, send):
    got = lax.ppermute(send.astype(jnp.bfloat16), "seq_core", PAIR)
    return (keep.astype(jnp.float32) + got.astype(jnp.float32)).astype(jnp.bfloat16)


def scatter_sum(parts, axis):
    arrived = lax.all_to_all(parts, axis, 0, 0, tiled=True)
    return jnp.sum(arrived.astype(jnp.float32), axis=0)


def scatter_sum_direct(parts, axes):
    count = parts.shape[0]
    me = lax.axis_index(axes)
    total = lax.dynamic_index_in_dim(parts, me, 0, keepdims=False).astype(jnp.float32)
    for step in range(1, count):
        piece = lax.dynamic_index_in_dim(parts, (me + step) % count, 0, keepdims=False)
        pairs = [(i, (i + step) % count) for i in range(count)]
        total = total + lax.ppermute(piece, axes, pairs).astype(jnp.float32)
    return total


def body(normed, w_query, w_key, w_value, positions, block_mask, grad_attn):
    tok_rows = normed.shape[0]
    group_size = w_query.shape[1] // w_key.shape[1]
    width_query = group_size * HEAD
    blk_local = tok_rows // BLOCK
    chips = lax.axis_size("seq_x") * lax.axis_size("seq_z")
    kvh_count = lax.axis_size("kvh_x") * lax.axis_size("kvh_y")
    core = lax.axis_index("seq_core")
    my_index = seq_position()
    queries = rotate(
        jnp.dot(normed, w_query, preferred_element_type=jnp.float32), positions, 1.0
    ).astype(jnp.bfloat16)
    keys = rotate(
        jnp.dot(normed, w_key, preferred_element_type=jnp.float32), positions, 1.0
    ).astype(jnp.bfloat16)
    values = jnp.dot(normed, w_value, preferred_element_type=jnp.float32).astype(jnp.bfloat16)
    kv_all = gather_rows(jnp.concatenate([keys, values], axis=1))
    keys_all = kv_all[:, :HEAD]
    values_all = kv_all[:, HEAD:]
    key_count = keys_all.shape[0]
    chunk = jnp.arange(key_count // BLOCK)
    per_shard = tok_rows // BLOCK
    side = chunk // (chips * per_shard)
    chip = (chunk // per_shard) % chips
    chunk_blocks = (chip * 2 + jnp.where(side == 0, core, 1 - core)) * per_shard + chunk % per_shard
    seen = visible(block_mask, my_index * blk_local, tok_rows, chunk_blocks, jnp.arange(key_count) % BLOCK)
    query_heads = queries.reshape(tok_rows, group_size, HEAD)
    grad_heads = grad_attn.reshape(tok_rows, group_size, HEAD)
    log_total, row_dots = softmax_stats(query_heads, keys_all, values_all, grad_heads, seen)
    grad_query, grad_key, grad_value = attention_grads(
        query_heads, keys_all, values_all, grad_heads, seen, log_total, row_dots
    )
    query_grad = rotate(grad_query.reshape(tok_rows, width_query), positions, -1.0).astype(
        jnp.bfloat16
    )
    kv_terms = jnp.concatenate([grad_key, grad_value], axis=1).reshape(2, chips, tok_rows, 2 * HEAD)
    feat_split = normed.reshape(tok_rows, chips, 2, normed.shape[1] // (2 * chips))
    normed_even = feat_split[:, :, 0, :]
    normed_odd = feat_split[:, :, 1, :]
    tokens_first = (((0,), (0,)), ((), ()))
    first = core == 0

    def weight_halves(grads):
        even = lax.dot_general(normed_even, grads, tokens_first, preferred_element_type=jnp.float32)
        odd = lax.dot_general(normed_odd, grads, tokens_first, preferred_element_type=jnp.float32)
        return jnp.where(first, even, odd), jnp.where(first, odd, even)

    wq_keep, wq_send = weight_halves(query_grad)
    joint = pair_sum(
        jnp.concatenate([kv_terms[0], wq_keep], axis=2), jnp.concatenate([kv_terms[1], wq_send], axis=2)
    )
    joint_total = scatter_sum(joint, ("seq_x", "seq_z"))
    kv_total = joint_total[:, : 2 * HEAD]
    grad_wq = joint_total[:, 2 * HEAD :]

    def weight_terms(grads):
        keep, send = weight_halves(grads)
        return scatter_sum_direct(pair_sum(keep, send), ("seq_x", "seq_z"))

    contract = (((1,), (1,)), ((), ()))
    partial_input = lax.dot_general(
        w_query, query_grad, contract, preferred_element_type=jnp.float32
    )
    key_grad = rotate(kv_total[:, :HEAD], positions, -1.0).astype(jnp.bfloat16)
    value_grad = kv_total[:, HEAD:].astype(jnp.bfloat16)
    kv_grad = jnp.concatenate([key_grad, value_grad], axis=1)
    grad_wkv = weight_terms(kv_grad)
    grad_wk = grad_wkv[:, :HEAD]
    grad_wv = grad_wkv[:, HEAD:]
    partial_input = partial_input + lax.dot_general(
        w_key, key_grad, contract, preferred_element_type=jnp.float32
    )
    partial_input = partial_input + lax.dot_general(
        w_value, value_grad, contract, preferred_element_type=jnp.float32
    )
    feat = partial_input.shape[0] // kvh_count
    input_terms = partial_input.astype(jnp.bfloat16).reshape(kvh_count, feat, tok_rows)
    grad_normed = scatter_sum(input_terms, KVH_AXES).T.astype(jnp.bfloat16)
    return (grad_normed, grad_wq, grad_wk, grad_wv)


def solution(mesh):
    seq_x = 2
    seq_size = mesh.shape["seq"]
    kvh_size = mesh.shape["kvh"]
    grid = mesh.devices.reshape(seq_x, seq_size // (2 * seq_x), 2, 2, kvh_size // 2)
    fine = jax.sharding.Mesh(grid, SEQ_AXES + KVH_AXES)
    in_specs = (
        P(SEQ_AXES, None),
        P(None, KVH_AXES),
        P(None, KVH_AXES),
        P(None, KVH_AXES),
        P(SEQ_AXES),
        P(SEQ_AXES, None),
        P(SEQ_AXES, KVH_AXES),
    )
    out_specs = (P(SEQ_AXES, KVH_AXES),) * 4
    return jax.shard_map(body, mesh=fine, in_specs=in_specs, out_specs=out_specs, check_vma=False)
```

```python
import jax
import jax.numpy as jnp
from jax import lax
from jax.sharding import PartitionSpec as P

HEAD = 128
BLOCK = 128


THETA = 500000.0


def rotate(values, positions, rotation_sign):
    tok_rows = values.shape[0]
    head_count = values.shape[1] // HEAD
    half_size = HEAD // 2
    pieces = values.reshape(tok_rows, head_count, HEAD)
    frequency = THETA ** (-(jnp.arange(half_size, dtype=jnp.float32) * (2.0 / HEAD)))
    angles = positions.astype(jnp.float32)[:, None] * frequency[None, :]
    cosine = jnp.cos(angles)[:, None, :]
    sine_part = rotation_sign * jnp.sin(angles)[:, None, :]
    lower_half = pieces[:, :, :half_size]
    upper_half = pieces[:, :, half_size:]
    turned = jnp.concatenate(
        [
            lower_half * cosine - upper_half * sine_part,
            upper_half * cosine + lower_half * sine_part,
        ],
        axis=2,
    )
    return turned.reshape(tok_rows, head_count * HEAD)


def visible(mask_rows, query_block0, query_count, chunk_blocks, key_inner):
    query_local = jnp.arange(query_count)
    query_block = query_block0 + query_local // BLOCK
    table = jnp.take(mask_rows, chunk_blocks, axis=1) == 1
    key_blocks = jnp.repeat(chunk_blocks, BLOCK)
    allowed = jnp.repeat(jnp.repeat(table, BLOCK, axis=0), BLOCK, axis=1)
    inner_ok = key_inner[None, :] <= (query_local % BLOCK)[:, None]
    return allowed & ((query_block[:, None] != key_blocks[None, :]) | inner_ok)


def product(form, left, right):
    return jnp.einsum(form, left, right, preferred_element_type=jnp.float32)


def masked_scores(queries, keys, seen):
    scores = product("tgd,sd->gts", queries, keys) * HEAD ** (-0.5)
    return jnp.where(seen[None], scores, -1e30)


def softmax_stats(queries, keys, values, grad_heads, seen):
    scores = masked_scores(queries, keys, seen)
    row_max = jnp.max(scores, axis=2, keepdims=True)
    log_total = row_max[:, :, 0] + jnp.log(jnp.sum(jnp.exp(scores - row_max), axis=2))
    weights = jnp.where(seen[None], jnp.exp(scores - log_total[:, :, None]), 0.0).astype(
        jnp.bfloat16
    )
    outputs = product("gts,sd->gtd", weights, values)
    row_dots = jnp.sum(outputs * jnp.transpose(grad_heads.astype(jnp.float32), (1, 0, 2)), axis=2)
    return (log_total, row_dots)


def attention_grads(queries, keys, values, grad_heads, seen, log_total, row_dots):
    scores = masked_scores(queries, keys, seen)
    probs = jnp.where(seen[None], jnp.exp(scores - log_total[:, :, None]), 0.0)
    weights = probs.astype(jnp.bfloat16)
    grad_probs = product("tgd,sd->gts", grad_heads, values)
    grad_scores = (probs * (grad_probs - row_dots[:, :, None]) * HEAD ** (-0.5)).astype(
        jnp.bfloat16
    )
    grad_query = product("gts,sd->tgd", grad_scores, keys)
    grad_key = product("gts,tgd->sd", grad_scores, queries)
    grad_value = product("gts,tgd->sd", weights, grad_heads)
    return (grad_query, grad_key, grad_value)


SEQ_AXES = ("seq_x", "seq_z", "seq_core")
KVH_AXES = ("kvh_x", "kvh_y")
PAIR = [(0, 1), (1, 0)]


def seq_position():
    return (lax.axis_index("seq_x") * lax.axis_size("seq_z") + lax.axis_index("seq_z")) * 2 + lax.axis_index(
        "seq_core"
    )


def gather_rows(block):
    chips = lax.axis_size("seq_x") * lax.axis_size("seq_z")
    copies = jnp.broadcast_to(block[None], (chips,) + block.shape)
    mine = lax.all_to_all(copies, ("seq_x", "seq_z"), 0, 0, tiled=True)
    other = lax.ppermute(mine, "seq_core", PAIR)
    joined = jnp.stack([mine, other], axis=0)
    return joined.reshape((2 * chips * block.shape[0],) + block.shape[1:])


def pair_sum(keep, send):
    got = lax.ppermute(send.astype(jnp.bfloat16), "seq_core", PAIR)
    return (keep.astype(jnp.float32) + got.astype(jnp.float32)).astype(jnp.bfloat16)


def scatter_sum(parts, axis):
    arrived = lax.all_to_all(parts, axis, 0, 0, tiled=True)
    return jnp.sum(arrived.astype(jnp.float32), axis=0)


def body(normed, w_query, w_key, w_value, positions, block_mask, grad_attn):
    tok_rows = normed.shape[0]
    group_size = w_query.shape[1] // w_key.shape[1]
    width_query = group_size * HEAD
    blk_local = tok_rows // BLOCK
    chips = lax.axis_size("seq_x") * lax.axis_size("seq_z")
    kvh_count = lax.axis_size("kvh_x") * lax.axis_size("kvh_y")
    core = lax.axis_index("seq_core")
    my_index = seq_position()
    queries = rotate(
        jnp.dot(normed, w_query, preferred_element_type=jnp.float32), positions, 1.0
    ).astype(jnp.bfloat16)
    keys = rotate(
        jnp.dot(normed, w_key, preferred_element_type=jnp.float32), positions, 1.0
    ).astype(jnp.bfloat16)
    values = jnp.dot(normed, w_value, preferred_element_type=jnp.float32).astype(jnp.bfloat16)
    kv_all = gather_rows(jnp.concatenate([keys, values], axis=1))
    keys_all = kv_all[:, :HEAD]
    values_all = kv_all[:, HEAD:]
    key_count = keys_all.shape[0]
    chunk = jnp.arange(key_count // BLOCK)
    per_shard = tok_rows // BLOCK
    side = chunk // (chips * per_shard)
    chip = (chunk // per_shard) % chips
    chunk_blocks = (chip * 2 + jnp.where(side == 0, core, 1 - core)) * per_shard + chunk % per_shard
    seen = visible(block_mask, my_index * blk_local, tok_rows, chunk_blocks, jnp.arange(key_count) % BLOCK)
    query_heads = queries.reshape(tok_rows, group_size, HEAD)
    grad_heads = grad_attn.reshape(tok_rows, group_size, HEAD)
    feat_split = normed.reshape(tok_rows, chips, 2, normed.shape[1] // (2 * chips))
    normed_even = feat_split[:, :, 0, :]
    normed_odd = feat_split[:, :, 1, :]
    tokens_first = (((0,), (0,)), ((), ()))
    first = core == 0

    def weight_halves(grads):
        even = lax.dot_general(normed_even, grads, tokens_first, preferred_element_type=jnp.float32)
        odd = lax.dot_general(normed_odd, grads, tokens_first, preferred_element_type=jnp.float32)
        return jnp.where(first, even, odd), jnp.where(first, odd, even)

    def head_pair(q_part, g_part):
        log_total, row_dots = softmax_stats(q_part, keys_all, values_all, g_part, seen)
        g_query, g_key, g_value = attention_grads(
            q_part, keys_all, values_all, g_part, seen, log_total, row_dots
        )
        q_grad = rotate(g_query.reshape(tok_rows, -1), positions, -1.0).astype(jnp.bfloat16)
        return lax.optimization_barrier(q_grad), g_key, g_value

    half = group_size // 2
    query_grad_a, key_a, value_a = head_pair(query_heads[:, :half], grad_heads[:, :half])
    wq_keep, wq_send = weight_halves(query_grad_a)
    wq_terms_a, q_part_b, g_part_b = lax.optimization_barrier(
        (pair_sum(wq_keep, wq_send), query_heads[:, half:], grad_heads[:, half:])
    )
    grad_wq_a = scatter_sum(wq_terms_a, ("seq_x", "seq_z"))
    query_grad_b, key_b, value_b = head_pair(q_part_b, g_part_b)
    grad_wq_a, query_grad_b, key_b, value_b = lax.optimization_barrier(
        (grad_wq_a, query_grad_b, key_b, value_b)
    )
    query_grad = jnp.concatenate([query_grad_a, query_grad_b], axis=1)
    kv_terms = jnp.concatenate([key_a + key_b, value_a + value_b], axis=1).reshape(
        2, chips, tok_rows, 2 * HEAD
    )
    wq_keep, wq_send = weight_halves(query_grad_b)
    joint = pair_sum(
        jnp.concatenate([kv_terms[0].astype(jnp.bfloat16), wq_keep.astype(jnp.bfloat16)], axis=2),
        jnp.concatenate([kv_terms[1].astype(jnp.bfloat16), wq_send.astype(jnp.bfloat16)], axis=2),
    )
    joint_total = scatter_sum(joint, ("seq_x", "seq_z"))
    kv_total = joint_total[:, : 2 * HEAD]
    grad_wq = jnp.concatenate([grad_wq_a, joint_total[:, 2 * HEAD :]], axis=1)

    def weight_terms(grads):
        keep, send = weight_halves(grads)
        return scatter_sum(pair_sum(keep, send), ("seq_x", "seq_z"))

    contract = (((1,), (1,)), ((), ()))
    partial_input = lax.dot_general(
        w_query, query_grad, contract, preferred_element_type=jnp.float32
    )
    key_grad = rotate(kv_total[:, :HEAD], positions, -1.0).astype(jnp.bfloat16)
    value_grad = kv_total[:, HEAD:].astype(jnp.bfloat16)
    kv_grad = jnp.concatenate([key_grad, value_grad], axis=1)
    grad_wkv = weight_terms(kv_grad)
    grad_wk = grad_wkv[:, :HEAD]
    grad_wv = grad_wkv[:, HEAD:]
    partial_input = partial_input + lax.dot_general(
        w_key, key_grad, contract, preferred_element_type=jnp.float32
    )
    partial_input = partial_input + lax.dot_general(
        w_value, value_grad, contract, preferred_element_type=jnp.float32
    )
    feat = partial_input.shape[0] // kvh_count
    input_terms = partial_input.astype(jnp.bfloat16).reshape(kvh_count, feat, tok_rows)
    grad_normed = scatter_sum(input_terms, KVH_AXES).T.astype(jnp.bfloat16)
    return (grad_normed, grad_wq, grad_wk, grad_wv)


def solution(mesh):
    seq_x = 2
    seq_size = mesh.shape["seq"]
    kvh_size = mesh.shape["kvh"]
    grid = mesh.devices.reshape(seq_x, seq_size // (2 * seq_x), 2, 2, kvh_size // 2)
    fine = jax.sharding.Mesh(grid, SEQ_AXES + KVH_AXES)
    in_specs = (
        P(SEQ_AXES, None),
        P(None, KVH_AXES),
        P(None, KVH_AXES),
        P(None, KVH_AXES),
        P(SEQ_AXES),
        P(SEQ_AXES, None),
        P(SEQ_AXES, KVH_AXES),
    )
    out_specs = (P(SEQ_AXES, KVH_AXES),) * 4
    return jax.shard_map(body, mesh=fine, in_specs=in_specs, out_specs=out_specs, check_vma=False)
```

```python
import jax
import jax.numpy as jnp
from jax import lax
from jax.sharding import PartitionSpec as P

HEAD = 128
BLOCK = 128


THETA = 500000.0


def rotate(values, positions, rotation_sign):
    tok_rows = values.shape[0]
    head_count = values.shape[1] // HEAD
    half_size = HEAD // 2
    pieces = values.reshape(tok_rows, head_count, HEAD)
    frequency = THETA ** (-(jnp.arange(half_size, dtype=jnp.float32) * (2.0 / HEAD)))
    angles = positions.astype(jnp.float32)[:, None] * frequency[None, :]
    cosine = jnp.cos(angles)[:, None, :]
    sine_part = rotation_sign * jnp.sin(angles)[:, None, :]
    lower_half = pieces[:, :, :half_size]
    upper_half = pieces[:, :, half_size:]
    turned = jnp.concatenate(
        [
            lower_half * cosine - upper_half * sine_part,
            upper_half * cosine + lower_half * sine_part,
        ],
        axis=2,
    )
    return turned.reshape(tok_rows, head_count * HEAD)


def visible(mask_rows, query_block0, query_count, chunk_blocks, key_inner):
    query_local = jnp.arange(query_count)
    query_block = query_block0 + query_local // BLOCK
    table = jnp.take(mask_rows, chunk_blocks, axis=1) == 1
    key_blocks = jnp.repeat(chunk_blocks, BLOCK)
    allowed = jnp.repeat(jnp.repeat(table, BLOCK, axis=0), BLOCK, axis=1)
    inner_ok = key_inner[None, :] <= (query_local % BLOCK)[:, None]
    return allowed & ((query_block[:, None] != key_blocks[None, :]) | inner_ok)


def product(form, left, right):
    return jnp.einsum(form, left, right, preferred_element_type=jnp.float32)


def masked_scores(queries, keys, seen):
    scores = product("tgd,sd->gts", queries, keys) * HEAD ** (-0.5)
    return jnp.where(seen[None], scores, -1e30)


def softmax_stats(queries, keys, values, grad_heads, seen):
    scores = masked_scores(queries, keys, seen)
    row_max = jnp.max(scores, axis=2, keepdims=True)
    log_total = row_max[:, :, 0] + jnp.log(jnp.sum(jnp.exp(scores - row_max), axis=2))
    weights = jnp.where(seen[None], jnp.exp(scores - log_total[:, :, None]), 0.0).astype(
        jnp.bfloat16
    )
    outputs = product("gts,sd->gtd", weights, values)
    row_dots = jnp.sum(outputs * jnp.transpose(grad_heads.astype(jnp.float32), (1, 0, 2)), axis=2)
    return (log_total, row_dots)


def attention_grads(queries, keys, values, grad_heads, seen, log_total, row_dots):
    scores = masked_scores(queries, keys, seen)
    probs = jnp.where(seen[None], jnp.exp(scores - log_total[:, :, None]), 0.0)
    weights = probs.astype(jnp.bfloat16)
    grad_probs = product("tgd,sd->gts", grad_heads, values)
    grad_scores = (probs * (grad_probs - row_dots[:, :, None]) * HEAD ** (-0.5)).astype(
        jnp.bfloat16
    )
    grad_query = product("gts,sd->tgd", grad_scores, keys)
    grad_key = product("gts,tgd->sd", grad_scores, queries)
    grad_value = product("gts,tgd->sd", weights, grad_heads)
    return (grad_query, grad_key, grad_value)


SEQ_AXES = ("seq_x", "seq_z", "seq_core")
KVH_AXES = ("kvh_x", "kvh_y")
PAIR = [(0, 1), (1, 0)]


def seq_position():
    return (lax.axis_index("seq_x") * lax.axis_size("seq_z") + lax.axis_index("seq_z")) * 2 + lax.axis_index(
        "seq_core"
    )


def gather_rows(block):
    chips = lax.axis_size("seq_x") * lax.axis_size("seq_z")
    copies = jnp.broadcast_to(block[None], (chips,) + block.shape)
    mine = lax.all_to_all(copies, ("seq_x", "seq_z"), 0, 0, tiled=True)
    other = lax.ppermute(mine, "seq_core", PAIR)
    joined = jnp.stack([mine, other], axis=0)
    return joined.reshape((2 * chips * block.shape[0],) + block.shape[1:])


def pair_sum(keep, send):
    got = lax.ppermute(send.astype(jnp.bfloat16), "seq_core", PAIR)
    return (keep.astype(jnp.float32) + got.astype(jnp.float32)).astype(jnp.bfloat16)


def scatter_sum(parts, axis):
    arrived = lax.all_to_all(parts, axis, 0, 0, tiled=True)
    return jnp.sum(arrived.astype(jnp.float32), axis=0)


def body(normed, w_query, w_key, w_value, positions, block_mask, grad_attn):
    tok_rows = normed.shape[0]
    group_size = w_query.shape[1] // w_key.shape[1]
    width_query = group_size * HEAD
    blk_local = tok_rows // BLOCK
    chips = lax.axis_size("seq_x") * lax.axis_size("seq_z")
    kvh_count = lax.axis_size("kvh_x") * lax.axis_size("kvh_y")
    core = lax.axis_index("seq_core")
    my_index = seq_position()
    queries = rotate(
        jnp.dot(normed, w_query, preferred_element_type=jnp.float32), positions, 1.0
    ).astype(jnp.bfloat16)
    keys = rotate(
        jnp.dot(normed, w_key, preferred_element_type=jnp.float32), positions, 1.0
    ).astype(jnp.bfloat16)
    values = jnp.dot(normed, w_value, preferred_element_type=jnp.float32).astype(jnp.bfloat16)
    kv_all = gather_rows(jnp.concatenate([keys, values], axis=1))
    rounds = chips // 2
    chip_me = lax.axis_index("seq_x") * lax.axis_size("seq_z") + lax.axis_index("seq_z")
    round_me = chip_me // 2
    kv_grid = kv_all.reshape(2, rounds, 2, tok_rows, 2 * HEAD)
    own_kv = lax.dynamic_index_in_dim(
        lax.dynamic_index_in_dim(kv_grid[0], round_me, 0, keepdims=False), chip_me % 2, 0, keepdims=False
    )
    later = jnp.roll(kv_grid, -(round_me + 1), axis=1)[:, : rounds - 1]
    kv_sel = jnp.concatenate([own_kv[None], later.reshape(-1, tok_rows, 2 * HEAD)], axis=0)
    kv_sel = kv_sel.reshape(-1, 2 * HEAD)
    keys_all = kv_sel[:, :HEAD]
    values_all = kv_sel[:, HEAD:]
    key_count = keys_all.shape[0]
    per_shard = tok_rows // BLOCK
    chunk = jnp.arange(key_count // BLOCK - per_shard)
    shard = chunk // per_shard
    side = shard // (2 * (rounds - 1))
    chip = ((round_me + 1 + (shard // 2) % (rounds - 1)) % rounds) * 2 + shard % 2
    source = chip * 2 + jnp.where(side == 0, core, 1 - core)
    chunk_blocks = jnp.concatenate(
        [my_index * per_shard + jnp.arange(per_shard), source * per_shard + chunk % per_shard]
    )
    seen = visible(block_mask, my_index * blk_local, tok_rows, chunk_blocks, jnp.arange(key_count) % BLOCK)
    query_heads = queries.reshape(tok_rows, group_size, HEAD)
    grad_heads = grad_attn.reshape(tok_rows, group_size, HEAD)
    log_total, row_dots = softmax_stats(query_heads, keys_all, values_all, grad_heads, seen)
    grad_query, grad_key, grad_value = attention_grads(
        query_heads, keys_all, values_all, grad_heads, seen, log_total, row_dots
    )
    query_grad = rotate(grad_query.reshape(tok_rows, width_query), positions, -1.0).astype(
        jnp.bfloat16
    )
    kv_sel_terms = jnp.concatenate([grad_key, grad_value], axis=1).reshape(-1, tok_rows, 2 * HEAD)
    later_terms = kv_sel_terms[1:].reshape(2, rounds - 1, 2, tok_rows, 2 * HEAD)
    place = (jnp.arange(2)[:, None] == 0) & (jnp.arange(2)[None, :] == chip_me % 2)
    own_round = jnp.where(place[:, :, None, None], kv_sel_terms[0][None, None], 0.0)
    kv_grid_terms = jnp.concatenate([later_terms, own_round[:, None]], axis=1)
    kv_grid_terms = jnp.roll(kv_grid_terms, round_me + 1, axis=1)
    kv_terms = kv_grid_terms.reshape(2, chips, tok_rows, 2 * HEAD)
    feat_split = normed.reshape(tok_rows, chips, 2, normed.shape[1] // (2 * chips))
    normed_even = feat_split[:, :, 0, :]
    normed_odd = feat_split[:, :, 1, :]
    tokens_first = (((0,), (0,)), ((), ()))
    first = core == 0

    def weight_halves(grads):
        even = lax.dot_general(normed_even, grads, tokens_first, preferred_element_type=jnp.float32)
        odd = lax.dot_general(normed_odd, grads, tokens_first, preferred_element_type=jnp.float32)
        return jnp.where(first, even, odd), jnp.where(first, odd, even)

    wq_keep, wq_send = weight_halves(query_grad)
    joint = pair_sum(
        jnp.concatenate([kv_terms[0], wq_keep], axis=2), jnp.concatenate([kv_terms[1], wq_send], axis=2)
    )
    joint_total = scatter_sum(joint, ("seq_x", "seq_z"))
    kv_total = joint_total[:, : 2 * HEAD]
    grad_wq = joint_total[:, 2 * HEAD :]

    def weight_terms(grads):
        keep, send = weight_halves(grads)
        return scatter_sum(pair_sum(keep, send), ("seq_x", "seq_z"))

    contract = (((1,), (1,)), ((), ()))
    partial_input = lax.dot_general(
        w_query, query_grad, contract, preferred_element_type=jnp.float32
    )
    key_grad = rotate(kv_total[:, :HEAD], positions, -1.0).astype(jnp.bfloat16)
    value_grad = kv_total[:, HEAD:].astype(jnp.bfloat16)
    kv_grad = jnp.concatenate([key_grad, value_grad], axis=1)
    grad_wkv = weight_terms(kv_grad)
    grad_wk = grad_wkv[:, :HEAD]
    grad_wv = grad_wkv[:, HEAD:]
    partial_input = partial_input + lax.dot_general(
        w_key, key_grad, contract, preferred_element_type=jnp.float32
    )
    partial_input = partial_input + lax.dot_general(
        w_value, value_grad, contract, preferred_element_type=jnp.float32
    )
    feat = partial_input.shape[0] // kvh_count
    input_terms = partial_input.astype(jnp.bfloat16).reshape(kvh_count, feat, tok_rows)
    grad_normed = scatter_sum(input_terms, KVH_AXES).T.astype(jnp.bfloat16)
    return (grad_normed, grad_wq, grad_wk, grad_wv)


def solution(mesh):
    seq_x = 2
    seq_size = mesh.shape["seq"]
    kvh_size = mesh.shape["kvh"]
    grid = mesh.devices.reshape(seq_x, seq_size // (2 * seq_x), 2, 2, kvh_size // 2)
    fine = jax.sharding.Mesh(grid, SEQ_AXES + KVH_AXES)
    in_specs = (
        P(SEQ_AXES, None),
        P(None, KVH_AXES),
        P(None, KVH_AXES),
        P(None, KVH_AXES),
        P(SEQ_AXES),
        P(SEQ_AXES, None),
        P(SEQ_AXES, KVH_AXES),
    )
    out_specs = (P(SEQ_AXES, KVH_AXES),) * 4
    return jax.shard_map(body, mesh=fine, in_specs=in_specs, out_specs=out_specs, check_vma=False)
```

```python
import jax
import jax.numpy as jnp
from jax import lax
from jax.sharding import PartitionSpec as P

HEAD = 128
BLOCK = 128


THETA = 500000.0


def rotate(values, positions, rotation_sign):
    tok_rows = values.shape[0]
    head_count = values.shape[1] // HEAD
    half_size = HEAD // 2
    pieces = values.reshape(tok_rows, head_count, HEAD)
    frequency = THETA ** (-(jnp.arange(half_size, dtype=jnp.float32) * (2.0 / HEAD)))
    angles = positions.astype(jnp.float32)[:, None] * frequency[None, :]
    cosine = jnp.cos(angles)[:, None, :]
    sine_part = rotation_sign * jnp.sin(angles)[:, None, :]
    lower_half = pieces[:, :, :half_size]
    upper_half = pieces[:, :, half_size:]
    turned = jnp.concatenate(
        [
            lower_half * cosine - upper_half * sine_part,
            upper_half * cosine + lower_half * sine_part,
        ],
        axis=2,
    )
    return turned.reshape(tok_rows, head_count * HEAD)


def visible(mask_rows, query_block0, query_count, chunk_blocks, key_inner):
    query_local = jnp.arange(query_count)
    query_block = query_block0 + query_local // BLOCK
    table = jnp.take(mask_rows, chunk_blocks, axis=1) == 1
    key_blocks = jnp.repeat(chunk_blocks, BLOCK)
    allowed = jnp.repeat(jnp.repeat(table, BLOCK, axis=0), BLOCK, axis=1)
    inner_ok = key_inner[None, :] <= (query_local % BLOCK)[:, None]
    return allowed & ((query_block[:, None] != key_blocks[None, :]) | inner_ok)


def product(form, left, right):
    return jnp.einsum(form, left, right, preferred_element_type=jnp.float32)


def masked_scores(queries, keys, seen):
    scores = product("tgd,sd->gts", queries, keys) * HEAD ** (-0.5)
    return jnp.where(seen[None], scores, -1e30)


def softmax_stats(queries, keys, values, grad_heads, seen):
    scores = masked_scores(queries, keys, seen)
    row_max = jnp.max(scores, axis=2, keepdims=True)
    log_total = row_max[:, :, 0] + jnp.log(jnp.sum(jnp.exp(scores - row_max), axis=2))
    weights = jnp.where(seen[None], jnp.exp(scores - log_total[:, :, None]), 0.0).astype(
        jnp.bfloat16
    )
    outputs = product("gts,sd->gtd", weights, values)
    row_dots = jnp.sum(outputs * jnp.transpose(grad_heads.astype(jnp.float32), (1, 0, 2)), axis=2)
    return (log_total, row_dots)


def attention_grads(queries, keys, values, grad_heads, seen, log_total, row_dots):
    scores = masked_scores(queries, keys, seen)
    probs = jnp.where(seen[None], jnp.exp(scores - log_total[:, :, None]), 0.0)
    weights = probs.astype(jnp.bfloat16)
    grad_probs = product("tgd,sd->gts", grad_heads, values)
    grad_scores = (probs * (grad_probs - row_dots[:, :, None]) * HEAD ** (-0.5)).astype(
        jnp.bfloat16
    )
    grad_query = product("gts,sd->tgd", grad_scores, keys)
    grad_key = product("gts,tgd->sd", grad_scores, queries)
    grad_value = product("gts,tgd->sd", weights, grad_heads)
    return (grad_query, grad_key, grad_value)


SEQ_AXES = ("seq_x", "seq_z", "seq_core")
KVH_AXES = ("kvh_x", "kvh_y")
PAIR = [(0, 1), (1, 0)]


def seq_position():
    return (lax.axis_index("seq_x") * lax.axis_size("seq_z") + lax.axis_index("seq_z")) * 2 + lax.axis_index(
        "seq_core"
    )


def gather_rows(block):
    chips = lax.axis_size("seq_x") * lax.axis_size("seq_z")
    copies = jnp.broadcast_to(block[None], (chips,) + block.shape)
    mine = lax.all_to_all(copies, ("seq_x", "seq_z"), 0, 0, tiled=True)
    other = lax.ppermute(mine, "seq_core", PAIR)
    joined = jnp.stack([mine, other], axis=0)
    return joined.reshape((2 * chips * block.shape[0],) + block.shape[1:])


def pair_sum(keep, send):
    got = lax.ppermute(send.astype(jnp.bfloat16), "seq_core", PAIR)
    return (keep.astype(jnp.float32) + got.astype(jnp.float32)).astype(jnp.bfloat16)


def scatter_sum(parts, axis):
    arrived = lax.all_to_all(parts, axis, 0, 0, tiled=True)
    return jnp.sum(arrived.astype(jnp.float32), axis=0)


def body(normed, w_query, w_key, w_value, positions, block_mask, grad_attn):
    tok_rows = normed.shape[0]
    group_size = w_query.shape[1] // w_key.shape[1]
    width_query = group_size * HEAD
    blk_local = tok_rows // BLOCK
    chips = lax.axis_size("seq_x") * lax.axis_size("seq_z")
    kvh_count = lax.axis_size("kvh_x") * lax.axis_size("kvh_y")
    core = lax.axis_index("seq_core")
    my_index = seq_position()
    queries = rotate(
        jnp.dot(normed, w_query, preferred_element_type=jnp.float32), positions, 1.0
    ).astype(jnp.bfloat16)
    keys = rotate(
        jnp.dot(normed, w_key, preferred_element_type=jnp.float32), positions, 1.0
    ).astype(jnp.bfloat16)
    values = jnp.dot(normed, w_value, preferred_element_type=jnp.float32).astype(jnp.bfloat16)
    kv_all = gather_rows(jnp.concatenate([keys, values], axis=1))
    rounds = chips // 2
    chip_me = lax.axis_index("seq_x") * lax.axis_size("seq_z") + lax.axis_index("seq_z")
    round_me = chip_me // 2
    shards = 2 * chips
    kept = 1 + 2 * 2 * (rounds - 1)
    pick = jnp.arange(kept - 1)
    pick_side = pick // (2 * (rounds - 1))
    pick_chip = ((round_me + 1 + (pick // 2) % (rounds - 1)) % rounds) * 2 + pick % 2
    slot = jnp.concatenate([chip_me[None], pick_side * chips + pick_chip])
    select = (jnp.arange(shards)[:, None] == slot[None, :]).astype(jnp.bfloat16)
    kv_sel = lax.dot_general(
        select, kv_all.reshape(shards, -1), (((0,), (0,)), ((), ())), preferred_element_type=jnp.bfloat16
    )
    kv_sel = kv_sel.reshape(-1, 2 * HEAD)
    keys_all = kv_sel[:, :HEAD]
    values_all = kv_sel[:, HEAD:]
    key_count = keys_all.shape[0]
    per_shard = tok_rows // BLOCK
    chunk = jnp.arange(key_count // BLOCK - per_shard)
    shard = chunk // per_shard
    side = shard // (2 * (rounds - 1))
    chip = ((round_me + 1 + (shard // 2) % (rounds - 1)) % rounds) * 2 + shard % 2
    source = chip * 2 + jnp.where(side == 0, core, 1 - core)
    chunk_blocks = jnp.concatenate(
        [my_index * per_shard + jnp.arange(per_shard), source * per_shard + chunk % per_shard]
    )
    seen = visible(block_mask, my_index * blk_local, tok_rows, chunk_blocks, jnp.arange(key_count) % BLOCK)
    query_heads = queries.reshape(tok_rows, group_size, HEAD)
    grad_heads = grad_attn.reshape(tok_rows, group_size, HEAD)
    log_total, row_dots = softmax_stats(query_heads, keys_all, values_all, grad_heads, seen)
    grad_query, grad_key, grad_value = attention_grads(
        query_heads, keys_all, values_all, grad_heads, seen, log_total, row_dots
    )
    query_grad = rotate(grad_query.reshape(tok_rows, width_query), positions, -1.0).astype(
        jnp.bfloat16
    )
    kv_sel_terms = jnp.concatenate([grad_key, grad_value], axis=1).astype(jnp.bfloat16)
    kv_grid_terms = jnp.dot(select, kv_sel_terms.reshape(kept, -1), preferred_element_type=jnp.bfloat16)
    kv_terms = kv_grid_terms.reshape(2, chips, tok_rows, 2 * HEAD)
    feat_split = normed.reshape(tok_rows, chips, 2, normed.shape[1] // (2 * chips))
    normed_even = feat_split[:, :, 0, :]
    normed_odd = feat_split[:, :, 1, :]
    tokens_first = (((0,), (0,)), ((), ()))
    first = core == 0

    def weight_halves(grads):
        even = lax.dot_general(normed_even, grads, tokens_first, preferred_element_type=jnp.float32)
        odd = lax.dot_general(normed_odd, grads, tokens_first, preferred_element_type=jnp.float32)
        return jnp.where(first, even, odd), jnp.where(first, odd, even)

    wq_keep, wq_send = weight_halves(query_grad)
    joint = pair_sum(
        jnp.concatenate([kv_terms[0], wq_keep], axis=2), jnp.concatenate([kv_terms[1], wq_send], axis=2)
    )
    joint_total = scatter_sum(joint, ("seq_x", "seq_z"))
    kv_total = joint_total[:, : 2 * HEAD]
    grad_wq = joint_total[:, 2 * HEAD :]

    def weight_terms(grads):
        keep, send = weight_halves(grads)
        return scatter_sum(pair_sum(keep, send), ("seq_x", "seq_z"))

    contract = (((1,), (1,)), ((), ()))
    partial_input = lax.dot_general(
        w_query, query_grad, contract, preferred_element_type=jnp.float32
    )
    key_grad = rotate(kv_total[:, :HEAD], positions, -1.0).astype(jnp.bfloat16)
    value_grad = kv_total[:, HEAD:].astype(jnp.bfloat16)
    kv_grad = jnp.concatenate([key_grad, value_grad], axis=1)
    grad_wkv = weight_terms(kv_grad)
    grad_wk = grad_wkv[:, :HEAD]
    grad_wv = grad_wkv[:, HEAD:]
    partial_input = partial_input + lax.dot_general(
        w_key, key_grad, contract, preferred_element_type=jnp.float32
    )
    partial_input = partial_input + lax.dot_general(
        w_value, value_grad, contract, preferred_element_type=jnp.float32
    )
    feat = partial_input.shape[0] // kvh_count
    input_terms = partial_input.astype(jnp.bfloat16).reshape(kvh_count, feat, tok_rows)
    grad_normed = scatter_sum(input_terms, KVH_AXES).T.astype(jnp.bfloat16)
    return (grad_normed, grad_wq, grad_wk, grad_wv)


def solution(mesh):
    seq_x = 2
    seq_size = mesh.shape["seq"]
    kvh_size = mesh.shape["kvh"]
    grid = mesh.devices.reshape(seq_x, seq_size // (2 * seq_x), 2, 2, kvh_size // 2)
    fine = jax.sharding.Mesh(grid, SEQ_AXES + KVH_AXES)
    in_specs = (
        P(SEQ_AXES, None),
        P(None, KVH_AXES),
        P(None, KVH_AXES),
        P(None, KVH_AXES),
        P(SEQ_AXES),
        P(SEQ_AXES, None),
        P(SEQ_AXES, KVH_AXES),
    )
    out_specs = (P(SEQ_AXES, KVH_AXES),) * 4
    return jax.shard_map(body, mesh=fine, in_specs=in_specs, out_specs=out_specs, check_vma=False)
```

```python
import jax
import jax.numpy as jnp
from jax import lax
from jax.sharding import PartitionSpec as P

HEAD = 128
BLOCK = 128


THETA = 500000.0


def rotate(values, positions, rotation_sign):
    tok_rows = values.shape[0]
    head_count = values.shape[1] // HEAD
    half_size = HEAD // 2
    pieces = values.reshape(tok_rows, head_count, HEAD)
    frequency = THETA ** (-(jnp.arange(half_size, dtype=jnp.float32) * (2.0 / HEAD)))
    angles = positions.astype(jnp.float32)[:, None] * frequency[None, :]
    cosine = jnp.cos(angles)[:, None, :]
    sine_part = rotation_sign * jnp.sin(angles)[:, None, :]
    lower_half = pieces[:, :, :half_size]
    upper_half = pieces[:, :, half_size:]
    turned = jnp.concatenate(
        [
            lower_half * cosine - upper_half * sine_part,
            upper_half * cosine + lower_half * sine_part,
        ],
        axis=2,
    )
    return turned.reshape(tok_rows, head_count * HEAD)


def visible(mask_rows, query_block0, query_count, chunk_blocks, key_inner):
    query_local = jnp.arange(query_count)
    query_block = query_block0 + query_local // BLOCK
    table = jnp.take(mask_rows, chunk_blocks, axis=1) == 1
    key_blocks = jnp.repeat(chunk_blocks, BLOCK)
    allowed = jnp.repeat(jnp.repeat(table, BLOCK, axis=0), BLOCK, axis=1)
    inner_ok = key_inner[None, :] <= (query_local % BLOCK)[:, None]
    return allowed & ((query_block[:, None] != key_blocks[None, :]) | inner_ok)


def product(form, left, right):
    return jnp.einsum(form, left, right, preferred_element_type=jnp.float32)


def masked_scores(queries, keys, seen):
    scores = product("tgd,sd->gts", queries, keys) * HEAD ** (-0.5)
    return jnp.where(seen[None], scores, -1e30)


def softmax_stats(queries, keys, values, grad_heads, seen):
    scores = masked_scores(queries, keys, seen)
    row_max = jnp.max(scores, axis=2, keepdims=True)
    log_total = row_max[:, :, 0] + jnp.log(jnp.sum(jnp.exp(scores - row_max), axis=2))
    weights = jnp.where(seen[None], jnp.exp(scores - log_total[:, :, None]), 0.0).astype(
        jnp.bfloat16
    )
    outputs = product("gts,sd->gtd", weights, values)
    row_dots = jnp.sum(outputs * jnp.transpose(grad_heads.astype(jnp.float32), (1, 0, 2)), axis=2)
    return (log_total, row_dots)


def attention_grads(queries, keys, values, grad_heads, seen, log_total, row_dots):
    scores = masked_scores(queries, keys, seen)
    probs = jnp.where(seen[None], jnp.exp(scores - log_total[:, :, None]), 0.0)
    weights = probs.astype(jnp.bfloat16)
    grad_probs = product("tgd,sd->gts", grad_heads, values)
    grad_scores = (probs * (grad_probs - row_dots[:, :, None]) * HEAD ** (-0.5)).astype(
        jnp.bfloat16
    )
    grad_query = product("gts,sd->tgd", grad_scores, keys)
    grad_key = product("gts,tgd->sd", grad_scores, queries)
    grad_value = product("gts,tgd->sd", weights, grad_heads)
    return (grad_query, grad_key, grad_value)


SEQ_AXES = ("seq_x", "seq_z", "seq_core")
KVH_AXES = ("kvh_x", "kvh_y")
PAIR = [(0, 1), (1, 0)]


def seq_position():
    return (lax.axis_index("seq_x") * lax.axis_size("seq_z") + lax.axis_index("seq_z")) * 2 + lax.axis_index(
        "seq_core"
    )


def gather_rows(block):
    chips = lax.axis_size("seq_x") * lax.axis_size("seq_z")
    copies = jnp.broadcast_to(block[None], (chips,) + block.shape)
    mine = lax.all_to_all(copies, ("seq_x", "seq_z"), 0, 0, tiled=True)
    other = lax.ppermute(mine, "seq_core", PAIR)
    joined = jnp.stack([mine, other], axis=0)
    return joined.reshape((2 * chips * block.shape[0],) + block.shape[1:])


def pair_sum(keep, send):
    got = lax.ppermute(send.astype(jnp.bfloat16), "seq_core", PAIR)
    return (keep.astype(jnp.float32) + got.astype(jnp.float32)).astype(jnp.bfloat16)


def scatter_sum(parts, axis):
    arrived = lax.all_to_all(parts, axis, 0, 0, tiled=True)
    return jnp.sum(arrived.astype(jnp.float32), axis=0)


def body(normed, w_query, w_key, w_value, positions, block_mask, grad_attn):
    tok_rows = normed.shape[0]
    group_size = w_query.shape[1] // w_key.shape[1]
    width_query = group_size * HEAD
    blk_local = tok_rows // BLOCK
    chips = lax.axis_size("seq_x") * lax.axis_size("seq_z")
    kvh_count = lax.axis_size("kvh_x") * lax.axis_size("kvh_y")
    core = lax.axis_index("seq_core")
    my_index = seq_position()
    queries = rotate(
        jnp.dot(normed, w_query, preferred_element_type=jnp.float32), positions, 1.0
    ).astype(jnp.bfloat16)
    keys = rotate(
        jnp.dot(normed, w_key, preferred_element_type=jnp.float32), positions, 1.0
    ).astype(jnp.bfloat16)
    values = jnp.dot(normed, w_value, preferred_element_type=jnp.float32).astype(jnp.bfloat16)
    kv_all = gather_rows(jnp.concatenate([keys, values], axis=1))
    rounds = chips // 2
    chip_me = lax.axis_index("seq_x") * lax.axis_size("seq_z") + lax.axis_index("seq_z")
    round_me = chip_me // 2
    kv_grid = kv_all.reshape(2, rounds, 2, tok_rows, 2 * HEAD)
    own_kv = lax.dynamic_index_in_dim(
        lax.dynamic_index_in_dim(kv_grid[0], round_me, 0, keepdims=False), chip_me % 2, 0, keepdims=False
    )
    later = jnp.roll(kv_grid, -(round_me + 1), axis=1)[:, : rounds - 1]
    kv_sel = jnp.concatenate([own_kv[None], later.reshape(-1, tok_rows, 2 * HEAD)], axis=0)
    kv_sel = kv_sel.reshape(-1, 2 * HEAD)
    keys_all = kv_sel[:, :HEAD]
    values_all = kv_sel[:, HEAD:]
    key_count = keys_all.shape[0]
    per_shard = tok_rows // BLOCK
    chunk = jnp.arange(key_count // BLOCK - per_shard)
    shard = chunk // per_shard
    side = shard // (2 * (rounds - 1))
    chip = ((round_me + 1 + (shard // 2) % (rounds - 1)) % rounds) * 2 + shard % 2
    source = chip * 2 + jnp.where(side == 0, core, 1 - core)
    chunk_blocks = jnp.concatenate(
        [my_index * per_shard + jnp.arange(per_shard), source * per_shard + chunk % per_shard]
    )
    seen = visible(block_mask, my_index * blk_local, tok_rows, chunk_blocks, jnp.arange(key_count) % BLOCK)
    query_heads = queries.reshape(tok_rows, group_size, HEAD)
    grad_heads = grad_attn.reshape(tok_rows, group_size, HEAD)
    log_total, row_dots = softmax_stats(query_heads, keys_all, values_all, grad_heads, seen)
    grad_query, grad_key, grad_value = attention_grads(
        query_heads, keys_all, values_all, grad_heads, seen, log_total, row_dots
    )
    query_grad = rotate(grad_query.reshape(tok_rows, width_query), positions, -1.0).astype(
        jnp.bfloat16
    )
    kv_sel_terms = (
        jnp.concatenate([grad_key, grad_value], axis=1).astype(jnp.bfloat16).reshape(-1, tok_rows, 2 * HEAD)
    )
    later_terms = kv_sel_terms[1:].reshape(2, rounds - 1, 2, tok_rows, 2 * HEAD)
    place = (jnp.arange(2)[:, None] == 0) & (jnp.arange(2)[None, :] == chip_me % 2)
    own_round = jnp.where(place[:, :, None, None], kv_sel_terms[0][None, None], jnp.zeros((), jnp.bfloat16))
    kv_grid_terms = jnp.concatenate([later_terms, own_round[:, None]], axis=1)
    kv_grid_terms = jnp.roll(kv_grid_terms, round_me + 1, axis=1)
    kv_terms = kv_grid_terms.reshape(2, chips, tok_rows, 2 * HEAD)
    feat_split = normed.reshape(tok_rows, chips, 2, normed.shape[1] // (2 * chips))
    normed_even = feat_split[:, :, 0, :]
    normed_odd = feat_split[:, :, 1, :]
    tokens_first = (((0,), (0,)), ((), ()))
    first = core == 0

    def weight_halves(grads):
        even = lax.dot_general(normed_even, grads, tokens_first, preferred_element_type=jnp.float32)
        odd = lax.dot_general(normed_odd, grads, tokens_first, preferred_element_type=jnp.float32)
        return jnp.where(first, even, odd), jnp.where(first, odd, even)

    wq_keep, wq_send = weight_halves(query_grad)
    joint = pair_sum(
        jnp.concatenate([kv_terms[0], wq_keep], axis=2), jnp.concatenate([kv_terms[1], wq_send], axis=2)
    )
    joint_total = scatter_sum(joint, ("seq_x", "seq_z"))
    kv_total = joint_total[:, : 2 * HEAD]
    grad_wq = joint_total[:, 2 * HEAD :]

    def weight_terms(grads):
        keep, send = weight_halves(grads)
        return scatter_sum(pair_sum(keep, send), ("seq_x", "seq_z"))

    contract = (((1,), (1,)), ((), ()))
    partial_input = lax.dot_general(
        w_query, query_grad, contract, preferred_element_type=jnp.float32
    )
    key_grad = rotate(kv_total[:, :HEAD], positions, -1.0).astype(jnp.bfloat16)
    value_grad = kv_total[:, HEAD:].astype(jnp.bfloat16)
    kv_grad = jnp.concatenate([key_grad, value_grad], axis=1)
    grad_wkv = weight_terms(kv_grad)
    grad_wk = grad_wkv[:, :HEAD]
    grad_wv = grad_wkv[:, HEAD:]
    partial_input = partial_input + lax.dot_general(
        w_key, key_grad, contract, preferred_element_type=jnp.float32
    )
    partial_input = partial_input + lax.dot_general(
        w_value, value_grad, contract, preferred_element_type=jnp.float32
    )
    feat = partial_input.shape[0] // kvh_count
    input_terms = partial_input.astype(jnp.bfloat16).reshape(kvh_count, feat, tok_rows)
    grad_normed = scatter_sum(input_terms, KVH_AXES).T.astype(jnp.bfloat16)
    return (grad_normed, grad_wq, grad_wk, grad_wv)


def solution(mesh):
    seq_x = 2
    seq_size = mesh.shape["seq"]
    kvh_size = mesh.shape["kvh"]
    grid = mesh.devices.reshape(seq_x, seq_size // (2 * seq_x), 2, 2, kvh_size // 2)
    fine = jax.sharding.Mesh(grid, SEQ_AXES + KVH_AXES)
    in_specs = (
        P(SEQ_AXES, None),
        P(None, KVH_AXES),
        P(None, KVH_AXES),
        P(None, KVH_AXES),
        P(SEQ_AXES),
        P(SEQ_AXES, None),
        P(SEQ_AXES, KVH_AXES),
    )
    out_specs = (P(SEQ_AXES, KVH_AXES),) * 4
    return jax.shard_map(body, mesh=fine, in_specs=in_specs, out_specs=out_specs, check_vma=False)
```

```python
import jax
import jax.numpy as jnp
from jax import lax
from jax.sharding import PartitionSpec as P

HEAD = 128
BLOCK = 128


THETA = 500000.0


def rotate(values, positions, rotation_sign):
    tok_rows = values.shape[0]
    head_count = values.shape[1] // HEAD
    half_size = HEAD // 2
    pieces = values.reshape(tok_rows, head_count, HEAD)
    frequency = THETA ** (-(jnp.arange(half_size, dtype=jnp.float32) * (2.0 / HEAD)))
    angles = positions.astype(jnp.float32)[:, None] * frequency[None, :]
    cosine = jnp.cos(angles)[:, None, :]
    sine_part = rotation_sign * jnp.sin(angles)[:, None, :]
    lower_half = pieces[:, :, :half_size]
    upper_half = pieces[:, :, half_size:]
    turned = jnp.concatenate(
        [
            lower_half * cosine - upper_half * sine_part,
            upper_half * cosine + lower_half * sine_part,
        ],
        axis=2,
    )
    return turned.reshape(tok_rows, head_count * HEAD)


def visible(mask_rows, query_block0, query_count, chunk_blocks, key_inner):
    query_local = jnp.arange(query_count)
    query_block = query_block0 + query_local // BLOCK
    table = jnp.take(mask_rows, chunk_blocks, axis=1) == 1
    key_blocks = jnp.repeat(chunk_blocks, BLOCK)
    allowed = jnp.repeat(jnp.repeat(table, BLOCK, axis=0), BLOCK, axis=1)
    inner_ok = key_inner[None, :] <= (query_local % BLOCK)[:, None]
    return allowed & ((query_block[:, None] != key_blocks[None, :]) | inner_ok)


def product(form, left, right):
    return jnp.einsum(form, left, right, preferred_element_type=jnp.float32)


def masked_scores(queries, keys, seen):
    scores = product("tgd,sd->gts", queries, keys) * HEAD ** (-0.5)
    return jnp.where(seen[None], scores, -1e30)


def softmax_stats(queries, keys, values, grad_heads, seen):
    scores = masked_scores(queries, keys, seen)
    row_max = jnp.max(scores, axis=2, keepdims=True)
    log_total = row_max[:, :, 0] + jnp.log(jnp.sum(jnp.exp(scores - row_max), axis=2))
    weights = jnp.where(seen[None], jnp.exp(scores - log_total[:, :, None]), 0.0).astype(
        jnp.bfloat16
    )
    outputs = product("gts,sd->gtd", weights, values)
    row_dots = jnp.sum(outputs * jnp.transpose(grad_heads.astype(jnp.float32), (1, 0, 2)), axis=2)
    return (log_total, row_dots)


def attention_grads(queries, keys, values, grad_heads, seen, log_total, row_dots):
    scores = masked_scores(queries, keys, seen)
    probs = jnp.where(seen[None], jnp.exp(scores - log_total[:, :, None]), 0.0)
    weights = probs.astype(jnp.bfloat16)
    grad_probs = product("tgd,sd->gts", grad_heads, values)
    grad_scores = (probs * (grad_probs - row_dots[:, :, None]) * HEAD ** (-0.5)).astype(
        jnp.bfloat16
    )
    grad_query = product("gts,sd->tgd", grad_scores, keys)
    grad_key = product("gts,tgd->sd", grad_scores, queries)
    grad_value = product("gts,tgd->sd", weights, grad_heads)
    return (grad_query, grad_key, grad_value)


SEQ_AXES = ("seq_x", "seq_z", "seq_core")
KVH_AXES = ("kvh_x", "kvh_y")
PAIR = [(0, 1), (1, 0)]


def seq_position():
    return (lax.axis_index("seq_x") * lax.axis_size("seq_z") + lax.axis_index("seq_z")) * 2 + lax.axis_index(
        "seq_core"
    )


def gather_rows(block):
    chips = lax.axis_size("seq_x") * lax.axis_size("seq_z")
    copies = jnp.broadcast_to(block[None], (chips,) + block.shape)
    mine = lax.all_to_all(copies, ("seq_x", "seq_z"), 0, 0, tiled=True)
    other = lax.ppermute(mine, "seq_core", PAIR)
    joined = jnp.stack([mine, other], axis=0)
    return joined.reshape((2 * chips * block.shape[0],) + block.shape[1:])


def pair_sum(keep, send):
    got = lax.ppermute(send.astype(jnp.bfloat16), "seq_core", PAIR)
    return (keep.astype(jnp.float32) + got.astype(jnp.float32)).astype(jnp.bfloat16)


def scatter_sum(parts, axis):
    arrived = lax.all_to_all(parts, axis, 0, 0, tiled=True)
    return jnp.sum(arrived.astype(jnp.float32), axis=0)


def body(normed, w_query, w_key, w_value, positions, block_mask, grad_attn):
    tok_rows = normed.shape[0]
    group_size = w_query.shape[1] // w_key.shape[1]
    width_query = group_size * HEAD
    blk_local = tok_rows // BLOCK
    chips = lax.axis_size("seq_x") * lax.axis_size("seq_z")
    kvh_count = lax.axis_size("kvh_x") * lax.axis_size("kvh_y")
    core = lax.axis_index("seq_core")
    my_index = seq_position()
    queries = rotate(
        jnp.dot(normed, w_query, preferred_element_type=jnp.float32), positions, 1.0
    ).astype(jnp.bfloat16)
    keys = rotate(
        jnp.dot(normed, w_key, preferred_element_type=jnp.float32), positions, 1.0
    ).astype(jnp.bfloat16)
    values = jnp.dot(normed, w_value, preferred_element_type=jnp.float32).astype(jnp.bfloat16)
    kv_all = gather_rows(jnp.concatenate([keys, values], axis=1))
    rounds = chips // 2
    chip_me = lax.axis_index("seq_x") * lax.axis_size("seq_z") + lax.axis_index("seq_z")
    round_me = chip_me // 2
    kv_grid = kv_all.reshape(2, rounds, 2, tok_rows, 2 * HEAD)
    own_kv = lax.dynamic_index_in_dim(
        lax.dynamic_index_in_dim(kv_grid[0], round_me, 0, keepdims=False), chip_me % 2, 0, keepdims=False
    )
    later = jnp.roll(kv_grid, -(round_me + 1), axis=1)[:, : rounds - 1]
    kv_sel = jnp.concatenate([own_kv[None], later.reshape(-1, tok_rows, 2 * HEAD)], axis=0)
    kv_sel = kv_sel.reshape(-1, 2 * HEAD)
    keys_all = kv_sel[:, :HEAD]
    values_all = kv_sel[:, HEAD:]
    key_count = keys_all.shape[0]
    per_shard = tok_rows // BLOCK
    chunk = jnp.arange(key_count // BLOCK - per_shard)
    shard = chunk // per_shard
    side = shard // (2 * (rounds - 1))
    chip = ((round_me + 1 + (shard // 2) % (rounds - 1)) % rounds) * 2 + shard % 2
    source = chip * 2 + jnp.where(side == 0, core, 1 - core)
    chunk_blocks = jnp.concatenate(
        [my_index * per_shard + jnp.arange(per_shard), source * per_shard + chunk % per_shard]
    )
    seen = visible(block_mask, my_index * blk_local, tok_rows, chunk_blocks, jnp.arange(key_count) % BLOCK)
    query_heads = queries.reshape(tok_rows, group_size, HEAD)
    grad_heads = grad_attn.reshape(tok_rows, group_size, HEAD)
    log_total, row_dots = softmax_stats(query_heads, keys_all, values_all, grad_heads, seen)
    grad_query, grad_key, grad_value = attention_grads(
        query_heads, keys_all, values_all, grad_heads, seen, log_total, row_dots
    )
    query_grad = rotate(grad_query.reshape(tok_rows, width_query), positions, -1.0).astype(
        jnp.bfloat16
    )
    kv_sel_terms = (
        jnp.concatenate([grad_key, grad_value], axis=1).astype(jnp.bfloat16).reshape(-1, tok_rows, 2 * HEAD)
    )
    later_terms = kv_sel_terms[1:].reshape(2, rounds - 1, 2, tok_rows, 2 * HEAD)
    place = (jnp.arange(2)[:, None] == 0) & (jnp.arange(2)[None, :] == chip_me % 2)
    own_round = jnp.where(place[:, :, None, None], kv_sel_terms[0][None, None], jnp.zeros((), jnp.bfloat16))
    kv_grid_terms = jnp.concatenate([later_terms, own_round[:, None]], axis=1)
    kv_grid_terms = jnp.roll(kv_grid_terms, round_me + 1, axis=1)
    kv_terms = kv_grid_terms.reshape(2, chips, tok_rows, 2 * HEAD)
    feat_split = normed.reshape(tok_rows, chips, 2, normed.shape[1] // (2 * chips))
    by_core = jnp.transpose(feat_split, (0, 2, 1, 3))
    normed_perm = jnp.where(core == 0, by_core, by_core[:, ::-1]).reshape(tok_rows, -1)
    tokens_first = (((0,), (0,)), ((), ()))

    def weight_halves(grads):
        full = lax.dot_general(normed_perm, grads, tokens_first, preferred_element_type=jnp.float32)
        full = full.reshape((2, chips, -1) + grads.shape[1:])
        return full[0], full[1]

    wq_keep, wq_send = weight_halves(query_grad)
    joint = pair_sum(
        jnp.concatenate([kv_terms[0], wq_keep], axis=2), jnp.concatenate([kv_terms[1], wq_send], axis=2)
    )
    joint_total = scatter_sum(joint, ("seq_x", "seq_z"))
    kv_total = joint_total[:, : 2 * HEAD]
    grad_wq = joint_total[:, 2 * HEAD :]

    def weight_terms(grads):
        keep, send = weight_halves(grads)
        return scatter_sum(pair_sum(keep, send), ("seq_x", "seq_z"))

    contract = (((1,), (1,)), ((), ()))
    partial_input = lax.dot_general(
        w_query, query_grad, contract, preferred_element_type=jnp.float32
    )
    key_grad = rotate(kv_total[:, :HEAD], positions, -1.0).astype(jnp.bfloat16)
    value_grad = kv_total[:, HEAD:].astype(jnp.bfloat16)
    kv_grad = jnp.concatenate([key_grad, value_grad], axis=1)
    grad_wkv = weight_terms(kv_grad)
    grad_wk = grad_wkv[:, :HEAD]
    grad_wv = grad_wkv[:, HEAD:]
    partial_input = partial_input + lax.dot_general(
        w_key, key_grad, contract, preferred_element_type=jnp.float32
    )
    partial_input = partial_input + lax.dot_general(
        w_value, value_grad, contract, preferred_element_type=jnp.float32
    )
    feat = partial_input.shape[0] // kvh_count
    input_terms = partial_input.astype(jnp.bfloat16).reshape(kvh_count, feat, tok_rows)
    grad_normed = scatter_sum(input_terms, KVH_AXES).T.astype(jnp.bfloat16)
    return (grad_normed, grad_wq, grad_wk, grad_wv)


def solution(mesh):
    seq_x = 2
    seq_size = mesh.shape["seq"]
    kvh_size = mesh.shape["kvh"]
    grid = mesh.devices.reshape(seq_x, seq_size // (2 * seq_x), 2, 2, kvh_size // 2)
    fine = jax.sharding.Mesh(grid, SEQ_AXES + KVH_AXES)
    in_specs = (
        P(SEQ_AXES, None),
        P(None, KVH_AXES),
        P(None, KVH_AXES),
        P(None, KVH_AXES),
        P(SEQ_AXES),
        P(SEQ_AXES, None),
        P(SEQ_AXES, KVH_AXES),
    )
    out_specs = (P(SEQ_AXES, KVH_AXES),) * 4
    return jax.shard_map(body, mesh=fine, in_specs=in_specs, out_specs=out_specs, check_vma=False)
```

```python
import jax
import jax.numpy as jnp
from jax import lax
from jax.sharding import PartitionSpec as P

HEAD = 128
BLOCK = 128


THETA = 500000.0


def rotate(values, positions, rotation_sign):
    tok_rows = values.shape[0]
    head_count = values.shape[1] // HEAD
    half_size = HEAD // 2
    pieces = values.reshape(tok_rows, head_count, HEAD)
    frequency = THETA ** (-(jnp.arange(half_size, dtype=jnp.float32) * (2.0 / HEAD)))
    angles = positions.astype(jnp.float32)[:, None] * frequency[None, :]
    cosine = jnp.cos(angles)[:, None, :]
    sine_part = rotation_sign * jnp.sin(angles)[:, None, :]
    lower_half = pieces[:, :, :half_size]
    upper_half = pieces[:, :, half_size:]
    turned = jnp.concatenate(
        [
            lower_half * cosine - upper_half * sine_part,
            upper_half * cosine + lower_half * sine_part,
        ],
        axis=2,
    )
    return turned.reshape(tok_rows, head_count * HEAD)


def visible(mask_rows, query_block0, query_count, chunk_blocks, key_inner):
    query_local = jnp.arange(query_count)
    query_block = query_block0 + query_local // BLOCK
    table = jnp.take(mask_rows, chunk_blocks, axis=1) == 1
    key_blocks = jnp.repeat(chunk_blocks, BLOCK)
    allowed = jnp.repeat(jnp.repeat(table, BLOCK, axis=0), BLOCK, axis=1)
    inner_ok = key_inner[None, :] <= (query_local % BLOCK)[:, None]
    return allowed & ((query_block[:, None] != key_blocks[None, :]) | inner_ok)


def product(form, left, right):
    return jnp.einsum(form, left, right, preferred_element_type=jnp.float32)


def masked_scores(queries, keys, seen):
    scores = product("tgd,sd->gts", queries, keys) * HEAD ** (-0.5)
    return jnp.where(seen[None], scores, -1e30)


def softmax_stats(queries, keys, values, grad_heads, seen):
    scores = masked_scores(queries, keys, seen)
    row_max = jnp.max(scores, axis=2, keepdims=True)
    log_total = row_max[:, :, 0] + jnp.log(jnp.sum(jnp.exp(scores - row_max), axis=2))
    weights = jnp.where(seen[None], jnp.exp(scores - log_total[:, :, None]), 0.0).astype(
        jnp.bfloat16
    )
    outputs = product("gts,sd->gtd", weights, values)
    row_dots = jnp.sum(outputs * jnp.transpose(grad_heads.astype(jnp.float32), (1, 0, 2)), axis=2)
    return (log_total, row_dots)


def attention_grads(queries, keys, values, grad_heads, seen, log_total, row_dots):
    scores = masked_scores(queries, keys, seen)
    probs = jnp.where(seen[None], jnp.exp(scores - log_total[:, :, None]), 0.0)
    weights = probs.astype(jnp.bfloat16)
    grad_probs = product("tgd,sd->gts", grad_heads, values)
    grad_scores = (probs * (grad_probs - row_dots[:, :, None]) * HEAD ** (-0.5)).astype(
        jnp.bfloat16
    )
    grad_query = product("gts,sd->tgd", grad_scores, keys)
    grad_key = product("gts,tgd->sd", grad_scores, queries)
    grad_value = product("gts,tgd->sd", weights, grad_heads)
    return (grad_query, grad_key, grad_value)


SEQ_AXES = ("seq_x", "seq_z", "seq_core")
KVH_AXES = ("kvh_x", "kvh_y")
PAIR = [(0, 1), (1, 0)]


def seq_position():
    return (lax.axis_index("seq_x") * lax.axis_size("seq_z") + lax.axis_index("seq_z")) * 2 + lax.axis_index(
        "seq_core"
    )


def gather_rows(block):
    chips = lax.axis_size("seq_x") * lax.axis_size("seq_z")
    copies = jnp.broadcast_to(block[None], (chips,) + block.shape)
    mine = lax.all_to_all(copies, ("seq_x", "seq_z"), 0, 0, tiled=True)
    other = lax.ppermute(mine, "seq_core", PAIR)
    joined = jnp.stack([mine, other], axis=0)
    return joined.reshape((2 * chips * block.shape[0],) + block.shape[1:])


def pair_sum(keep, send):
    got = lax.ppermute(send.astype(jnp.bfloat16), "seq_core", PAIR)
    return (keep.astype(jnp.float32) + got.astype(jnp.float32)).astype(jnp.bfloat16)


def scatter_sum(parts, axis):
    arrived = lax.all_to_all(parts, axis, 0, 0, tiled=True)
    return jnp.sum(arrived.astype(jnp.float32), axis=0)


def body(normed, w_query, w_key, w_value, positions, block_mask, grad_attn):
    tok_rows = normed.shape[0]
    group_size = w_query.shape[1] // w_key.shape[1]
    width_query = group_size * HEAD
    blk_local = tok_rows // BLOCK
    chips = lax.axis_size("seq_x") * lax.axis_size("seq_z")
    kvh_count = lax.axis_size("kvh_x") * lax.axis_size("kvh_y")
    core = lax.axis_index("seq_core")
    my_index = seq_position()
    queries = rotate(
        jnp.dot(normed, w_query, preferred_element_type=jnp.float32), positions, 1.0
    ).astype(jnp.bfloat16)
    keys = rotate(
        jnp.dot(normed, w_key, preferred_element_type=jnp.float32), positions, 1.0
    ).astype(jnp.bfloat16)
    values = jnp.dot(normed, w_value, preferred_element_type=jnp.float32).astype(jnp.bfloat16)
    kv_all = gather_rows(jnp.concatenate([keys, values], axis=1))
    rounds = chips // 2
    chip_me = lax.axis_index("seq_x") * lax.axis_size("seq_z") + lax.axis_index("seq_z")
    round_me = chip_me // 2
    kv_grid = kv_all.reshape(2, rounds, 2, tok_rows, 2 * HEAD)
    own_kv = lax.dynamic_index_in_dim(
        lax.dynamic_index_in_dim(kv_grid[0], round_me, 0, keepdims=False), chip_me % 2, 0, keepdims=False
    )
    later = jnp.roll(kv_grid, -(round_me + 1), axis=1)[:, : rounds - 1]
    kv_sel = jnp.concatenate([own_kv[None], later.reshape(-1, tok_rows, 2 * HEAD)], axis=0)
    kv_sel = kv_sel.reshape(-1, 2 * HEAD)
    keys_all = kv_sel[:, :HEAD]
    values_all = kv_sel[:, HEAD:]
    key_count = keys_all.shape[0]
    per_shard = tok_rows // BLOCK
    chunk = jnp.arange(key_count // BLOCK - per_shard)
    shard = chunk // per_shard
    side = shard // (2 * (rounds - 1))
    chip = ((round_me + 1 + (shard // 2) % (rounds - 1)) % rounds) * 2 + shard % 2
    source = chip * 2 + jnp.where(side == 0, core, 1 - core)
    chunk_blocks = jnp.concatenate(
        [my_index * per_shard + jnp.arange(per_shard), source * per_shard + chunk % per_shard]
    )
    seen = visible(block_mask, my_index * blk_local, tok_rows, chunk_blocks, jnp.arange(key_count) % BLOCK)
    query_heads = queries.reshape(tok_rows, group_size, HEAD)
    grad_heads = grad_attn.reshape(tok_rows, group_size, HEAD)
    log_total, row_dots = softmax_stats(query_heads, keys_all, values_all, grad_heads, seen)
    grad_query, grad_key, grad_value = attention_grads(
        query_heads, keys_all, values_all, grad_heads, seen, log_total, row_dots
    )
    query_grad = rotate(grad_query.reshape(tok_rows, width_query), positions, -1.0).astype(
        jnp.bfloat16
    )
    kv_sel_terms = (
        jnp.concatenate([grad_key, grad_value], axis=1).astype(jnp.bfloat16).reshape(-1, tok_rows, 2 * HEAD)
    )
    later_terms = kv_sel_terms[1:].reshape(2, rounds - 1, 2, tok_rows, 2 * HEAD)
    place = (jnp.arange(2)[:, None] == 0) & (jnp.arange(2)[None, :] == chip_me % 2)
    own_round = jnp.where(place[:, :, None, None], kv_sel_terms[0][None, None], jnp.zeros((), jnp.bfloat16))
    kv_grid_terms = jnp.concatenate([later_terms, own_round[:, None]], axis=1)
    kv_grid_terms = jnp.roll(kv_grid_terms, round_me + 1, axis=1)
    kv_terms = kv_grid_terms.reshape(2, chips, tok_rows, 2 * HEAD)
    feat_split = normed.reshape(tok_rows, chips, 2, normed.shape[1] // (2 * chips))
    normed_even = feat_split[:, :, 0, :]
    normed_odd = feat_split[:, :, 1, :]
    tokens_first = (((0,), (0,)), ((), ()))
    first = core == 0

    def weight_halves(grads):
        even = lax.dot_general(normed_even, grads, tokens_first, preferred_element_type=jnp.float32)
        odd = lax.dot_general(normed_odd, grads, tokens_first, preferred_element_type=jnp.float32)
        return jnp.where(first, even, odd), jnp.where(first, odd, even)

    kv_total = scatter_sum(pair_sum(kv_terms[0], kv_terms[1]), ("seq_x", "seq_z"))
    wq_keep, wq_send = weight_halves(query_grad)
    grad_wq = scatter_sum(pair_sum(wq_keep, wq_send), ("seq_x", "seq_z"))

    def weight_terms(grads):
        keep, send = weight_halves(grads)
        return scatter_sum(pair_sum(keep, send), ("seq_x", "seq_z"))

    contract = (((1,), (1,)), ((), ()))
    partial_input = lax.dot_general(
        w_query, query_grad, contract, preferred_element_type=jnp.float32
    )
    key_grad = rotate(kv_total[:, :HEAD], positions, -1.0).astype(jnp.bfloat16)
    value_grad = kv_total[:, HEAD:].astype(jnp.bfloat16)
    kv_grad = jnp.concatenate([key_grad, value_grad], axis=1)
    grad_wkv = weight_terms(kv_grad)
    grad_wk = grad_wkv[:, :HEAD]
    grad_wv = grad_wkv[:, HEAD:]
    partial_input = partial_input + lax.dot_general(
        w_key, key_grad, contract, preferred_element_type=jnp.float32
    )
    partial_input = partial_input + lax.dot_general(
        w_value, value_grad, contract, preferred_element_type=jnp.float32
    )
    feat = partial_input.shape[0] // kvh_count
    input_terms = partial_input.astype(jnp.bfloat16).reshape(kvh_count, feat, tok_rows)
    grad_normed = scatter_sum(input_terms, KVH_AXES).T.astype(jnp.bfloat16)
    return (grad_normed, grad_wq, grad_wk, grad_wv)


def solution(mesh):
    seq_x = 2
    seq_size = mesh.shape["seq"]
    kvh_size = mesh.shape["kvh"]
    grid = mesh.devices.reshape(seq_x, seq_size // (2 * seq_x), 2, 2, kvh_size // 2)
    fine = jax.sharding.Mesh(grid, SEQ_AXES + KVH_AXES)
    in_specs = (
        P(SEQ_AXES, None),
        P(None, KVH_AXES),
        P(None, KVH_AXES),
        P(None, KVH_AXES),
        P(SEQ_AXES),
        P(SEQ_AXES, None),
        P(SEQ_AXES, KVH_AXES),
    )
    out_specs = (P(SEQ_AXES, KVH_AXES),) * 4
    return jax.shard_map(body, mesh=fine, in_specs=in_specs, out_specs=out_specs, check_vma=False)
```

```python
import jax
import jax.numpy as jnp
from jax import lax
from jax.sharding import PartitionSpec as P

HEAD = 128
BLOCK = 128


THETA = 500000.0


def rotate(values, positions, rotation_sign):
    tok_rows = values.shape[0]
    head_count = values.shape[1] // HEAD
    half_size = HEAD // 2
    pieces = values.reshape(tok_rows, head_count, HEAD)
    frequency = THETA ** (-(jnp.arange(half_size, dtype=jnp.float32) * (2.0 / HEAD)))
    angles = positions.astype(jnp.float32)[:, None] * frequency[None, :]
    cosine = jnp.cos(angles)[:, None, :]
    sine_part = rotation_sign * jnp.sin(angles)[:, None, :]
    lower_half = pieces[:, :, :half_size]
    upper_half = pieces[:, :, half_size:]
    turned = jnp.concatenate(
        [
            lower_half * cosine - upper_half * sine_part,
            upper_half * cosine + lower_half * sine_part,
        ],
        axis=2,
    )
    return turned.reshape(tok_rows, head_count * HEAD)


def visible(mask_rows, query_block0, query_count, chunk_blocks, key_inner):
    query_local = jnp.arange(query_count)
    query_block = query_block0 + query_local // BLOCK
    table = jnp.take(mask_rows, chunk_blocks, axis=1) == 1
    key_blocks = jnp.repeat(chunk_blocks, BLOCK)
    allowed = jnp.repeat(jnp.repeat(table, BLOCK, axis=0), BLOCK, axis=1)
    inner_ok = key_inner[None, :] <= (query_local % BLOCK)[:, None]
    return allowed & ((query_block[:, None] != key_blocks[None, :]) | inner_ok)


def product(form, left, right):
    return jnp.einsum(form, left, right, preferred_element_type=jnp.float32)


def masked_scores(queries, keys, seen):
    scores = product("tgd,sd->gts", queries, keys) * HEAD ** (-0.5)
    return jnp.where(seen[None], scores, -1e30)


def softmax_stats(queries, keys, values, grad_heads, seen):
    scores = masked_scores(queries, keys, seen)
    row_max = jnp.max(scores, axis=2, keepdims=True)
    log_total = row_max[:, :, 0] + jnp.log(jnp.sum(jnp.exp(scores - row_max), axis=2))
    weights = jnp.where(seen[None], jnp.exp(scores - log_total[:, :, None]), 0.0).astype(
        jnp.bfloat16
    )
    outputs = product("gts,sd->gtd", weights, values)
    row_dots = jnp.sum(outputs * jnp.transpose(grad_heads.astype(jnp.float32), (1, 0, 2)), axis=2)
    return (log_total, row_dots)


def attention_grads(queries, keys, values, grad_heads, seen, log_total, row_dots):
    scores = masked_scores(queries, keys, seen)
    probs = jnp.where(seen[None], jnp.exp(scores - log_total[:, :, None]), 0.0)
    weights = probs.astype(jnp.bfloat16)
    grad_probs = product("tgd,sd->gts", grad_heads, values)
    grad_scores = (probs * (grad_probs - row_dots[:, :, None]) * HEAD ** (-0.5)).astype(
        jnp.bfloat16
    )
    grad_query = product("gts,sd->tgd", grad_scores, keys)
    grad_key = product("gts,tgd->sd", grad_scores, queries)
    grad_value = product("gts,tgd->sd", weights, grad_heads)
    return (grad_query, grad_key, grad_value)


SEQ_AXES = ("seq_x", "seq_z", "seq_core")
KVH_AXES = ("kvh_x", "kvh_y")
PAIR = [(0, 1), (1, 0)]


def seq_position():
    return (lax.axis_index("seq_x") * lax.axis_size("seq_z") + lax.axis_index("seq_z")) * 2 + lax.axis_index(
        "seq_core"
    )


def gather_rows(block):
    chips = lax.axis_size("seq_x") * lax.axis_size("seq_z")
    copies = jnp.broadcast_to(block[None], (chips,) + block.shape)
    mine = lax.all_to_all(copies, ("seq_x", "seq_z"), 0, 0, tiled=True)
    other = lax.ppermute(mine, "seq_core", PAIR)
    joined = jnp.stack([mine, other], axis=0)
    return joined.reshape((2 * chips * block.shape[0],) + block.shape[1:])


def pair_sum(keep, send):
    got = lax.ppermute(send.astype(jnp.bfloat16), "seq_core", PAIR)
    return (keep.astype(jnp.float32) + got.astype(jnp.float32)).astype(jnp.bfloat16)


def scatter_sum(parts, axis):
    arrived = lax.all_to_all(parts, axis, 0, 0, tiled=True)
    return jnp.sum(arrived.astype(jnp.float32), axis=0)


def body(normed, w_query, w_key, w_value, positions, block_mask, grad_attn):
    tok_rows = normed.shape[0]
    group_size = w_query.shape[1] // w_key.shape[1]
    width_query = group_size * HEAD
    blk_local = tok_rows // BLOCK
    chips = lax.axis_size("seq_x") * lax.axis_size("seq_z")
    kvh_count = lax.axis_size("kvh_x") * lax.axis_size("kvh_y")
    core = lax.axis_index("seq_core")
    my_index = seq_position()
    queries = rotate(
        jnp.dot(normed, w_query, preferred_element_type=jnp.float32), positions, 1.0
    ).astype(jnp.bfloat16)
    keys = rotate(
        jnp.dot(normed, w_key, preferred_element_type=jnp.float32), positions, 1.0
    ).astype(jnp.bfloat16)
    values = jnp.dot(normed, w_value, preferred_element_type=jnp.float32).astype(jnp.bfloat16)
    kv_all = gather_rows(jnp.concatenate([keys, values], axis=1))
    rounds = chips // 2
    chip_me = lax.axis_index("seq_x") * lax.axis_size("seq_z") + lax.axis_index("seq_z")
    round_me = chip_me // 2
    kv_grid = kv_all.reshape(2, rounds, 2, tok_rows, 2 * HEAD)
    own_kv = lax.dynamic_index_in_dim(
        lax.dynamic_index_in_dim(kv_grid[0], round_me, 0, keepdims=False), chip_me % 2, 0, keepdims=False
    )
    later = jnp.roll(kv_grid, -(round_me + 1), axis=1)[:, : rounds - 1]
    kv_sel = jnp.concatenate([own_kv[None], later.reshape(-1, tok_rows, 2 * HEAD)], axis=0)
    kv_sel = kv_sel.reshape(-1, 2 * HEAD)
    keys_all = kv_sel[:, :HEAD]
    values_all = kv_sel[:, HEAD:]
    key_count = keys_all.shape[0]
    per_shard = tok_rows // BLOCK
    chunk = jnp.arange(key_count // BLOCK - per_shard)
    shard = chunk // per_shard
    side = shard // (2 * (rounds - 1))
    chip = ((round_me + 1 + (shard // 2) % (rounds - 1)) % rounds) * 2 + shard % 2
    source = chip * 2 + jnp.where(side == 0, core, 1 - core)
    chunk_blocks = jnp.concatenate(
        [my_index * per_shard + jnp.arange(per_shard), source * per_shard + chunk % per_shard]
    )
    seen = visible(block_mask, my_index * blk_local, tok_rows, chunk_blocks, jnp.arange(key_count) % BLOCK)
    query_heads = queries.reshape(tok_rows, group_size, HEAD)
    grad_heads = grad_attn.reshape(tok_rows, group_size, HEAD)
    log_total, row_dots = softmax_stats(query_heads, keys_all, values_all, grad_heads, seen)
    grad_query, grad_key, grad_value = attention_grads(
        query_heads, keys_all, values_all, grad_heads, seen, log_total, row_dots
    )
    query_grad = rotate(grad_query.reshape(tok_rows, width_query), positions, -1.0).astype(
        jnp.bfloat16
    )
    kv_sel_terms = (
        jnp.concatenate([grad_key, grad_value], axis=1).astype(jnp.bfloat16).reshape(-1, tok_rows, 2 * HEAD)
    )
    later_terms = kv_sel_terms[1:].reshape(2, rounds - 1, 2, tok_rows, 2 * HEAD)
    place = (jnp.arange(2)[:, None] == 0) & (jnp.arange(2)[None, :] == chip_me % 2)
    own_round = jnp.where(place[:, :, None, None], kv_sel_terms[0][None, None], jnp.zeros((), jnp.bfloat16))
    kv_grid_terms = jnp.concatenate([later_terms, own_round[:, None]], axis=1)
    kv_grid_terms = jnp.roll(kv_grid_terms, round_me + 1, axis=1)
    kv_terms = kv_grid_terms.reshape(2, chips, tok_rows, 2 * HEAD)
    feat_split = normed.reshape(tok_rows, chips, 2, normed.shape[1] // (2 * chips))
    normed_even = feat_split[:, :, 0, :]
    normed_odd = feat_split[:, :, 1, :]
    tokens_first = (((0,), (0,)), ((), ()))
    first = core == 0

    def weight_halves(grads):
        even = lax.dot_general(normed_even, grads, tokens_first, preferred_element_type=jnp.float32)
        odd = lax.dot_general(normed_odd, grads, tokens_first, preferred_element_type=jnp.float32)
        return jnp.where(first, even, odd), jnp.where(first, odd, even)

    kv_total = scatter_sum(pair_sum(kv_terms[0], kv_terms[1]), ("seq_x", "seq_z"))
    wq_keep, wq_send = weight_halves(query_grad)

    def weight_terms(grads):
        keep, send = weight_halves(grads)
        return scatter_sum(pair_sum(keep, send), ("seq_x", "seq_z"))

    contract = (((1,), (1,)), ((), ()))
    partial_input = lax.dot_general(
        w_query, query_grad, contract, preferred_element_type=jnp.float32
    )
    key_grad = rotate(kv_total[:, :HEAD], positions, -1.0).astype(jnp.bfloat16)
    value_grad = kv_total[:, HEAD:].astype(jnp.bfloat16)
    kv_grad = jnp.concatenate([key_grad, value_grad], axis=1)
    wkv_keep, wkv_send = weight_halves(kv_grad)
    grad_w = scatter_sum(
        pair_sum(jnp.concatenate([wq_keep, wkv_keep], axis=-1), jnp.concatenate([wq_send, wkv_send], axis=-1)),
        ("seq_x", "seq_z"),
    )
    query_cols = wq_keep.shape[-1]
    grad_wq = grad_w[:, :query_cols]
    grad_wk = grad_w[:, query_cols : query_cols + HEAD]
    grad_wv = grad_w[:, query_cols + HEAD :]
    partial_input = partial_input + lax.dot_general(
        w_key, key_grad, contract, preferred_element_type=jnp.float32
    )
    partial_input = partial_input + lax.dot_general(
        w_value, value_grad, contract, preferred_element_type=jnp.float32
    )
    feat = partial_input.shape[0] // kvh_count
    input_terms = partial_input.astype(jnp.bfloat16).reshape(kvh_count, feat, tok_rows)
    grad_normed = scatter_sum(input_terms, KVH_AXES).T.astype(jnp.bfloat16)
    return (grad_normed, grad_wq, grad_wk, grad_wv)


def solution(mesh):
    seq_x = 2
    seq_size = mesh.shape["seq"]
    kvh_size = mesh.shape["kvh"]
    grid = mesh.devices.reshape(seq_x, seq_size // (2 * seq_x), 2, 2, kvh_size // 2)
    fine = jax.sharding.Mesh(grid, SEQ_AXES + KVH_AXES)
    in_specs = (
        P(SEQ_AXES, None),
        P(None, KVH_AXES),
        P(None, KVH_AXES),
        P(None, KVH_AXES),
        P(SEQ_AXES),
        P(SEQ_AXES, None),
        P(SEQ_AXES, KVH_AXES),
    )
    out_specs = (P(SEQ_AXES, KVH_AXES),) * 4
    return jax.shard_map(body, mesh=fine, in_specs=in_specs, out_specs=out_specs, check_vma=False)
```

```python
import jax
import jax.numpy as jnp
from jax import lax
from jax.sharding import PartitionSpec as P

HEAD = 128
BLOCK = 128


THETA = 500000.0


def rotate(values, positions, rotation_sign):
    tok_rows = values.shape[0]
    head_count = values.shape[1] // HEAD
    half_size = HEAD // 2
    pieces = values.reshape(tok_rows, head_count, HEAD)
    frequency = THETA ** (-(jnp.arange(half_size, dtype=jnp.float32) * (2.0 / HEAD)))
    angles = positions.astype(jnp.float32)[:, None] * frequency[None, :]
    cosine = jnp.cos(angles)[:, None, :]
    sine_part = rotation_sign * jnp.sin(angles)[:, None, :]
    lower_half = pieces[:, :, :half_size]
    upper_half = pieces[:, :, half_size:]
    turned = jnp.concatenate(
        [
            lower_half * cosine - upper_half * sine_part,
            upper_half * cosine + lower_half * sine_part,
        ],
        axis=2,
    )
    return turned.reshape(tok_rows, head_count * HEAD)


def visible(mask_rows, query_block0, query_count, chunk_blocks, key_inner):
    query_local = jnp.arange(query_count)
    query_block = query_block0 + query_local // BLOCK
    table = jnp.take(mask_rows, chunk_blocks, axis=1) == 1
    key_blocks = jnp.repeat(chunk_blocks, BLOCK)
    allowed = jnp.repeat(jnp.repeat(table, BLOCK, axis=0), BLOCK, axis=1)
    inner_ok = key_inner[None, :] <= (query_local % BLOCK)[:, None]
    return allowed & ((query_block[:, None] != key_blocks[None, :]) | inner_ok)


def product(form, left, right):
    return jnp.einsum(form, left, right, preferred_element_type=jnp.float32)


def masked_scores(queries, keys, seen):
    scores = product("tgd,sd->gts", queries, keys) * HEAD ** (-0.5)
    return jnp.where(seen[None], scores, -1e30)


def softmax_stats(queries, keys, values, grad_heads, seen):
    scores = masked_scores(queries, keys, seen)
    row_max = jnp.max(scores, axis=2, keepdims=True)
    log_total = row_max[:, :, 0] + jnp.log(jnp.sum(jnp.exp(scores - row_max), axis=2))
    weights = jnp.where(seen[None], jnp.exp(scores - log_total[:, :, None]), 0.0).astype(
        jnp.bfloat16
    )
    outputs = product("gts,sd->gtd", weights, values)
    row_dots = jnp.sum(outputs * jnp.transpose(grad_heads.astype(jnp.float32), (1, 0, 2)), axis=2)
    return (log_total, row_dots)


def attention_grads(queries, keys, values, grad_heads, seen, log_total, row_dots):
    scores = masked_scores(queries, keys, seen)
    probs = jnp.where(seen[None], jnp.exp(scores - log_total[:, :, None]), 0.0)
    weights = probs.astype(jnp.bfloat16)
    grad_probs = product("tgd,sd->gts", grad_heads, values)
    grad_scores = (probs * (grad_probs - row_dots[:, :, None]) * HEAD ** (-0.5)).astype(
        jnp.bfloat16
    )
    grad_query = product("gts,sd->tgd", grad_scores, keys)
    grad_key = product("gts,tgd->sd", grad_scores, queries)
    grad_value = product("gts,tgd->sd", weights, grad_heads)
    return (grad_query, grad_key, grad_value)


SEQ_AXES = ("seq_x", "seq_z", "seq_core")
KVH_AXES = ("kvh_x", "kvh_y")
PAIR = [(0, 1), (1, 0)]


def seq_position():
    return (lax.axis_index("seq_x") * lax.axis_size("seq_z") + lax.axis_index("seq_z")) * 2 + lax.axis_index(
        "seq_core"
    )


def gather_rows(block):
    chips = lax.axis_size("seq_x") * lax.axis_size("seq_z")
    copies = jnp.broadcast_to(block[None], (chips,) + block.shape)
    mine = lax.all_to_all(copies, ("seq_x", "seq_z"), 0, 0, tiled=True)
    other = lax.ppermute(mine, "seq_core", PAIR)
    joined = jnp.stack([mine, other], axis=0)
    return joined.reshape((2 * chips * block.shape[0],) + block.shape[1:])


def pair_sum(keep, send):
    got = lax.ppermute(send.astype(jnp.bfloat16), "seq_core", PAIR)
    return (keep.astype(jnp.float32) + got.astype(jnp.float32)).astype(jnp.bfloat16)


def scatter_sum(parts, axis):
    arrived = lax.all_to_all(parts, axis, 0, 0, tiled=True)
    return jnp.sum(arrived.astype(jnp.float32), axis=0)


def body(normed, w_query, w_key, w_value, positions, block_mask, grad_attn):
    tok_rows = normed.shape[0]
    group_size = w_query.shape[1] // w_key.shape[1]
    width_query = group_size * HEAD
    blk_local = tok_rows // BLOCK
    chips = lax.axis_size("seq_x") * lax.axis_size("seq_z")
    kvh_count = lax.axis_size("kvh_x") * lax.axis_size("kvh_y")
    core = lax.axis_index("seq_core")
    my_index = seq_position()
    queries = rotate(
        jnp.dot(normed, w_query, preferred_element_type=jnp.float32), positions, 1.0
    ).astype(jnp.bfloat16)
    keys = rotate(
        jnp.dot(normed, w_key, preferred_element_type=jnp.float32), positions, 1.0
    ).astype(jnp.bfloat16)
    values = jnp.dot(normed, w_value, preferred_element_type=jnp.float32).astype(jnp.bfloat16)
    kv_all = gather_rows(jnp.concatenate([keys, values], axis=1))
    rounds = chips // 2
    chip_me = lax.axis_index("seq_x") * lax.axis_size("seq_z") + lax.axis_index("seq_z")
    round_me = chip_me // 2
    kv_grid = kv_all.reshape(2, rounds, 2, tok_rows, 2 * HEAD)
    own_kv = lax.dynamic_index_in_dim(
        lax.dynamic_index_in_dim(kv_grid[0], round_me, 0, keepdims=False), chip_me % 2, 0, keepdims=False
    )
    later = jnp.roll(kv_grid, -(round_me + 1), axis=1)[:, : rounds - 1]
    kv_sel = jnp.concatenate([own_kv[None], later.reshape(-1, tok_rows, 2 * HEAD)], axis=0)
    kv_sel = kv_sel.reshape(-1, 2 * HEAD)
    keys_all = kv_sel[:, :HEAD]
    values_all = kv_sel[:, HEAD:]
    key_count = keys_all.shape[0]
    per_shard = tok_rows // BLOCK
    chunk = jnp.arange(key_count // BLOCK - per_shard)
    shard = chunk // per_shard
    side = shard // (2 * (rounds - 1))
    chip = ((round_me + 1 + (shard // 2) % (rounds - 1)) % rounds) * 2 + shard % 2
    source = chip * 2 + jnp.where(side == 0, core, 1 - core)
    chunk_blocks = jnp.concatenate(
        [my_index * per_shard + jnp.arange(per_shard), source * per_shard + chunk % per_shard]
    )
    seen = visible(block_mask, my_index * blk_local, tok_rows, chunk_blocks, jnp.arange(key_count) % BLOCK)
    query_heads = queries.reshape(tok_rows, group_size, HEAD)
    grad_heads = grad_attn.reshape(tok_rows, group_size, HEAD)
    log_total, row_dots = softmax_stats(query_heads, keys_all, values_all, grad_heads, seen)
    grad_query, grad_key, grad_value = attention_grads(
        query_heads, keys_all, values_all, grad_heads, seen, log_total, row_dots
    )
    query_grad = rotate(grad_query.reshape(tok_rows, width_query), positions, -1.0).astype(
        jnp.bfloat16
    )
    kv_sel_terms = (
        jnp.concatenate([grad_key, grad_value], axis=1).astype(jnp.bfloat16).reshape(-1, tok_rows, 2 * HEAD)
    )
    later_terms = kv_sel_terms[1:].reshape(2, rounds - 1, 2, tok_rows, 2 * HEAD)
    place = (jnp.arange(2)[:, None] == 0) & (jnp.arange(2)[None, :] == chip_me % 2)
    own_round = jnp.where(place[:, :, None, None], kv_sel_terms[0][None, None], jnp.zeros((), jnp.bfloat16))
    kv_grid_terms = jnp.concatenate([later_terms, own_round[:, None]], axis=1)
    kv_grid_terms = jnp.roll(kv_grid_terms, round_me + 1, axis=1)
    kv_terms = kv_grid_terms.reshape(2, chips, tok_rows, 2 * HEAD)
    feat_split = normed.reshape(tok_rows, chips, 2, normed.shape[1] // (2 * chips))
    normed_even = feat_split[:, :, 0, :]
    normed_odd = feat_split[:, :, 1, :]
    tokens_first = (((0,), (0,)), ((), ()))
    first = core == 0

    def weight_halves(grads):
        even = lax.dot_general(normed_even, grads, tokens_first, preferred_element_type=jnp.float32)
        odd = lax.dot_general(normed_odd, grads, tokens_first, preferred_element_type=jnp.float32)
        return jnp.where(first, even, odd), jnp.where(first, odd, even)

    kv_total = scatter_sum(pair_sum(kv_terms[0], kv_terms[1]), ("seq_x", "seq_z"))
    wq_keep, wq_send = weight_halves(query_grad)
    kv_total, wq_terms = lax.optimization_barrier((kv_total, pair_sum(wq_keep, wq_send)))
    grad_wq = scatter_sum(wq_terms, ("seq_x", "seq_z"))

    def weight_terms(grads):
        keep, send = weight_halves(grads)
        return scatter_sum(pair_sum(keep, send), ("seq_x", "seq_z"))

    contract = (((1,), (1,)), ((), ()))
    partial_input = lax.dot_general(
        w_query, query_grad, contract, preferred_element_type=jnp.float32
    )
    key_grad = rotate(kv_total[:, :HEAD], positions, -1.0).astype(jnp.bfloat16)
    value_grad = kv_total[:, HEAD:].astype(jnp.bfloat16)
    grad_wq, key_grad, value_grad = lax.optimization_barrier((grad_wq, key_grad, value_grad))
    kv_grad = jnp.concatenate([key_grad, value_grad], axis=1)
    grad_wkv = weight_terms(kv_grad)
    grad_wk = grad_wkv[:, :HEAD]
    grad_wv = grad_wkv[:, HEAD:]
    partial_input = partial_input + lax.dot_general(
        w_key, key_grad, contract, preferred_element_type=jnp.float32
    )
    partial_input = partial_input + lax.dot_general(
        w_value, value_grad, contract, preferred_element_type=jnp.float32
    )
    feat = partial_input.shape[0] // kvh_count
    input_terms = partial_input.astype(jnp.bfloat16).reshape(kvh_count, feat, tok_rows)
    grad_normed = scatter_sum(input_terms, KVH_AXES).T.astype(jnp.bfloat16)
    return (grad_normed, grad_wq, grad_wk, grad_wv)


def solution(mesh):
    seq_x = 2
    seq_size = mesh.shape["seq"]
    kvh_size = mesh.shape["kvh"]
    grid = mesh.devices.reshape(seq_x, seq_size // (2 * seq_x), 2, 2, kvh_size // 2)
    fine = jax.sharding.Mesh(grid, SEQ_AXES + KVH_AXES)
    in_specs = (
        P(SEQ_AXES, None),
        P(None, KVH_AXES),
        P(None, KVH_AXES),
        P(None, KVH_AXES),
        P(SEQ_AXES),
        P(SEQ_AXES, None),
        P(SEQ_AXES, KVH_AXES),
    )
    out_specs = (P(SEQ_AXES, KVH_AXES),) * 4
    return jax.shard_map(body, mesh=fine, in_specs=in_specs, out_specs=out_specs, check_vma=False)
```

```python
import jax
import jax.numpy as jnp
from jax import lax
from jax.sharding import PartitionSpec as P

HEAD = 128
BLOCK = 128


THETA = 500000.0


def rotate(values, positions, rotation_sign):
    tok_rows = values.shape[0]
    head_count = values.shape[1] // HEAD
    half_size = HEAD // 2
    pieces = values.reshape(tok_rows, head_count, HEAD)
    frequency = THETA ** (-(jnp.arange(half_size, dtype=jnp.float32) * (2.0 / HEAD)))
    angles = positions.astype(jnp.float32)[:, None] * frequency[None, :]
    cosine = jnp.cos(angles)[:, None, :]
    sine_part = rotation_sign * jnp.sin(angles)[:, None, :]
    lower_half = pieces[:, :, :half_size]
    upper_half = pieces[:, :, half_size:]
    turned = jnp.concatenate(
        [
            lower_half * cosine - upper_half * sine_part,
            upper_half * cosine + lower_half * sine_part,
        ],
        axis=2,
    )
    return turned.reshape(tok_rows, head_count * HEAD)


def visible(mask_rows, query_block0, query_count, chunk_blocks, key_inner):
    query_local = jnp.arange(query_count)
    query_block = query_block0 + query_local // BLOCK
    table = jnp.take(mask_rows, chunk_blocks, axis=1) == 1
    key_blocks = jnp.repeat(chunk_blocks, BLOCK)
    allowed = jnp.repeat(jnp.repeat(table, BLOCK, axis=0), BLOCK, axis=1)
    inner_ok = key_inner[None, :] <= (query_local % BLOCK)[:, None]
    return allowed & ((query_block[:, None] != key_blocks[None, :]) | inner_ok)


def product(form, left, right):
    return jnp.einsum(form, left, right, preferred_element_type=jnp.float32)


def masked_scores(queries, keys, seen):
    scores = product("tgd,sd->gts", queries, keys) * HEAD ** (-0.5)
    return jnp.where(seen[None], scores, -1e30)


def softmax_stats(queries, keys, values, grad_heads, seen):
    scores = masked_scores(queries, keys, seen)
    row_max = jnp.max(scores, axis=2, keepdims=True)
    log_total = row_max[:, :, 0] + jnp.log(jnp.sum(jnp.exp(scores - row_max), axis=2))
    weights = jnp.where(seen[None], jnp.exp(scores - log_total[:, :, None]), 0.0).astype(
        jnp.bfloat16
    )
    outputs = product("gts,sd->gtd", weights, values)
    row_dots = jnp.sum(outputs * jnp.transpose(grad_heads.astype(jnp.float32), (1, 0, 2)), axis=2)
    return (log_total, row_dots)


def attention_grads(queries, keys, values, grad_heads, seen, log_total, row_dots):
    scores = masked_scores(queries, keys, seen)
    probs = jnp.where(seen[None], jnp.exp(scores - log_total[:, :, None]), 0.0)
    weights = probs.astype(jnp.bfloat16)
    grad_probs = product("tgd,sd->gts", grad_heads, values)
    grad_scores = (probs * (grad_probs - row_dots[:, :, None]) * HEAD ** (-0.5)).astype(
        jnp.bfloat16
    )
    grad_query = product("gts,sd->tgd", grad_scores, keys)
    grad_key = product("gts,tgd->sd", grad_scores, queries)
    grad_value = product("gts,tgd->sd", weights, grad_heads)
    return (grad_query, grad_key, grad_value)


SEQ_AXES = ("seq_x", "seq_z", "seq_core")
KVH_AXES = ("kvh_x", "kvh_y")
PAIR = [(0, 1), (1, 0)]


def seq_position():
    return (lax.axis_index("seq_x") * lax.axis_size("seq_z") + lax.axis_index("seq_z")) * 2 + lax.axis_index(
        "seq_core"
    )


def gather_rows(block):
    chips = lax.axis_size("seq_x") * lax.axis_size("seq_z")
    copies = jnp.broadcast_to(block[None], (chips,) + block.shape)
    mine = lax.all_to_all(copies, ("seq_x", "seq_z"), 0, 0, tiled=True)
    other = lax.ppermute(mine, "seq_core", PAIR)
    joined = jnp.stack([mine, other], axis=0)
    return joined.reshape((2 * chips * block.shape[0],) + block.shape[1:])


def pair_sum(keep, send):
    got = lax.ppermute(send.astype(jnp.bfloat16), "seq_core", PAIR)
    return (keep.astype(jnp.float32) + got.astype(jnp.float32)).astype(jnp.bfloat16)


def scatter_sum(parts, axis):
    arrived = lax.all_to_all(parts, axis, 0, 0, tiled=True)
    return jnp.sum(arrived.astype(jnp.float32), axis=0)


def body(normed, w_query, w_key, w_value, positions, block_mask, grad_attn):
    tok_rows = normed.shape[0]
    group_size = w_query.shape[1] // w_key.shape[1]
    width_query = group_size * HEAD
    blk_local = tok_rows // BLOCK
    chips = lax.axis_size("seq_x") * lax.axis_size("seq_z")
    kvh_count = lax.axis_size("kvh_x") * lax.axis_size("kvh_y")
    core = lax.axis_index("seq_core")
    my_index = seq_position()
    queries = rotate(
        jnp.dot(normed, w_query, preferred_element_type=jnp.float32), positions, 1.0
    ).astype(jnp.bfloat16)
    keys = rotate(
        jnp.dot(normed, w_key, preferred_element_type=jnp.float32), positions, 1.0
    ).astype(jnp.bfloat16)
    values = jnp.dot(normed, w_value, preferred_element_type=jnp.float32).astype(jnp.bfloat16)
    kv_all = gather_rows(jnp.concatenate([keys, values], axis=1))
    keys_all = kv_all[:, :HEAD]
    values_all = kv_all[:, HEAD:]
    key_count = keys_all.shape[0]
    chunk = jnp.arange(key_count // BLOCK)
    per_shard = tok_rows // BLOCK
    side = chunk // (chips * per_shard)
    chip = (chunk // per_shard) % chips
    chunk_blocks = (chip * 2 + jnp.where(side == 0, core, 1 - core)) * per_shard + chunk % per_shard
    seen = visible(block_mask, my_index * blk_local, tok_rows, chunk_blocks, jnp.arange(key_count) % BLOCK)
    query_heads = queries.reshape(tok_rows, group_size, HEAD)
    grad_heads = grad_attn.reshape(tok_rows, group_size, HEAD)
    log_total, row_dots = softmax_stats(query_heads, keys_all, values_all, grad_heads, seen)
    grad_query, grad_key, grad_value = attention_grads(
        query_heads, keys_all, values_all, grad_heads, seen, log_total, row_dots
    )
    query_grad = rotate(grad_query.reshape(tok_rows, width_query), positions, -1.0).astype(
        jnp.bfloat16
    )
    kv_terms = jnp.concatenate([grad_key, grad_value], axis=1).reshape(2, chips, tok_rows, 2 * HEAD)
    feat_split = normed.reshape(tok_rows, chips, 2, normed.shape[1] // (2 * chips))
    normed_even = feat_split[:, :, 0, :]
    normed_odd = feat_split[:, :, 1, :]
    tokens_first = (((0,), (0,)), ((), ()))
    first = core == 0

    def weight_halves(grads):
        even = lax.dot_general(normed_even, grads, tokens_first, preferred_element_type=jnp.float32)
        odd = lax.dot_general(normed_odd, grads, tokens_first, preferred_element_type=jnp.float32)
        return jnp.where(first, even, odd), jnp.where(first, odd, even)

    wq_keep, wq_send = weight_halves(query_grad)
    joint = pair_sum(
        jnp.concatenate([kv_terms[0], wq_keep], axis=2), jnp.concatenate([kv_terms[1], wq_send], axis=2)
    )
    joint_total = scatter_sum(joint, ("seq_x", "seq_z"))
    kv_total = joint_total[:, : 2 * HEAD]
    grad_wq = joint_total[:, 2 * HEAD :]

    def weight_terms(grads):
        keep, send = weight_halves(grads)
        return scatter_sum(pair_sum(keep, send), ("seq_x", "seq_z"))

    contract = (((1,), (1,)), ((), ()))
    partial_input = lax.dot_general(
        query_grad, w_query, contract, preferred_element_type=jnp.float32
    )
    key_grad = rotate(kv_total[:, :HEAD], positions, -1.0).astype(jnp.bfloat16)
    value_grad = kv_total[:, HEAD:].astype(jnp.bfloat16)
    kv_grad = jnp.concatenate([key_grad, value_grad], axis=1)
    grad_wkv = weight_terms(kv_grad)
    grad_wk = grad_wkv[:, :HEAD]
    grad_wv = grad_wkv[:, HEAD:]
    partial_input = partial_input + lax.dot_general(
        key_grad, w_key, contract, preferred_element_type=jnp.float32
    )
    partial_input = partial_input + lax.dot_general(
        value_grad, w_value, contract, preferred_element_type=jnp.float32
    )
    feat = partial_input.shape[1] // kvh_count
    input_terms = partial_input.astype(jnp.bfloat16).reshape(tok_rows, kvh_count, feat)
    arrived = lax.all_to_all(input_terms, KVH_AXES, 1, 1, tiled=True)
    grad_normed = jnp.sum(arrived.astype(jnp.float32), axis=1).astype(jnp.bfloat16)
    return (grad_normed, grad_wq, grad_wk, grad_wv)


def solution(mesh):
    seq_x = 2
    seq_size = mesh.shape["seq"]
    kvh_size = mesh.shape["kvh"]
    grid = mesh.devices.reshape(seq_x, seq_size // (2 * seq_x), 2, 2, kvh_size // 2)
    fine = jax.sharding.Mesh(grid, SEQ_AXES + KVH_AXES)
    in_specs = (
        P(SEQ_AXES, None),
        P(None, KVH_AXES),
        P(None, KVH_AXES),
        P(None, KVH_AXES),
        P(SEQ_AXES),
        P(SEQ_AXES, None),
        P(SEQ_AXES, KVH_AXES),
    )
    out_specs = (P(SEQ_AXES, KVH_AXES),) * 4
    return jax.shard_map(body, mesh=fine, in_specs=in_specs, out_specs=out_specs, check_vma=False)
```

```python
import jax
import jax.numpy as jnp
from jax import lax
from jax.sharding import PartitionSpec as P

HEAD = 128
BLOCK = 128


THETA = 500000.0


def rotate(values, positions, rotation_sign):
    tok_rows = values.shape[0]
    head_count = values.shape[1] // HEAD
    half_size = HEAD // 2
    pieces = values.reshape(tok_rows, head_count, HEAD)
    frequency = THETA ** (-(jnp.arange(half_size, dtype=jnp.float32) * (2.0 / HEAD)))
    angles = positions.astype(jnp.float32)[:, None] * frequency[None, :]
    cosine = jnp.cos(angles)[:, None, :]
    sine_part = rotation_sign * jnp.sin(angles)[:, None, :]
    lower_half = pieces[:, :, :half_size]
    upper_half = pieces[:, :, half_size:]
    turned = jnp.concatenate(
        [
            lower_half * cosine - upper_half * sine_part,
            upper_half * cosine + lower_half * sine_part,
        ],
        axis=2,
    )
    return turned.reshape(tok_rows, head_count * HEAD)


def visible(mask_rows, query_block0, query_count, chunk_blocks, key_inner):
    query_local = jnp.arange(query_count)
    query_block = query_block0 + query_local // BLOCK
    table = jnp.take(mask_rows, chunk_blocks, axis=1) == 1
    key_blocks = jnp.repeat(chunk_blocks, BLOCK)
    allowed = jnp.repeat(jnp.repeat(table, BLOCK, axis=0), BLOCK, axis=1)
    inner_ok = key_inner[None, :] <= (query_local % BLOCK)[:, None]
    return allowed & ((query_block[:, None] != key_blocks[None, :]) | inner_ok)


def product(form, left, right):
    return jnp.einsum(form, left, right, preferred_element_type=jnp.float32)


def masked_scores(queries, keys, seen):
    scores = product("tgd,sd->gts", queries, keys) * HEAD ** (-0.5)
    return jnp.where(seen[None], scores, -1e30)


def softmax_stats(queries, keys, values, grad_heads, seen):
    scores = masked_scores(queries, keys, seen)
    row_max = jnp.max(scores, axis=2, keepdims=True)
    log_total = row_max[:, :, 0] + jnp.log(jnp.sum(jnp.exp(scores - row_max), axis=2))
    weights = jnp.where(seen[None], jnp.exp(scores - log_total[:, :, None]), 0.0).astype(
        jnp.bfloat16
    )
    outputs = product("gts,sd->gtd", weights, values)
    row_dots = jnp.sum(outputs * jnp.transpose(grad_heads.astype(jnp.float32), (1, 0, 2)), axis=2)
    return (log_total, row_dots)


def attention_grads(queries, keys, values, grad_heads, seen, log_total, row_dots):
    scores = masked_scores(queries, keys, seen)
    probs = jnp.where(seen[None], jnp.exp(scores - log_total[:, :, None]), 0.0)
    weights = probs.astype(jnp.bfloat16)
    grad_probs = product("tgd,sd->gts", grad_heads, values)
    grad_scores = (probs * (grad_probs - row_dots[:, :, None]) * HEAD ** (-0.5)).astype(
        jnp.bfloat16
    )
    grad_query = product("gts,sd->tgd", grad_scores, keys)
    grad_key = product("gts,tgd->sd", grad_scores, queries)
    grad_value = product("gts,tgd->sd", weights, grad_heads)
    return (grad_query, grad_key, grad_value)


SEQ_AXES = ("seq_x", "seq_z", "seq_core")
KVH_AXES = ("kvh_x", "kvh_y")
PAIR = [(0, 1), (1, 0)]


def seq_position():
    return (lax.axis_index("seq_x") * lax.axis_size("seq_z") + lax.axis_index("seq_z")) * 2 + lax.axis_index(
        "seq_core"
    )


def gather_rows(block):
    chips = lax.axis_size("seq_x") * lax.axis_size("seq_z")
    copies = jnp.broadcast_to(block[None], (chips,) + block.shape)
    mine = lax.all_to_all(copies, ("seq_x", "seq_z"), 0, 0, tiled=True)
    other = lax.ppermute(mine, "seq_core", PAIR)
    joined = jnp.stack([mine, other], axis=0)
    return joined.reshape((2 * chips * block.shape[0],) + block.shape[1:])


def pair_sum(keep, send):
    got = lax.ppermute(send.astype(jnp.bfloat16), "seq_core", PAIR)
    return (keep.astype(jnp.float32) + got.astype(jnp.float32)).astype(jnp.bfloat16)


def scatter_sum(parts, axis):
    arrived = lax.all_to_all(parts, axis, 0, 0, tiled=True)
    return jnp.sum(arrived.astype(jnp.float32), axis=0)


def body(normed, w_query, w_key, w_value, positions, block_mask, grad_attn):
    tok_rows = normed.shape[0]
    group_size = w_query.shape[1] // w_key.shape[1]
    width_query = group_size * HEAD
    blk_local = tok_rows // BLOCK
    chips = lax.axis_size("seq_x") * lax.axis_size("seq_z")
    kvh_count = lax.axis_size("kvh_x") * lax.axis_size("kvh_y")
    core = lax.axis_index("seq_core")
    my_index = seq_position()
    queries = rotate(
        jnp.dot(normed, w_query, preferred_element_type=jnp.float32), positions, 1.0
    ).astype(jnp.bfloat16)
    keys = rotate(
        jnp.dot(normed, w_key, preferred_element_type=jnp.float32), positions, 1.0
    ).astype(jnp.bfloat16)
    values = jnp.dot(normed, w_value, preferred_element_type=jnp.float32).astype(jnp.bfloat16)
    kv_all = gather_rows(jnp.concatenate([keys, values], axis=1))
    rounds = chips // 2
    chip_me = lax.axis_index("seq_x") * lax.axis_size("seq_z") + lax.axis_index("seq_z")
    round_me = chip_me // 2
    kv_grid = kv_all.reshape(2, rounds, 2, tok_rows, 2 * HEAD)
    own_kv = lax.dynamic_index_in_dim(
        lax.dynamic_index_in_dim(kv_grid[0], round_me, 0, keepdims=False), chip_me % 2, 0, keepdims=False
    )
    later = jnp.roll(kv_grid, -(round_me + 1), axis=1)[:, : rounds - 1]
    kv_sel = jnp.concatenate([own_kv[None], later.reshape(-1, tok_rows, 2 * HEAD)], axis=0)
    kv_sel = kv_sel.reshape(-1, 2 * HEAD)
    keys_all = kv_sel[:, :HEAD]
    values_all = kv_sel[:, HEAD:]
    key_count = keys_all.shape[0]
    per_shard = tok_rows // BLOCK
    chunk = jnp.arange(key_count // BLOCK - per_shard)
    shard = chunk // per_shard
    side = shard // (2 * (rounds - 1))
    chip = ((round_me + 1 + (shard // 2) % (rounds - 1)) % rounds) * 2 + shard % 2
    source = chip * 2 + jnp.where(side == 0, core, 1 - core)
    chunk_blocks = jnp.concatenate(
        [my_index * per_shard + jnp.arange(per_shard), source * per_shard + chunk % per_shard]
    )
    seen = visible(block_mask, my_index * blk_local, tok_rows, chunk_blocks, jnp.arange(key_count) % BLOCK)
    query_heads = queries.reshape(tok_rows, group_size, HEAD)
    grad_heads = grad_attn.reshape(tok_rows, group_size, HEAD)
    log_total, row_dots = softmax_stats(query_heads, keys_all, values_all, grad_heads, seen)
    grad_query, grad_key, grad_value = attention_grads(
        query_heads, keys_all, values_all, grad_heads, seen, log_total, row_dots
    )
    query_grad = rotate(grad_query.reshape(tok_rows, width_query), positions, -1.0).astype(
        jnp.bfloat16
    )
    kv_sel_terms = (
        jnp.concatenate([grad_key, grad_value], axis=1).astype(jnp.bfloat16).reshape(-1, tok_rows, 2 * HEAD)
    )
    later_terms = kv_sel_terms[1:].reshape(2, rounds - 1, 2, tok_rows, 2 * HEAD)
    place = (jnp.arange(2)[:, None] == 0) & (jnp.arange(2)[None, :] == chip_me % 2)
    own_round = jnp.where(place[:, :, None, None], kv_sel_terms[0][None, None], jnp.zeros((), jnp.bfloat16))
    kv_grid_terms = jnp.concatenate([later_terms, own_round[:, None]], axis=1)
    kv_grid_terms = jnp.roll(kv_grid_terms, round_me + 1, axis=1)
    kv_terms = kv_grid_terms.reshape(2, chips, tok_rows, 2 * HEAD)
    feat_split = normed.reshape(tok_rows, chips, 2, normed.shape[1] // (2 * chips))
    normed_even = feat_split[:, :, 0, :]
    normed_odd = feat_split[:, :, 1, :]
    tokens_first = (((0,), (0,)), ((), ()))
    first = core == 0

    def weight_halves(grads):
        even = lax.dot_general(normed_even, grads, tokens_first, preferred_element_type=jnp.float32)
        odd = lax.dot_general(normed_odd, grads, tokens_first, preferred_element_type=jnp.float32)
        return jnp.where(first, even, odd), jnp.where(first, odd, even)

    kv_total = scatter_sum(pair_sum(kv_terms[0], kv_terms[1]), ("seq_x", "seq_z"))
    wq_keep, wq_send = weight_halves(query_grad)
    grad_wq = scatter_sum(pair_sum(wq_keep, wq_send), ("seq_x", "seq_z"))

    def weight_terms(grads):
        keep, send = weight_halves(grads)
        return scatter_sum(pair_sum(keep, send), ("seq_x", "seq_z"))

    contract = (((1,), (1,)), ((), ()))
    partial_input = lax.dot_general(
        query_grad, w_query, contract, preferred_element_type=jnp.float32
    )
    key_grad = rotate(kv_total[:, :HEAD], positions, -1.0).astype(jnp.bfloat16)
    value_grad = kv_total[:, HEAD:].astype(jnp.bfloat16)
    kv_grad = jnp.concatenate([key_grad, value_grad], axis=1)
    grad_wkv = weight_terms(kv_grad)
    grad_wk = grad_wkv[:, :HEAD]
    grad_wv = grad_wkv[:, HEAD:]
    partial_input = partial_input + lax.dot_general(
        key_grad, w_key, contract, preferred_element_type=jnp.float32
    )
    partial_input = partial_input + lax.dot_general(
        value_grad, w_value, contract, preferred_element_type=jnp.float32
    )
    feat = partial_input.shape[1] // kvh_count
    input_terms = partial_input.astype(jnp.bfloat16).reshape(tok_rows, kvh_count, feat)
    arrived = lax.all_to_all(input_terms, KVH_AXES, 1, 1, tiled=True)
    grad_normed = jnp.sum(arrived.astype(jnp.float32), axis=1).astype(jnp.bfloat16)
    return (grad_normed, grad_wq, grad_wk, grad_wv)


def solution(mesh):
    seq_x = 2
    seq_size = mesh.shape["seq"]
    kvh_size = mesh.shape["kvh"]
    grid = mesh.devices.reshape(seq_x, seq_size // (2 * seq_x), 2, 2, kvh_size // 2)
    fine = jax.sharding.Mesh(grid, SEQ_AXES + KVH_AXES)
    in_specs = (
        P(SEQ_AXES, None),
        P(None, KVH_AXES),
        P(None, KVH_AXES),
        P(None, KVH_AXES),
        P(SEQ_AXES),
        P(SEQ_AXES, None),
        P(SEQ_AXES, KVH_AXES),
    )
    out_specs = (P(SEQ_AXES, KVH_AXES),) * 4
    return jax.shard_map(body, mesh=fine, in_specs=in_specs, out_specs=out_specs, check_vma=False)
```
